32 devices in a mesh: blk: 4 (over y, x), patch: 8 (over z, core).
Axes of the slice: x: 2, y: 2, z: 4, core: 2. Of those that a mesh axis runs over, the one named last changes fastest.
Arguments:
- patches: bfloat16 [64, 256, 256], P(('blk', 'patch')), may hold values from -6 to 6
- owner_of_patch: int32 [64], P('blk'), may hold values from 0 to 7, as said below
- group_of_patch: int32 [64], P('blk'), may hold values from 0 to 31
- defocus: float32 [32], replicated, may hold values from 10 to 60
- templ_re: bfloat16 [16, 256, 256], P('blk'), may hold values from -6 to 6
- templ_im: bfloat16 [16, 256, 256], P('blk'), may hold values from -6 to 6
- orientation: int32 [16], replicated, may hold values from 0 to 15, each once
Outputs:
- top_map: float32 [128, 256, 256], P(('blk', 'patch'))
- mean_map: float32 [128, 256, 256], P(('blk', 'patch'))
- var_map: float32 [128, 256, 256], P(('blk', 'patch'))
- peak_table: float32 [128, 16], P(('blk', 'patch'))
The draws below stay inside these ranges and needn't reach their ends.
Inputs may be any that keep to these rules, and one draw needn't show every extreme that they name: `owner_of_patch`: within each block of 16 consecutive entries, the 2 entries of one device name no owner more than 2 times and no owner is named more than 4 times; both bounds are reached in every block.
All inputs are finite; a program needn't handle non-finite values.
Results may differ from the reference program's by a relative error of at most 0.015.
Values may be sent and summed in bfloat16 or wider, within the bound.
No kernel may reach another device: no remote copies, remote signals or barrier semaphores. Data moves between devices by JAX's collectives and lax.ppermute only.
A program may use at most 256 MiB of HBM per device.

```python
import math
import jax
import jax.numpy as jnp
from jax import lax

SIDE = 256
PATCH_DEV = 2
CAP = 4
GROUPS = 32
ORIENTS = 16
NPATCH = 64
SLOTS = 128
N_BLK = 4
N_PATCH = 8


def owner_row(row_key):
    key_order, key_rank, key_shuffle = jax.random.split(row_key, 3)
    owner_order = jax.random.permutation(key_order, N_PATCH)
    source_rank = jax.random.permutation(key_rank, N_PATCH)
    column = jnp.arange(PATCH_DEV, dtype=jnp.int32)[None, :]
    heavy_src = source_rank[:, None] < PATCH_DEV
    offset = jnp.where(heavy_src, column - 2, column)
    other_owner = owner_order[1 + (source_rank[:, None] + offset) % (N_PATCH - 1)]
    chosen = jnp.where(heavy_src & (column < 2), owner_order[0], other_owner)
    scores = jax.random.randint(key_shuffle, (N_PATCH, PATCH_DEV), 0, 1 << 20) * PATCH_DEV + column
    shuffle = jnp.argsort(scores, axis=1)
    return jnp.take_along_axis(chosen, shuffle, axis=1)


def draw_owner_of_patch(key, part):
    row_keys = jax.random.split(jax.random.fold_in(key, 7), N_BLK)
    owner_rows = jax.vmap(owner_row)(row_keys)
    return owner_rows.reshape(-1).astype(jnp.int32)


def with_ends(result, own_key, smallest, largest):
    dims = result.shape
    spot = [jax.random.randint(jax.random.fold_in(own_key, axis), (), 0, dims[axis]) for axis in range(len(dims))]
    result = result.at[tuple(spot)].set(smallest)
    longest = dims.index(max(dims))
    spot[longest] = (spot[longest] + 1) % dims[longest]
    return result.at[tuple(spot)].set(largest)


def steps_of(key, dims, pieces, smallest, top_value):
    def one(dim, shards_of):
        heights = jax.random.uniform(jax.random.fold_in(jax.random.fold_in(key, 6), dim), (shards_of,), jnp.float32, smallest / len(pieces), top_value / len(pieces))
        return jnp.repeat(jnp.exp(heights), dims[dim] // shards_of).reshape((-1,) + (1,) * (len(dims) - dim - 1))

    loudness = one(*pieces[0])
    for cut in pieces[1:]:
        loudness = loudness * one(*cut)
    return loudness


def normal_values(rng, dims, spread, limit, shards=(), kind=jnp.bfloat16):
    loudness = steps_of(rng, dims, shards, -0.22, 0.18) if shards else 1.0
    result = jax.random.normal(rng, dims, jnp.float32) * spread * loudness
    return jnp.minimum(jnp.maximum(result, -limit), limit).astype(kind)


def setup_inputs(seed: int = 0) -> dict:
    key_list = jax.random.split(jax.random.key(seed), 8)
    patches = normal_values(key_list[0], (NPATCH, SIDE, SIDE), 1.0, 6.0, ((0, 32),))
    owner_of_patch = draw_owner_of_patch(jax.random.fold_in(key_list[7], 71), 0)
    group_of_patch = with_ends(jax.random.randint(key_list[2], (NPATCH,), 0, GROUPS), jax.random.fold_in(key_list[2], 1), 0, GROUPS - 1).astype(jnp.int32)
    defocus = jnp.clip(jnp.exp(jax.random.uniform(key_list[3], (GROUPS,), jnp.float32, math.log(10.0), math.log(60.0))), 10.0, 60.0)
    templ_re = normal_values(key_list[4], (ORIENTS, SIDE, SIDE), 1.0, 6.0, ((0, 4),))
    templ_im = normal_values(key_list[5], (ORIENTS, SIDE, SIDE), 1.0, 6.0, ((0, 4),))
    orientation = jax.random.permutation(key_list[6], ORIENTS).astype(jnp.int32)
    return dict(patches=patches, owner_of_patch=owner_of_patch, group_of_patch=group_of_patch, defocus=defocus, templ_re=templ_re, templ_im=templ_im, orientation=orientation)


AMPLITUDE = 0.07


def dft_tables(extent):
    indices = jnp.arange(extent, dtype=jnp.int32)
    turn_count = (indices[:, None] * indices[None, :]) % extent
    angles = turn_count.astype(jnp.float32) * (2.0 * math.pi / extent)
    return jnp.cos(angles).astype(jnp.bfloat16), jnp.sin(angles).astype(jnp.bfloat16)


def ctf_filter(defocus_values, extent):
    indices = jnp.arange(extent, dtype=jnp.int32)
    signed = jnp.where(indices < extent // 2, indices, indices - extent).astype(jnp.float32) / extent
    radius = signed[:, None] * signed[:, None] + signed[None, :] * signed[None, :]
    phases = math.pi * defocus_values[:, None, None] * radius[None, :, :] - AMPLITUDE
    return -jnp.sin(phases)


def filtered_spectra(images, filters, cosine, sine):
    extent = images.shape[-1]
    cos_wide = cosine.astype(jnp.float32)
    sin_wide = sine.astype(jnp.float32)
    image_wide = images.astype(jnp.float32)
    half_re = jnp.einsum("nuv,vy->nuy", image_wide, cos_wide).astype(jnp.bfloat16).astype(jnp.float32)
    half_im = jnp.einsum("nuv,vy->nuy", image_wide, -sin_wide).astype(jnp.bfloat16).astype(jnp.float32)
    real = jnp.einsum("xu,nuy->nxy", cos_wide, half_re) + jnp.einsum("xu,nuy->nxy", sin_wide, half_im)
    imag = jnp.einsum("xu,nuy->nxy", cos_wide, half_im) - jnp.einsum("xu,nuy->nxy", sin_wide, half_re)
    scale = filters / extent
    return (real * scale).astype(jnp.bfloat16), (imag * scale).astype(jnp.bfloat16)


def correlate(spec_re, spec_im, templ_re, templ_im, cosine, sine):
    extent = templ_re.shape[-1]
    spec_rw = spec_re.astype(jnp.float32)
    spec_iw = spec_im.astype(jnp.float32)
    templ_rw = templ_re.astype(jnp.float32)
    templ_iw = templ_im.astype(jnp.float32)
    prod_re = (spec_rw * templ_rw + spec_iw * templ_iw).astype(jnp.bfloat16).astype(jnp.float32)
    prod_im = (spec_iw * templ_rw - spec_rw * templ_iw).astype(jnp.bfloat16).astype(jnp.float32)
    cos_wide = cosine.astype(jnp.float32)
    sin_wide = sine.astype(jnp.float32)
    q_re = (jnp.einsum("nuv,vy->nuy", prod_re, cos_wide) - jnp.einsum("nuv,vy->nuy", prod_im, sin_wide))
    q_im = (jnp.einsum("nuv,vy->nuy", prod_re, sin_wide) + jnp.einsum("nuv,vy->nuy", prod_im, cos_wide))
    q_re = q_re.astype(jnp.bfloat16).astype(jnp.float32)
    q_im = q_im.astype(jnp.bfloat16).astype(jnp.float32)
    return (jnp.einsum("xu,nuy->nxy", cos_wide, q_re) - jnp.einsum("xu,nuy->nxy", sin_wide, q_im)) / extent


def reference(patches, owner_of_patch, group_of_patch, defocus, templ_re, templ_im, orientation):
    extent = SIDE
    cosine, sine = dft_tables(extent)

    def one_patch(operands):
        image, group = operands
        filters = ctf_filter(defocus[group][None], extent)
        spec_re, spec_im = filtered_spectra(image[None], filters, cosine, sine)
        corr = correlate(spec_re, spec_im, templ_re, templ_im, cosine, sine)
        top_map = jnp.max(corr, axis=0)
        mean_map = jnp.sum(corr, axis=0) / ORIENTS
        var_map = jnp.sum(corr * corr, axis=0) / ORIENTS - mean_map * mean_map
        peak_rows = jnp.zeros((ORIENTS,), jnp.float32).at[orientation].set(jnp.max(corr, axis=(1, 2)))
        return top_map, mean_map, var_map, peak_rows

    top_map, mean_map, var_map, peak_rows = lax.map(one_patch, (patches, group_of_patch))
    per_group = N_PATCH * PATCH_DEV
    owners = owner_of_patch.reshape(N_BLK, per_group)
    owner_hits = (owners[:, :, None] == jnp.arange(N_PATCH, dtype=jnp.int32)[None, None, :]).astype(jnp.int32)
    earlier = jnp.cumsum(owner_hits, axis=1) - owner_hits
    rank_in = jnp.sum(earlier * owner_hits, axis=2)
    slot = ((jnp.arange(N_BLK, dtype=jnp.int32)[:, None] * N_PATCH + owners) * CAP + rank_in).reshape(-1)

    def place(values):
        return jnp.zeros((SLOTS,) + values.shape[1:], jnp.float32).at[slot].set(values)

    return place(top_map), place(mean_map), place(var_map), place(peak_rows)
```

```python
import functools
import math

import jax
import jax.numpy as jnp
from jax import lax
from jax.experimental import pallas as pl
from jax.experimental.pallas import tpu as pltpu
from jax.sharding import PartitionSpec as P

SLOT = 2
CAP = 4
TILE_T = 4


AMPLITUDE = 0.07


def dft_tables(extent):
    indices = jnp.arange(extent, dtype=jnp.int32)
    turn_count = indices[:, None] * indices[None, :] % extent
    angles = turn_count.astype(jnp.float32) * (2.0 * math.pi / extent)
    return (jnp.cos(angles).astype(jnp.bfloat16), jnp.sin(angles).astype(jnp.bfloat16))


def ctf_filter(defocus_values, extent):
    indices = jnp.arange(extent, dtype=jnp.int32)
    signed = (
        jnp.where(indices < extent // 2, indices, indices - extent).astype(jnp.float32) / extent
    )
    radius = signed[:, None] * signed[:, None] + signed[None, :] * signed[None, :]
    phases = math.pi * defocus_values[:, None, None] * radius[None, :, :] - AMPLITUDE
    return -jnp.sin(phases)


def routing(row_owner, my_index):
    sources, number = row_owner.shape
    owner_ids = jnp.arange(sources, dtype=jnp.int32)
    owner_hits = (row_owner[:, :, None] == owner_ids[None, None, :]).astype(jnp.int32)
    earlier = jnp.cumsum(owner_hits, axis=1) - owner_hits
    rank_in = jnp.sum(earlier * owner_hits, axis=2)
    counts = jnp.sum(owner_hits, axis=1)
    slot_key = row_owner * SLOT + rank_in
    targets = jnp.arange(sources * SLOT, dtype=jnp.int32)
    matches = slot_key[:, :, None] == targets[None, None, :]
    local_idx = jnp.sum(
        jnp.where(matches, jnp.arange(number, dtype=jnp.int32)[None, :, None], 0), axis=1
    )
    send_table = jnp.where(jnp.any(matches, axis=1), local_idx, number)
    arrived = lax.dynamic_slice_in_dim(counts, my_index, 1, 1)[:, 0]
    offsets = jnp.cumsum(arrived) - arrived
    within = jnp.arange(SLOT, dtype=jnp.int32)
    usable = within[None, :] < arrived[:, None]
    position = jnp.where(usable, offsets[:, None] + within[None, :], -1).reshape(-1)
    slot_ids = jnp.arange(CAP, dtype=jnp.int32)
    picked = position[None, :] == slot_ids[:, None]
    received_row = jnp.sum(jnp.where(picked, targets[None, :], 0), axis=1)
    take_table = jnp.where(jnp.any(picked, axis=1), received_row, sources * SLOT)
    my_columns = lax.dynamic_slice_in_dim(send_table, my_index * SLOT, SLOT, 1)
    row_of = jnp.where(
        my_columns < number, owner_ids[:, None] * number + my_columns, sources * number
    ).reshape(-1)
    row_of = jnp.concatenate([row_of, jnp.full((1,), sources * number, jnp.int32)])
    slot_row = jnp.take(row_of, take_table)
    my_send = lax.dynamic_slice_in_dim(send_table, my_index, 1, 0)[0]
    return (my_send, take_table, slot_row)


def make_spectra(images, focus_values, cosine, sine):
    count, extent = (images.shape[0], images.shape[-1])
    flat_images = images.reshape(count * extent, extent)
    half_re = jnp.dot(flat_images, cosine, preferred_element_type=jnp.float32).astype(jnp.bfloat16)
    half_im = jnp.dot(flat_images, -sine, preferred_element_type=jnp.float32).astype(jnp.bfloat16)
    half_stack = jnp.concatenate(
        [half_re.reshape(count, extent, extent), half_im.reshape(count, extent, extent)], axis=1
    )
    left_real = jnp.concatenate([cosine, sine], axis=1)
    left_imag = jnp.concatenate([-sine, cosine], axis=1)
    real = jnp.einsum("xk,nky->nxy", left_real, half_stack, preferred_element_type=jnp.float32)
    imag = jnp.einsum("xk,nky->nxy", left_imag, half_stack, preferred_element_type=jnp.float32)
    scale = ctf_filter(focus_values, extent) / extent
    return ((real * scale).astype(jnp.bfloat16), (imag * scale).astype(jnp.bfloat16))


def corr_kernel(first, *refs):
    if first:
        (sr_ref, si_ref, tr_ref, ti_ref, c_ref, s_ref, top_ref, sum_ref, sq_ref, peak_ref) = refs
    else:
        (sr_ref, si_ref, tr_ref, ti_ref, c_ref, s_ref, top_in, sum_in, sq_in,
         top_ref, sum_ref, sq_ref, peak_ref) = refs
    t = pl.program_id(1)
    extent = sr_ref.shape[-1]
    sr = sr_ref[0].astype(jnp.float32)
    si = si_ref[0].astype(jnp.float32)
    tr = tr_ref[0].astype(jnp.float32)
    ti = ti_ref[0].astype(jnp.float32)
    pre = (sr * tr + si * ti).astype(jnp.bfloat16)
    pim = (si * tr - sr * ti).astype(jnp.bfloat16)
    cos_t = c_ref[...]
    sin_t = s_ref[...]

    def mm(a, b):
        return jnp.dot(a, b, preferred_element_type=jnp.float32)

    q_re = (mm(pre, cos_t) - mm(pim, sin_t)).astype(jnp.bfloat16)
    q_im = (mm(pre, sin_t) + mm(pim, cos_t)).astype(jnp.bfloat16)
    corr = (mm(cos_t, q_re) - mm(sin_t, q_im)) / extent
    peak_ref[...] = jnp.full(peak_ref.shape, jnp.max(corr), jnp.float32)

    if first:
        @pl.when(t == 0)
        def _():
            top_ref[0] = corr
            sum_ref[0] = corr
            sq_ref[0] = corr * corr
    else:
        @pl.when(t == 0)
        def _():
            top_ref[0] = jnp.maximum(top_in[0], corr)
            sum_ref[0] = sum_in[0] + corr
            sq_ref[0] = sq_in[0] + corr * corr

    @pl.when(t > 0)
    def _():
        top_ref[0] = jnp.maximum(top_ref[0], corr)
        sum_ref[0] = sum_ref[0] + corr
        sq_ref[0] = sq_ref[0] + corr * corr


def correlate_chunk(spec_re, spec_im, templ_re, templ_im, cosine, sine, stats):
    count, extent = (spec_re.shape[0], spec_re.shape[-1])
    tiles = templ_re.shape[0]
    first = stats is None
    plane = pl.BlockSpec((1, extent, extent), lambda s, t: (s, 0, 0))
    templ_spec = pl.BlockSpec((1, extent, extent), lambda s, t: (t, 0, 0))
    table = pl.BlockSpec((extent, extent), lambda s, t: (0, 0))
    in_specs = [plane, plane, templ_spec, templ_spec, table, table]
    operands = [spec_re, spec_im, templ_re, templ_im, cosine, sine]
    aliases = {}
    if not first:
        in_specs += [plane, plane, plane]
        operands += list(stats)
        aliases = {6: 0, 7: 1, 8: 2}
    map_shape = jax.ShapeDtypeStruct((count, extent, extent), jnp.float32)
    flops = tiles * count * 12 * extent * extent * extent
    outs = pl.pallas_call(
        functools.partial(corr_kernel, first),
        grid=(count, tiles),
        in_specs=in_specs,
        out_specs=[plane, plane, plane, pl.BlockSpec((1, 1, 8, 128), lambda s, t: (s, t, 0, 0))],
        out_shape=[map_shape, map_shape, map_shape,
                   jax.ShapeDtypeStruct((count, tiles, 8, 128), jnp.float32)],
        input_output_aliases=aliases,
        compiler_params=pltpu.CompilerParams(dimension_semantics=("parallel", "arbitrary")),
        cost_estimate=pl.CostEstimate(
            flops=flops, transcendentals=0,
            bytes_accessed=tiles * count * 4 * extent * extent * 2 + count * 6 * extent * extent * 4),
    )(*operands)
    return outs[:3], outs[3][:, :, 0, 0]


def correlate_all(spec_re, spec_im, templ_re, templ_im, orientation, cosine, sine):
    blocks = lax.axis_size("blk")
    me = lax.axis_index("blk")
    tiles = templ_re.shape[0]
    stats, peak = correlate_chunk(spec_re, spec_im, templ_re, templ_im, cosine, sine, None)
    peaks = [(me, peak)]
    for k in range(1, blocks):
        pairs = [(b, b ^ k) for b in range(blocks)]
        got_re = lax.ppermute(templ_re, "blk", pairs)
        got_im = lax.ppermute(templ_im, "blk", pairs)
        stats, peak = correlate_chunk(spec_re, spec_im, got_re, got_im, cosine, sine, stats)
        peaks.append((me ^ k, peak))
    top_map, totals, squares = stats
    orient_total = orientation.shape[0]
    count = spec_re.shape[0]
    peak_rows = jnp.zeros((count, orient_total), jnp.float32)
    within = jnp.arange(tiles, dtype=jnp.int32)
    for source, peak in peaks:
        columns = jnp.take(orientation, source * tiles + within)
        peak_rows = peak_rows.at[:, columns].set(peak)
    mean_map = totals / orient_total
    var_map = squares / orient_total - mean_map * mean_map
    return (top_map, mean_map, var_map, peak_rows)


def body(patches, owner_of_patch, group_of_patch, defocus, templ_re, templ_im, orientation):
    sources = lax.axis_size("patch")
    my_index = lax.axis_index("patch")
    number, extent = (patches.shape[0], patches.shape[1])
    cosine, sine = dft_tables(extent)
    row_owner = owner_of_patch.reshape(sources, number)
    my_send, take_table, slot_row = routing(row_owner, my_index)
    padded = jnp.concatenate([patches, jnp.zeros((1, extent, extent), jnp.bfloat16)], axis=0)
    outgoing = jnp.take(padded, my_send, axis=0).reshape(sources, SLOT, extent, extent)
    incoming = lax.all_to_all(outgoing, "patch", split_axis=0, concat_axis=0, tiled=True)
    flattened = jnp.concatenate(
        [
            incoming.reshape(sources * SLOT, extent, extent),
            jnp.zeros((1, extent, extent), jnp.bfloat16),
        ],
        axis=0,
    )
    my_slots = jnp.take(flattened, take_table, axis=0)
    groups = jnp.take(jnp.concatenate([group_of_patch, jnp.zeros((1,), jnp.int32)]), slot_row)
    focus_values = jnp.take(defocus, groups)
    spec_re, spec_im = make_spectra(my_slots, focus_values, cosine, sine)
    return correlate_all(spec_re, spec_im, templ_re, templ_im, orientation, cosine, sine)


def solution(mesh):
    placed = (
        P(("blk", "patch"), None, None),
        P("blk"),
        P("blk"),
        P(),
        P("blk", None, None),
        P("blk", None, None),
        P(),
    )
    return jax.shard_map(
        body,
        mesh=mesh,
        in_specs=placed,
        out_specs=(
            P(("blk", "patch"), None, None),
            P(("blk", "patch"), None, None),
            P(("blk", "patch"), None, None),
            P(("blk", "patch"), None),
        ),
        check_vma=False,
    )
```

```python
import functools
import math

import jax
import jax.numpy as jnp
from jax import lax
from jax.experimental import pallas as pl
from jax.experimental.pallas import tpu as pltpu
from jax.sharding import PartitionSpec as P

SLOT = 2
CAP = 4
TILE_T = 4


AMPLITUDE = 0.07


def dft_tables(extent):
    indices = jnp.arange(extent, dtype=jnp.int32)
    turn_count = indices[:, None] * indices[None, :] % extent
    angles = turn_count.astype(jnp.float32) * (2.0 * math.pi / extent)
    return (jnp.cos(angles).astype(jnp.bfloat16), jnp.sin(angles).astype(jnp.bfloat16))


def ctf_filter(defocus_values, extent):
    indices = jnp.arange(extent, dtype=jnp.int32)
    signed = (
        jnp.where(indices < extent // 2, indices, indices - extent).astype(jnp.float32) / extent
    )
    radius = signed[:, None] * signed[:, None] + signed[None, :] * signed[None, :]
    phases = math.pi * defocus_values[:, None, None] * radius[None, :, :] - AMPLITUDE
    return -jnp.sin(phases)


def xor_pairs(count, shift):
    return [(d, d ^ shift) for d in range(count)]


def route_patches(patches, row_owner, my_index):
    sources, number = row_owner.shape
    extent = patches.shape[-1]
    chips = sources // 2
    devs = jnp.arange(sources, dtype=jnp.int32)
    chip_of = devs // 2
    owner_chip = row_owner // 2
    masks = [row_owner == (devs ^ 1)[:, None]]
    for m in range(1, chips):
        masks.append(owner_chip == (chip_of ^ m)[:, None])
    match = jnp.stack(masks, axis=1)
    first = jnp.where(match[..., 0], 0, jnp.where(match[..., 1], 1, number))
    second = jnp.where(match[..., 0] & match[..., 1], 1, number)
    send_sel = jnp.stack([first, second], axis=-1)
    send_pid = jnp.where(send_sel < number, devs[:, None, None] * number + send_sel, -1)
    padded = jnp.concatenate([patches, jnp.zeros((1, extent, extent), patches.dtype)], axis=0)
    my_sel = lax.dynamic_index_in_dim(send_sel, my_index, 0, keepdims=False)
    outgoing = jnp.take(padded, my_sel.reshape(-1), axis=0).reshape(chips, 2, extent, extent)
    partner = my_index ^ 1
    my_chip = my_index // 2
    direct = lax.ppermute(outgoing[0], "patch", xor_pairs(sources, 1))
    received = []
    for m in range(1, chips):
        received.append(lax.ppermute(outgoing[m], "patch", xor_pairs(sources, 2 * m)))
    received = jnp.concatenate(received, axis=0)
    forwarded = lax.ppermute(received, "patch", xor_pairs(sources, 1))
    cand_pid = [my_index * number + jnp.arange(number, dtype=jnp.int32)]
    cand_pid.append(lax.dynamic_index_in_dim(send_pid, partner, 0, keepdims=False)[0])
    for core in (my_index % 2, partner % 2):
        for m in range(1, chips):
            source = (my_chip ^ m) * 2 + core
            cand_pid.append(lax.dynamic_index_in_dim(send_pid, source, 0, keepdims=False)[m])
    cand_pid = jnp.concatenate(cand_pid)
    candidates = jnp.concatenate(
        [patches, direct, received, forwarded, jnp.zeros((1, extent, extent), patches.dtype)],
        axis=0,
    )
    flat_owner = row_owner.reshape(-1)
    hits = (flat_owner == my_index).astype(jnp.int32)
    rank_in = jnp.cumsum(hits) - hits
    slot_ids = jnp.arange(CAP, dtype=jnp.int32)
    wanted = (hits[None, :] == 1) & (rank_in[None, :] == slot_ids[:, None])
    patch_ids = jnp.arange(sources * number, dtype=jnp.int32)
    slot_pid = jnp.sum(jnp.where(wanted, patch_ids[None, :], 0), axis=1)
    present = jnp.any(wanted, axis=1)
    cand_ids = jnp.arange(cand_pid.shape[0], dtype=jnp.int32)
    found = cand_pid[None, :] == slot_pid[:, None]
    take_idx = jnp.sum(jnp.where(found, cand_ids[None, :], 0), axis=1)
    take_idx = jnp.where(present, take_idx, cand_pid.shape[0])
    my_slots = jnp.take(candidates, take_idx, axis=0)
    return my_slots, jnp.where(present, slot_pid, sources * number)


def make_spectra(images, focus_values, cosine, sine):
    count, extent = (images.shape[0], images.shape[-1])
    flat_images = images.reshape(count * extent, extent)
    half_re = jnp.dot(flat_images, cosine, preferred_element_type=jnp.float32).astype(jnp.bfloat16)
    half_im = jnp.dot(flat_images, -sine, preferred_element_type=jnp.float32).astype(jnp.bfloat16)
    half_stack = jnp.concatenate(
        [half_re.reshape(count, extent, extent), half_im.reshape(count, extent, extent)], axis=1
    )
    left_real = jnp.concatenate([cosine, sine], axis=1)
    left_imag = jnp.concatenate([-sine, cosine], axis=1)
    real = jnp.einsum("xk,nky->nxy", left_real, half_stack, preferred_element_type=jnp.float32)
    imag = jnp.einsum("xk,nky->nxy", left_imag, half_stack, preferred_element_type=jnp.float32)
    scale = ctf_filter(focus_values, extent) / extent
    return ((real * scale).astype(jnp.bfloat16), (imag * scale).astype(jnp.bfloat16))


def corr_kernel(first, *refs):
    if first:
        (sr_ref, si_ref, tr_ref, ti_ref, c_ref, s_ref, top_ref, sum_ref, sq_ref, peak_ref) = refs
    else:
        (sr_ref, si_ref, tr_ref, ti_ref, c_ref, s_ref, top_in, sum_in, sq_in,
         top_ref, sum_ref, sq_ref, peak_ref) = refs
    t = pl.program_id(1)
    extent = sr_ref.shape[-1]
    sr = sr_ref[0].astype(jnp.float32)
    si = si_ref[0].astype(jnp.float32)
    tr = tr_ref[0].astype(jnp.float32)
    ti = ti_ref[0].astype(jnp.float32)
    pre = (sr * tr + si * ti).astype(jnp.bfloat16)
    pim = (si * tr - sr * ti).astype(jnp.bfloat16)
    cos_t = c_ref[...]
    sin_t = s_ref[...]

    def mm(a, b):
        return jnp.dot(a, b, preferred_element_type=jnp.float32)

    q_re = (mm(pre, cos_t) - mm(pim, sin_t)).astype(jnp.bfloat16)
    q_im = (mm(pre, sin_t) + mm(pim, cos_t)).astype(jnp.bfloat16)
    corr = (mm(cos_t, q_re) - mm(sin_t, q_im)) / extent
    peak_ref[...] = jnp.full(peak_ref.shape, jnp.max(corr), jnp.float32)

    if first:
        @pl.when(t == 0)
        def _():
            top_ref[0] = corr
            sum_ref[0] = corr
            sq_ref[0] = corr * corr
    else:
        @pl.when(t == 0)
        def _():
            top_ref[0] = jnp.maximum(top_in[0], corr)
            sum_ref[0] = sum_in[0] + corr
            sq_ref[0] = sq_in[0] + corr * corr

    @pl.when(t > 0)
    def _():
        top_ref[0] = jnp.maximum(top_ref[0], corr)
        sum_ref[0] = sum_ref[0] + corr
        sq_ref[0] = sq_ref[0] + corr * corr


def correlate_chunk(spec_re, spec_im, templ_re, templ_im, cosine, sine, stats):
    count, extent = (spec_re.shape[0], spec_re.shape[-1])
    tiles = templ_re.shape[0]
    first = stats is None
    plane = pl.BlockSpec((1, extent, extent), lambda s, t: (s, 0, 0))
    templ_spec = pl.BlockSpec((1, extent, extent), lambda s, t: (t, 0, 0))
    table = pl.BlockSpec((extent, extent), lambda s, t: (0, 0))
    in_specs = [plane, plane, templ_spec, templ_spec, table, table]
    operands = [spec_re, spec_im, templ_re, templ_im, cosine, sine]
    aliases = {}
    if not first:
        in_specs += [plane, plane, plane]
        operands += list(stats)
        aliases = {6: 0, 7: 1, 8: 2}
    map_shape = jax.ShapeDtypeStruct((count, extent, extent), jnp.float32)
    flops = tiles * count * 12 * extent * extent * extent
    outs = pl.pallas_call(
        functools.partial(corr_kernel, first),
        grid=(count, tiles),
        in_specs=in_specs,
        out_specs=[plane, plane, plane, pl.BlockSpec((1, 1, 8, 128), lambda s, t: (s, t, 0, 0))],
        out_shape=[map_shape, map_shape, map_shape,
                   jax.ShapeDtypeStruct((count, tiles, 8, 128), jnp.float32)],
        input_output_aliases=aliases,
        compiler_params=pltpu.CompilerParams(dimension_semantics=("parallel", "arbitrary")),
        cost_estimate=pl.CostEstimate(
            flops=flops, transcendentals=0,
            bytes_accessed=tiles * count * 4 * extent * extent * 2 + count * 6 * extent * extent * 4),
    )(*operands)
    return outs[:3], outs[3][:, :, 0, 0]


def correlate_all(spec_re, spec_im, templ_re, templ_im, orientation, cosine, sine):
    blocks = lax.axis_size("blk")
    me = lax.axis_index("blk")
    tiles = templ_re.shape[0]
    stats, peak = correlate_chunk(spec_re, spec_im, templ_re, templ_im, cosine, sine, None)
    peaks = [(me, peak)]
    for k in range(1, blocks):
        pairs = [(b, b ^ k) for b in range(blocks)]
        got_re = lax.ppermute(templ_re, "blk", pairs)
        got_im = lax.ppermute(templ_im, "blk", pairs)
        stats, peak = correlate_chunk(spec_re, spec_im, got_re, got_im, cosine, sine, stats)
        peaks.append((me ^ k, peak))
    top_map, totals, squares = stats
    orient_total = orientation.shape[0]
    count = spec_re.shape[0]
    peak_rows = jnp.zeros((count, orient_total), jnp.float32)
    within = jnp.arange(tiles, dtype=jnp.int32)
    for source, peak in peaks:
        columns = jnp.take(orientation, source * tiles + within)
        peak_rows = peak_rows.at[:, columns].set(peak)
    mean_map = totals / orient_total
    var_map = squares / orient_total - mean_map * mean_map
    return (top_map, mean_map, var_map, peak_rows)


def body(patches, owner_of_patch, group_of_patch, defocus, templ_re, templ_im, orientation):
    sources = lax.axis_size("patch")
    my_index = lax.axis_index("patch")
    number, extent = (patches.shape[0], patches.shape[1])
    cosine, sine = dft_tables(extent)
    row_owner = owner_of_patch.reshape(sources, number)
    my_slots, slot_row = route_patches(patches, row_owner, my_index)
    groups = jnp.take(jnp.concatenate([group_of_patch, jnp.zeros((1,), jnp.int32)]), slot_row)
    focus_values = jnp.take(defocus, groups)
    spec_re, spec_im = make_spectra(my_slots, focus_values, cosine, sine)
    return correlate_all(spec_re, spec_im, templ_re, templ_im, orientation, cosine, sine)


def solution(mesh):
    placed = (
        P(("blk", "patch"), None, None),
        P("blk"),
        P("blk"),
        P(),
        P("blk", None, None),
        P("blk", None, None),
        P(),
    )
    return jax.shard_map(
        body,
        mesh=mesh,
        in_specs=placed,
        out_specs=(
            P(("blk", "patch"), None, None),
            P(("blk", "patch"), None, None),
            P(("blk", "patch"), None, None),
            P(("blk", "patch"), None),
        ),
        check_vma=False,
    )
```

```python
import functools
import math

import jax
import jax.numpy as jnp
from jax import lax
from jax.experimental import pallas as pl
from jax.experimental.pallas import tpu as pltpu
from jax.sharding import PartitionSpec as P

SLOT = 2
CAP = 4
TILE_T = 4


AMPLITUDE = 0.07


def dft_tables(extent):
    indices = jnp.arange(extent, dtype=jnp.int32)
    turn_count = indices[:, None] * indices[None, :] % extent
    angles = turn_count.astype(jnp.float32) * (2.0 * math.pi / extent)
    return (jnp.cos(angles).astype(jnp.bfloat16), jnp.sin(angles).astype(jnp.bfloat16))


def ctf_filter(defocus_values, extent):
    indices = jnp.arange(extent, dtype=jnp.int32)
    signed = (
        jnp.where(indices < extent // 2, indices, indices - extent).astype(jnp.float32) / extent
    )
    radius = signed[:, None] * signed[:, None] + signed[None, :] * signed[None, :]
    phases = math.pi * defocus_values[:, None, None] * radius[None, :, :] - AMPLITUDE
    return -jnp.sin(phases)


def xor_pairs(count, shift):
    return [(d, d ^ shift) for d in range(count)]


def route_patches(patches, row_owner, my_index):
    sources, number = row_owner.shape
    extent = patches.shape[-1]
    chips = sources // 2
    devs = jnp.arange(sources, dtype=jnp.int32)
    chip_of = devs // 2
    owner_chip = row_owner // 2
    masks = [row_owner == (devs ^ 1)[:, None]]
    for m in range(1, chips):
        masks.append(owner_chip == (chip_of ^ m)[:, None])
    match = jnp.stack(masks, axis=1)
    first = jnp.where(match[..., 0], 0, jnp.where(match[..., 1], 1, number))
    second = jnp.where(match[..., 0] & match[..., 1], 1, number)
    send_sel = jnp.stack([first, second], axis=-1)
    send_pid = jnp.where(send_sel < number, devs[:, None, None] * number + send_sel, -1)
    padded = jnp.concatenate([patches, jnp.zeros((1, extent, extent), patches.dtype)], axis=0)
    my_sel = lax.dynamic_index_in_dim(send_sel, my_index, 0, keepdims=False)
    outgoing = jnp.take(padded, my_sel.reshape(-1), axis=0).reshape(chips, 2, extent, extent)
    partner = my_index ^ 1
    my_chip = my_index // 2
    direct = lax.ppermute(outgoing[0], "patch", xor_pairs(sources, 1))
    received = []
    for m in range(1, chips):
        received.append(lax.ppermute(outgoing[m], "patch", xor_pairs(sources, 2 * m)))
    received = jnp.concatenate(received, axis=0)
    forwarded = lax.ppermute(received, "patch", xor_pairs(sources, 1))
    cand_pid = [my_index * number + jnp.arange(number, dtype=jnp.int32)]
    cand_pid.append(lax.dynamic_index_in_dim(send_pid, partner, 0, keepdims=False)[0])
    for core in (my_index % 2, partner % 2):
        for m in range(1, chips):
            source = (my_chip ^ m) * 2 + core
            cand_pid.append(lax.dynamic_index_in_dim(send_pid, source, 0, keepdims=False)[m])
    cand_pid = jnp.concatenate(cand_pid)
    candidates = jnp.concatenate(
        [patches, direct, received, forwarded, jnp.zeros((1, extent, extent), patches.dtype)],
        axis=0,
    )
    flat_owner = row_owner.reshape(-1)
    hits = (flat_owner == my_index).astype(jnp.int32)
    rank_in = jnp.cumsum(hits) - hits
    slot_ids = jnp.arange(CAP, dtype=jnp.int32)
    wanted = (hits[None, :] == 1) & (rank_in[None, :] == slot_ids[:, None])
    patch_ids = jnp.arange(sources * number, dtype=jnp.int32)
    slot_pid = jnp.sum(jnp.where(wanted, patch_ids[None, :], 0), axis=1)
    present = jnp.any(wanted, axis=1)
    cand_ids = jnp.arange(cand_pid.shape[0], dtype=jnp.int32)
    found = cand_pid[None, :] == slot_pid[:, None]
    take_idx = jnp.sum(jnp.where(found, cand_ids[None, :], 0), axis=1)
    take_idx = jnp.where(present, take_idx, cand_pid.shape[0])
    my_slots = jnp.take(candidates, take_idx, axis=0)
    return my_slots, jnp.where(present, slot_pid, sources * number)


def make_spectra(images, focus_values, cosine, sine):
    count, extent = (images.shape[0], images.shape[-1])
    flat_images = images.reshape(count * extent, extent)
    half_re = jnp.dot(flat_images, cosine, preferred_element_type=jnp.float32).astype(jnp.bfloat16)
    half_im = jnp.dot(flat_images, -sine, preferred_element_type=jnp.float32).astype(jnp.bfloat16)
    half_stack = jnp.concatenate(
        [half_re.reshape(count, extent, extent), half_im.reshape(count, extent, extent)], axis=1
    )
    left_real = jnp.concatenate([cosine, sine], axis=1)
    left_imag = jnp.concatenate([-sine, cosine], axis=1)
    real = jnp.einsum("xk,nky->nxy", left_real, half_stack, preferred_element_type=jnp.float32)
    imag = jnp.einsum("xk,nky->nxy", left_imag, half_stack, preferred_element_type=jnp.float32)
    scale = ctf_filter(focus_values, extent) / extent
    return ((real * scale).astype(jnp.bfloat16), (imag * scale).astype(jnp.bfloat16))


def corr_kernel(first, tiles, *refs):
    if first:
        (sr_ref, si_ref, tr_ref, ti_ref, fw_ref, inv_ref, top_ref, sum_ref, sq_ref, peak_ref) = refs
    else:
        (sr_ref, si_ref, tr_ref, ti_ref, fw_ref, inv_ref, top_in, sum_in, sq_in,
         top_ref, sum_ref, sq_ref, peak_ref) = refs
    extent = sr_ref.shape[-1]
    sr = sr_ref[0].astype(jnp.float32)
    si = si_ref[0].astype(jnp.float32)
    forward = fw_ref[...]
    inverse = inv_ref[...]
    top = total = square = None
    for t in range(tiles):
        tr = tr_ref[t].astype(jnp.float32)
        ti = ti_ref[t].astype(jnp.float32)
        pre = (sr * tr + si * ti).astype(jnp.bfloat16)
        pim = (si * tr - sr * ti).astype(jnp.bfloat16)
        prod = jnp.concatenate([pre, pim], axis=1)
        q = jnp.dot(prod, forward, preferred_element_type=jnp.float32).astype(jnp.bfloat16)
        q_stack = jnp.concatenate([q[:, :extent], q[:, extent:]], axis=0)
        corr = jnp.dot(inverse, q_stack, preferred_element_type=jnp.float32)
        peak_ref[0, t] = jnp.full(peak_ref.shape[2:], jnp.max(corr), jnp.float32)
        if top is None:
            top, total, square = corr, corr, corr * corr
        else:
            top = jnp.maximum(top, corr)
            total = total + corr
            square = square + corr * corr
    if first:
        top_ref[0] = top
        sum_ref[0] = total
        sq_ref[0] = square
    else:
        top_ref[0] = jnp.maximum(top_in[0], top)
        sum_ref[0] = sum_in[0] + total
        sq_ref[0] = sq_in[0] + square


def correlate_chunk(spec_re, spec_im, templ_re, templ_im, forward, inverse, stats):
    count, extent = (spec_re.shape[0], spec_re.shape[-1])
    tiles = templ_re.shape[0]
    first = stats is None
    plane = pl.BlockSpec((1, extent, extent), lambda s: (s, 0, 0))
    templ_spec = pl.BlockSpec((tiles, extent, extent), lambda s: (0, 0, 0))
    fw_spec = pl.BlockSpec(forward.shape, lambda s: (0, 0))
    inv_spec = pl.BlockSpec(inverse.shape, lambda s: (0, 0))
    in_specs = [plane, plane, templ_spec, templ_spec, fw_spec, inv_spec]
    operands = [spec_re, spec_im, templ_re, templ_im, forward, inverse]
    aliases = {}
    if not first:
        in_specs += [plane, plane, plane]
        operands += list(stats)
        aliases = {6: 0, 7: 1, 8: 2}
    map_shape = jax.ShapeDtypeStruct((count, extent, extent), jnp.float32)
    flops = tiles * count * 12 * extent * extent * extent
    outs = pl.pallas_call(
        functools.partial(corr_kernel, first, tiles),
        grid=(count,),
        in_specs=in_specs,
        out_specs=[plane, plane, plane,
                   pl.BlockSpec((1, tiles, 8, 128), lambda s: (s, 0, 0, 0))],
        out_shape=[map_shape, map_shape, map_shape,
                   jax.ShapeDtypeStruct((count, tiles, 8, 128), jnp.float32)],
        input_output_aliases=aliases,
        compiler_params=pltpu.CompilerParams(dimension_semantics=("arbitrary",)),
        cost_estimate=pl.CostEstimate(
            flops=flops, transcendentals=0,
            bytes_accessed=tiles * 4 * extent * extent * 2 + count * 10 * extent * extent * 4),
    )(*operands)
    return outs[:3], outs[3][:, :, 0, 0]


def correlate_all(spec_re, spec_im, templ_re, templ_im, orientation, cosine, sine):
    blocks = lax.axis_size("blk")
    me = lax.axis_index("blk")
    tiles = templ_re.shape[0]
    extent = cosine.shape[0]
    forward = jnp.concatenate(
        [jnp.concatenate([cosine, sine], axis=1), jnp.concatenate([-sine, cosine], axis=1)], axis=0
    )
    scale = jnp.asarray(1.0 / extent, jnp.bfloat16)
    inverse = jnp.concatenate([cosine * scale, -sine * scale], axis=1)
    stats, peak = correlate_chunk(spec_re, spec_im, templ_re, templ_im, forward, inverse, None)
    peaks = [(me, peak)]
    for k in range(1, blocks):
        pairs = [(b, b ^ k) for b in range(blocks)]
        got_re = lax.ppermute(templ_re, "blk", pairs)
        got_im = lax.ppermute(templ_im, "blk", pairs)
        stats, peak = correlate_chunk(spec_re, spec_im, got_re, got_im, forward, inverse, stats)
        peaks.append((me ^ k, peak))
    top_map, totals, squares = stats
    orient_total = orientation.shape[0]
    count = spec_re.shape[0]
    peak_rows = jnp.zeros((count, orient_total), jnp.float32)
    within = jnp.arange(tiles, dtype=jnp.int32)
    for source, peak in peaks:
        columns = jnp.take(orientation, source * tiles + within)
        peak_rows = peak_rows.at[:, columns].set(peak)
    mean_map = totals / orient_total
    var_map = squares / orient_total - mean_map * mean_map
    return (top_map, mean_map, var_map, peak_rows)


def body(patches, owner_of_patch, group_of_patch, defocus, templ_re, templ_im, orientation):
    sources = lax.axis_size("patch")
    my_index = lax.axis_index("patch")
    number, extent = (patches.shape[0], patches.shape[1])
    cosine, sine = dft_tables(extent)
    row_owner = owner_of_patch.reshape(sources, number)
    my_slots, slot_row = route_patches(patches, row_owner, my_index)
    groups = jnp.take(jnp.concatenate([group_of_patch, jnp.zeros((1,), jnp.int32)]), slot_row)
    focus_values = jnp.take(defocus, groups)
    spec_re, spec_im = make_spectra(my_slots, focus_values, cosine, sine)
    return correlate_all(spec_re, spec_im, templ_re, templ_im, orientation, cosine, sine)


def solution(mesh):
    placed = (
        P(("blk", "patch"), None, None),
        P("blk"),
        P("blk"),
        P(),
        P("blk", None, None),
        P("blk", None, None),
        P(),
    )
    return jax.shard_map(
        body,
        mesh=mesh,
        in_specs=placed,
        out_specs=(
            P(("blk", "patch"), None, None),
            P(("blk", "patch"), None, None),
            P(("blk", "patch"), None, None),
            P(("blk", "patch"), None),
        ),
        check_vma=False,
    )
```

```python
import functools
import math

import jax
import jax.numpy as jnp
from jax import lax
from jax.experimental import pallas as pl
from jax.experimental.pallas import tpu as pltpu
from jax.sharding import PartitionSpec as P

SLOT = 2
CAP = 4
TILE_T = 4


AMPLITUDE = 0.07


def dft_tables(extent):
    indices = jnp.arange(extent, dtype=jnp.int32)
    turn_count = indices[:, None] * indices[None, :] % extent
    angles = turn_count.astype(jnp.float32) * (2.0 * math.pi / extent)
    return (jnp.cos(angles).astype(jnp.bfloat16), jnp.sin(angles).astype(jnp.bfloat16))


def ctf_filter(defocus_values, extent):
    indices = jnp.arange(extent, dtype=jnp.int32)
    signed = (
        jnp.where(indices < extent // 2, indices, indices - extent).astype(jnp.float32) / extent
    )
    radius = signed[:, None] * signed[:, None] + signed[None, :] * signed[None, :]
    phases = math.pi * defocus_values[:, None, None] * radius[None, :, :] - AMPLITUDE
    return -jnp.sin(phases)


def xor_pairs(count, shift):
    return [(d, d ^ shift) for d in range(count)]


def route_patches(patches, row_owner, my_index):
    sources, number = row_owner.shape
    extent = patches.shape[-1]
    chips = sources // 2
    devs = jnp.arange(sources, dtype=jnp.int32)
    chip_of = devs // 2
    owner_chip = row_owner // 2
    masks = [row_owner == (devs ^ 1)[:, None]]
    for m in range(1, chips):
        masks.append(owner_chip == (chip_of ^ m)[:, None])
    match = jnp.stack(masks, axis=1)
    first = jnp.where(match[..., 0], 0, jnp.where(match[..., 1], 1, number))
    second = jnp.where(match[..., 0] & match[..., 1], 1, number)
    send_sel = jnp.stack([first, second], axis=-1)
    send_pid = jnp.where(send_sel < number, devs[:, None, None] * number + send_sel, -1)
    padded = jnp.concatenate([patches, jnp.zeros((1, extent, extent), patches.dtype)], axis=0)
    my_sel = lax.dynamic_index_in_dim(send_sel, my_index, 0, keepdims=False)
    outgoing = jnp.take(padded, my_sel.reshape(-1), axis=0).reshape(chips, 2, extent, extent)
    partner = my_index ^ 1
    my_chip = my_index // 2
    direct = lax.ppermute(outgoing[0], "patch", xor_pairs(sources, 1))
    received = []
    for m in range(1, chips):
        received.append(lax.ppermute(outgoing[m], "patch", xor_pairs(sources, 2 * m)))
    received = jnp.concatenate(received, axis=0)
    forwarded = lax.ppermute(received, "patch", xor_pairs(sources, 1))
    cand_pid = [my_index * number + jnp.arange(number, dtype=jnp.int32)]
    cand_pid.append(lax.dynamic_index_in_dim(send_pid, partner, 0, keepdims=False)[0])
    for core in (my_index % 2, partner % 2):
        for m in range(1, chips):
            source = (my_chip ^ m) * 2 + core
            cand_pid.append(lax.dynamic_index_in_dim(send_pid, source, 0, keepdims=False)[m])
    cand_pid = jnp.concatenate(cand_pid)
    flat_owner = row_owner.reshape(-1)
    hits = (flat_owner == my_index).astype(jnp.int32)
    rank_in = jnp.cumsum(hits) - hits
    slot_ids = jnp.arange(CAP, dtype=jnp.int32)
    wanted = (hits[None, :] == 1) & (rank_in[None, :] == slot_ids[:, None])
    patch_ids = jnp.arange(sources * number, dtype=jnp.int32)
    slot_pid = jnp.sum(jnp.where(wanted, patch_ids[None, :], 0), axis=1)
    present = jnp.any(wanted, axis=1)
    cand_ids = jnp.arange(cand_pid.shape[0], dtype=jnp.int32)
    found = cand_pid[None, :] == slot_pid[:, None]
    take_idx = jnp.sum(jnp.where(found, cand_ids[None, :], 0), axis=1)
    take_idx = jnp.where(present, take_idx, cand_pid.shape[0])
    pieces = (patches, direct, received, forwarded)
    return take_idx, pieces, jnp.where(present, slot_pid, sources * number)


def spectra_kernel(rows, take_ref, own_ref, direct_ref, recv_ref, fwd_ref, scale_ref, half_ref,
                   full_ref, re_ref, im_ref):
    s = pl.program_id(0)
    idx = take_ref[s]
    number = own_ref.shape[0]
    pick_own = own_ref[jnp.clip(idx, 0, number - 1)]
    pick_direct = direct_ref[jnp.clip(idx - number, 0, number - 1)]
    pick_recv = recv_ref[jnp.clip(idx - 2 * number, 0, rows - 1)]
    pick_fwd = fwd_ref[jnp.clip(idx - 2 * number - rows, 0, rows - 1)]
    zero = jnp.zeros_like(pick_own)
    image = jnp.where(
        idx < number, pick_own,
        jnp.where(idx < 2 * number, pick_direct,
                  jnp.where(idx < 2 * number + rows, pick_recv,
                            jnp.where(idx < 2 * number + 2 * rows, pick_fwd, zero))))
    extent = image.shape[-1]
    half = jnp.dot(image, half_ref[...], preferred_element_type=jnp.float32).astype(jnp.bfloat16)
    half_stack = jnp.concatenate([half[:, :extent], half[:, extent:]], axis=0)
    spec = jnp.dot(full_ref[...], half_stack, preferred_element_type=jnp.float32)
    scale = scale_ref[0]
    re_ref[0] = (spec[:extent] * scale).astype(jnp.bfloat16)
    im_ref[0] = (spec[extent:] * scale).astype(jnp.bfloat16)


def make_spectra(take_idx, own, direct, received, forwarded, scale, half_table, full_table):
    count, extent = (scale.shape[0], scale.shape[-1])
    rows = received.shape[0]
    whole = pl.BlockSpec(memory_space=pltpu.VMEM)
    plane = pl.BlockSpec((1, extent, extent), lambda s: (s, 0, 0))
    spec_shape = jax.ShapeDtypeStruct((count, extent, extent), jnp.bfloat16)
    return pl.pallas_call(
        functools.partial(spectra_kernel, rows),
        grid=(count,),
        in_specs=[pl.BlockSpec(memory_space=pltpu.SMEM), whole, whole, whole, whole, plane,
                  pl.BlockSpec(half_table.shape, lambda s: (0, 0)),
                  pl.BlockSpec(full_table.shape, lambda s: (0, 0))],
        out_specs=[plane, plane],
        out_shape=[spec_shape, spec_shape],
        compiler_params=pltpu.CompilerParams(dimension_semantics=("arbitrary",)),
        cost_estimate=pl.CostEstimate(
            flops=count * 6 * extent * extent * extent, transcendentals=0,
            bytes_accessed=count * 10 * extent * extent),
    )(take_idx, own, direct, received, forwarded, scale, half_table, full_table)


def corr_kernel(first, last, tiles, orient_total, *refs):
    if first:
        (orient_ref, sr_ref, si_ref, tr_ref, ti_ref, fw_ref, inv_ref,
         top_ref, sum_ref, sq_ref, peak_ref) = refs
    else:
        (orient_ref, sr_ref, si_ref, tr_ref, ti_ref, fw_ref, inv_ref, top_in, sum_in, sq_in, peak_in,
         top_ref, sum_ref, sq_ref, peak_ref) = refs
    extent = sr_ref.shape[-1]
    sr = sr_ref[0].astype(jnp.float32)
    si = si_ref[0].astype(jnp.float32)
    forward = fw_ref[...]
    inverse = inv_ref[...]
    lanes = lax.broadcasted_iota(jnp.int32, peak_ref.shape[1:], 1)
    peak_row = jnp.zeros(peak_ref.shape[1:], jnp.float32) if first else peak_in[0]
    top = total = square = None
    for t in range(tiles):
        tr = tr_ref[t].astype(jnp.float32)
        ti = ti_ref[t].astype(jnp.float32)
        pre = (sr * tr + si * ti).astype(jnp.bfloat16)
        pim = (si * tr - sr * ti).astype(jnp.bfloat16)
        prod = jnp.concatenate([pre, pim], axis=1)
        q = jnp.dot(prod, forward, preferred_element_type=jnp.float32).astype(jnp.bfloat16)
        q_stack = jnp.concatenate([q[:, :extent], q[:, extent:]], axis=0)
        corr = jnp.dot(inverse, q_stack, preferred_element_type=jnp.float32)
        peak_row = jnp.where(lanes == orient_ref[t], jnp.max(corr), peak_row)
        if top is None:
            top, total, square = corr, corr, corr * corr
        else:
            top = jnp.maximum(top, corr)
            total = total + corr
            square = square + corr * corr
    if not first:
        top = jnp.maximum(top_in[0], top)
        total = sum_in[0] + total
        square = sq_in[0] + square
    top_ref[0] = top
    peak_ref[0] = peak_row
    if last:
        mean = total / orient_total
        sum_ref[0] = mean
        sq_ref[0] = square / orient_total - mean * mean
    else:
        sum_ref[0] = total
        sq_ref[0] = square


def correlate_chunk(spec_re, spec_im, templ_re, templ_im, forward, inverse, orient_chunk,
                    orient_total, stats, last):
    count, extent = (spec_re.shape[0], spec_re.shape[-1])
    tiles = templ_re.shape[0]
    first = stats is None
    lanes = 128 * ((orient_total + 127) // 128)
    plane = pl.BlockSpec((1, extent, extent), lambda s: (s, 0, 0))
    peak_spec = pl.BlockSpec((1, 8, lanes), lambda s: (s, 0, 0))
    templ_spec = pl.BlockSpec((tiles, extent, extent), lambda s: (0, 0, 0))
    fw_spec = pl.BlockSpec(forward.shape, lambda s: (0, 0))
    inv_spec = pl.BlockSpec(inverse.shape, lambda s: (0, 0))
    in_specs = [pl.BlockSpec(memory_space=pltpu.SMEM), plane, plane, templ_spec, templ_spec,
                fw_spec, inv_spec]
    operands = [orient_chunk, spec_re, spec_im, templ_re, templ_im, forward, inverse]
    aliases = {}
    if not first:
        in_specs += [plane, plane, plane, peak_spec]
        operands += list(stats)
        aliases = {7: 0, 8: 1, 9: 2, 10: 3}
    map_shape = jax.ShapeDtypeStruct((count, extent, extent), jnp.float32)
    flops = tiles * count * 12 * extent * extent * extent
    return pl.pallas_call(
        functools.partial(corr_kernel, first, last, tiles, orient_total),
        grid=(count,),
        in_specs=in_specs,
        out_specs=[plane, plane, plane, peak_spec],
        out_shape=[map_shape, map_shape, map_shape,
                   jax.ShapeDtypeStruct((count, 8, lanes), jnp.float32)],
        input_output_aliases=aliases,
        compiler_params=pltpu.CompilerParams(dimension_semantics=("arbitrary",)),
        cost_estimate=pl.CostEstimate(
            flops=flops, transcendentals=0,
            bytes_accessed=tiles * 4 * extent * extent * 2 + count * 10 * extent * extent * 4),
    )(*operands)


def correlate_all(spec_re, spec_im, templ_re, templ_im, orientation, forward, inverse):
    blocks = lax.axis_size("blk")
    me = lax.axis_index("blk")
    tiles = templ_re.shape[0]
    orient_total = orientation.shape[0]
    within = jnp.arange(tiles, dtype=jnp.int32)
    chunks = [(me, templ_re, templ_im)]
    for k in range(1, blocks):
        pairs = [(b, b ^ k) for b in range(blocks)]
        chunks.append((me ^ k, lax.ppermute(templ_re, "blk", pairs),
                       lax.ppermute(templ_im, "blk", pairs)))
    stats = None
    for n, (source, got_re, got_im) in enumerate(chunks):
        orient_chunk = jnp.take(orientation, source * tiles + within)
        stats = correlate_chunk(spec_re, spec_im, got_re, got_im, forward, inverse, orient_chunk,
                                orient_total, stats, n == len(chunks) - 1)
    top_map, mean_map, var_map, peak = stats
    return (top_map, mean_map, var_map, peak[:, 0, :orient_total])


def body(patches, owner_of_patch, group_of_patch, defocus, templ_re, templ_im, orientation):
    sources = lax.axis_size("patch")
    my_index = lax.axis_index("patch")
    number, extent = (patches.shape[0], patches.shape[1])
    cosine, sine = dft_tables(extent)
    row_owner = owner_of_patch.reshape(sources, number)
    take_idx, pieces, slot_row = route_patches(patches, row_owner, my_index)
    groups = jnp.take(jnp.concatenate([group_of_patch, jnp.zeros((1,), jnp.int32)]), slot_row)
    focus_values = jnp.take(defocus, groups)
    scale = ctf_filter(focus_values, extent) / extent
    forward = jnp.concatenate(
        [jnp.concatenate([cosine, sine], axis=1), jnp.concatenate([-sine, cosine], axis=1)], axis=0
    )
    half_table = jnp.concatenate([cosine, -sine], axis=1)
    inverse = half_table * jnp.asarray(1.0 / extent, jnp.bfloat16)
    spec_re, spec_im = make_spectra(take_idx, *pieces, scale, half_table, forward)
    return correlate_all(spec_re, spec_im, templ_re, templ_im, orientation, forward, inverse)


def solution(mesh):
    placed = (
        P(("blk", "patch"), None, None),
        P("blk"),
        P("blk"),
        P(),
        P("blk", None, None),
        P("blk", None, None),
        P(),
    )
    return jax.shard_map(
        body,
        mesh=mesh,
        in_specs=placed,
        out_specs=(
            P(("blk", "patch"), None, None),
            P(("blk", "patch"), None, None),
            P(("blk", "patch"), None, None),
            P(("blk", "patch"), None),
        ),
        check_vma=False,
    )
```

```python
import functools
import math

import jax
import jax.numpy as jnp
from jax import lax
from jax.experimental import pallas as pl
from jax.experimental.pallas import tpu as pltpu
from jax.sharding import PartitionSpec as P

SLOT = 2
CAP = 4
TILE_T = 4


AMPLITUDE = 0.07


def dft_tables(extent):
    indices = jnp.arange(extent, dtype=jnp.int32)
    turn_count = indices[:, None] * indices[None, :] % extent
    angles = turn_count.astype(jnp.float32) * (2.0 * math.pi / extent)
    return (jnp.cos(angles).astype(jnp.bfloat16), jnp.sin(angles).astype(jnp.bfloat16))


def ctf_filter(defocus_values, extent):
    indices = jnp.arange(extent, dtype=jnp.int32)
    signed = (
        jnp.where(indices < extent // 2, indices, indices - extent).astype(jnp.float32) / extent
    )
    radius = signed[:, None] * signed[:, None] + signed[None, :] * signed[None, :]
    phases = math.pi * defocus_values[:, None, None] * radius[None, :, :] - AMPLITUDE
    return -jnp.sin(phases)


def ctf_scale(defocus_values, extent):
    indices = jnp.arange(extent, dtype=jnp.int32)
    signed = (
        jnp.where(indices < extent // 2, indices, indices - extent).astype(jnp.float32) / extent
    )
    square = signed * signed
    turn = math.pi * defocus_values[:, None]
    row_phase = turn * square[None, :] - AMPLITUDE
    col_phase = turn * square[None, :]
    row_sin, row_cos = jnp.sin(row_phase), jnp.cos(row_phase)
    col_sin, col_cos = jnp.sin(col_phase), jnp.cos(col_phase)
    ctf = -(row_sin[:, :, None] * col_cos[:, None, :] + row_cos[:, :, None] * col_sin[:, None, :])
    return ctf / extent


def xor_pairs(count, shift):
    return [(d, d ^ shift) for d in range(count)]


def route_patches(patches, row_owner, my_index):
    sources, number = row_owner.shape
    extent = patches.shape[-1]
    chips = sources // 2
    devs = jnp.arange(sources, dtype=jnp.int32)
    chip_of = devs // 2
    owner_chip = row_owner // 2
    masks = [row_owner == (devs ^ 1)[:, None]]
    for m in range(1, chips):
        masks.append(owner_chip == (chip_of ^ m)[:, None])
    match = jnp.stack(masks, axis=1)
    first = jnp.where(match[..., 0], 0, jnp.where(match[..., 1], 1, number))
    second = jnp.where(match[..., 0] & match[..., 1], 1, number)
    send_sel = jnp.stack([first, second], axis=-1)
    send_pid = jnp.where(send_sel < number, devs[:, None, None] * number + send_sel, -1)
    padded = jnp.concatenate([patches, jnp.zeros((1, extent, extent), patches.dtype)], axis=0)
    my_sel = lax.dynamic_index_in_dim(send_sel, my_index, 0, keepdims=False)
    outgoing = jnp.take(padded, my_sel.reshape(-1), axis=0).reshape(chips, 2, extent, extent)
    partner = my_index ^ 1
    my_chip = my_index // 2
    direct = lax.ppermute(outgoing[0], "patch", xor_pairs(sources, 1))
    received = []
    for m in range(1, chips):
        received.append(lax.ppermute(outgoing[m], "patch", xor_pairs(sources, 2 * m)))
    received = jnp.concatenate(received, axis=0)
    forwarded = lax.ppermute(received, "patch", xor_pairs(sources, 1))
    cand_pid = [my_index * number + jnp.arange(number, dtype=jnp.int32)]
    cand_pid.append(lax.dynamic_index_in_dim(send_pid, partner, 0, keepdims=False)[0])
    for core in (my_index % 2, partner % 2):
        for m in range(1, chips):
            source = (my_chip ^ m) * 2 + core
            cand_pid.append(lax.dynamic_index_in_dim(send_pid, source, 0, keepdims=False)[m])
    cand_pid = jnp.concatenate(cand_pid)
    flat_owner = row_owner.reshape(-1)
    hits = (flat_owner == my_index).astype(jnp.int32)
    rank_in = jnp.cumsum(hits) - hits
    slot_ids = jnp.arange(CAP, dtype=jnp.int32)
    wanted = (hits[None, :] == 1) & (rank_in[None, :] == slot_ids[:, None])
    patch_ids = jnp.arange(sources * number, dtype=jnp.int32)
    slot_pid = jnp.sum(jnp.where(wanted, patch_ids[None, :], 0), axis=1)
    present = jnp.any(wanted, axis=1)
    cand_ids = jnp.arange(cand_pid.shape[0], dtype=jnp.int32)
    found = cand_pid[None, :] == slot_pid[:, None]
    take_idx = jnp.sum(jnp.where(found, cand_ids[None, :], 0), axis=1)
    take_idx = jnp.where(present, take_idx, cand_pid.shape[0])
    pieces = (patches, direct, received, forwarded)
    return take_idx, pieces, jnp.where(present, slot_pid, sources * number)


def spectra_kernel(rows, take_ref, own_ref, direct_ref, recv_ref, fwd_ref, scale_ref, half_ref,
                   full_ref, re_ref, im_ref):
    s = pl.program_id(0)
    idx = take_ref[s]
    number = own_ref.shape[0]
    pick_own = own_ref[jnp.clip(idx, 0, number - 1)]
    pick_direct = direct_ref[jnp.clip(idx - number, 0, number - 1)]
    pick_recv = recv_ref[jnp.clip(idx - 2 * number, 0, rows - 1)]
    pick_fwd = fwd_ref[jnp.clip(idx - 2 * number - rows, 0, rows - 1)]
    zero = jnp.zeros_like(pick_own)
    image = jnp.where(
        idx < number, pick_own,
        jnp.where(idx < 2 * number, pick_direct,
                  jnp.where(idx < 2 * number + rows, pick_recv,
                            jnp.where(idx < 2 * number + 2 * rows, pick_fwd, zero))))
    extent = image.shape[-1]
    half = jnp.dot(image, half_ref[...], preferred_element_type=jnp.float32).astype(jnp.bfloat16)
    half_stack = jnp.concatenate([half[:, :extent], half[:, extent:]], axis=0)
    spec = jnp.dot(full_ref[...], half_stack, preferred_element_type=jnp.float32)
    scale = scale_ref[0]
    re_ref[0] = (spec[:extent] * scale).astype(jnp.bfloat16)
    im_ref[0] = (spec[extent:] * scale).astype(jnp.bfloat16)


def make_spectra(take_idx, own, direct, received, forwarded, scale, half_table, full_table):
    count, extent = (scale.shape[0], scale.shape[-1])
    rows = received.shape[0]
    whole = pl.BlockSpec(memory_space=pltpu.VMEM)
    plane = pl.BlockSpec((1, extent, extent), lambda s: (s, 0, 0))
    spec_shape = jax.ShapeDtypeStruct((count, extent, extent), jnp.bfloat16)
    return pl.pallas_call(
        functools.partial(spectra_kernel, rows),
        grid=(count,),
        in_specs=[pl.BlockSpec(memory_space=pltpu.SMEM), whole, whole, whole, whole, plane,
                  pl.BlockSpec(half_table.shape, lambda s: (0, 0)),
                  pl.BlockSpec(full_table.shape, lambda s: (0, 0))],
        out_specs=[plane, plane],
        out_shape=[spec_shape, spec_shape],
        compiler_params=pltpu.CompilerParams(dimension_semantics=("arbitrary",)),
        cost_estimate=pl.CostEstimate(
            flops=3 * count * 6 * extent * extent * extent, transcendentals=0,
            bytes_accessed=count * 10 * extent * extent),
    )(take_idx, own, direct, received, forwarded, scale, half_table, full_table)


def corr_kernel(first, last, tiles, orient_total, *refs):
    if first:
        (orient_ref, sr_ref, si_ref, tr_ref, ti_ref, fw_ref, inv_ref,
         top_ref, sum_ref, sq_ref, peak_ref) = refs
    else:
        (orient_ref, sr_ref, si_ref, tr_ref, ti_ref, fw_ref, inv_ref, top_in, sum_in, sq_in, peak_in,
         top_ref, sum_ref, sq_ref, peak_ref) = refs
    extent = sr_ref.shape[-1]
    sr = sr_ref[0].astype(jnp.float32)
    si = si_ref[0].astype(jnp.float32)
    forward = fw_ref[...]
    inverse = inv_ref[...]
    lanes = lax.broadcasted_iota(jnp.int32, peak_ref.shape[1:], 1)
    peak_row = jnp.zeros(peak_ref.shape[1:], jnp.float32) if first else peak_in[0]
    top = total = square = None
    for t in range(tiles):
        tr = tr_ref[t].astype(jnp.float32)
        ti = ti_ref[t].astype(jnp.float32)
        pre = (sr * tr + si * ti).astype(jnp.bfloat16)
        pim = (si * tr - sr * ti).astype(jnp.bfloat16)
        prod = jnp.concatenate([pre, pim], axis=1)
        q = jnp.dot(prod, forward, preferred_element_type=jnp.float32).astype(jnp.bfloat16)
        q_stack = jnp.concatenate([q[:, :extent], q[:, extent:]], axis=0)
        corr = jnp.dot(inverse, q_stack, preferred_element_type=jnp.float32)
        peak_row = jnp.where(lanes == orient_ref[t], jnp.max(corr), peak_row)
        if top is None:
            top, total, square = corr, corr, corr * corr
        else:
            top = jnp.maximum(top, corr)
            total = total + corr
            square = square + corr * corr
    if not first:
        top = jnp.maximum(top_in[0], top)
        total = sum_in[0] + total
        square = sq_in[0] + square
    top_ref[0] = top
    peak_ref[0] = peak_row
    if last:
        mean = total / orient_total
        sum_ref[0] = mean
        sq_ref[0] = square / orient_total - mean * mean
    else:
        sum_ref[0] = total
        sq_ref[0] = square


def correlate_chunk(spec_re, spec_im, templ_re, templ_im, forward, inverse, orient_chunk,
                    orient_total, stats, last):
    count, extent = (spec_re.shape[0], spec_re.shape[-1])
    tiles = templ_re.shape[0]
    first = stats is None
    lanes = 128 * ((orient_total + 127) // 128)
    plane = pl.BlockSpec((1, extent, extent), lambda s: (s, 0, 0))
    peak_spec = pl.BlockSpec((1, 8, lanes), lambda s: (s, 0, 0))
    templ_spec = pl.BlockSpec((tiles, extent, extent), lambda s: (0, 0, 0))
    fw_spec = pl.BlockSpec(forward.shape, lambda s: (0, 0))
    inv_spec = pl.BlockSpec(inverse.shape, lambda s: (0, 0))
    in_specs = [pl.BlockSpec(memory_space=pltpu.SMEM), plane, plane, templ_spec, templ_spec,
                fw_spec, inv_spec]
    operands = [orient_chunk, spec_re, spec_im, templ_re, templ_im, forward, inverse]
    aliases = {}
    if not first:
        in_specs += [plane, plane, plane, peak_spec]
        operands += list(stats)
        aliases = {7: 0, 8: 1, 9: 2, 10: 3}
    map_shape = jax.ShapeDtypeStruct((count, extent, extent), jnp.float32)
    flops = 3 * tiles * count * 12 * extent * extent * extent
    return pl.pallas_call(
        functools.partial(corr_kernel, first, last, tiles, orient_total),
        grid=(count,),
        in_specs=in_specs,
        out_specs=[plane, plane, plane, peak_spec],
        out_shape=[map_shape, map_shape, map_shape,
                   jax.ShapeDtypeStruct((count, 8, lanes), jnp.float32)],
        input_output_aliases=aliases,
        compiler_params=pltpu.CompilerParams(dimension_semantics=("arbitrary",)),
        cost_estimate=pl.CostEstimate(
            flops=flops, transcendentals=0,
            bytes_accessed=tiles * 4 * extent * extent * 2 + count * 10 * extent * extent * 4),
    )(*operands)


def correlate_all(spec_re, spec_im, templ_re, templ_im, orientation, forward, inverse):
    blocks = lax.axis_size("blk")
    me = lax.axis_index("blk")
    tiles = templ_re.shape[0]
    orient_total = orientation.shape[0]
    within = jnp.arange(tiles, dtype=jnp.int32)
    chunks = [(me, templ_re, templ_im)]
    for k in range(1, blocks):
        pairs = [(b, b ^ k) for b in range(blocks)]
        chunks.append((me ^ k, lax.ppermute(templ_re, "blk", pairs),
                       lax.ppermute(templ_im, "blk", pairs)))
    stats = None
    for n, (source, got_re, got_im) in enumerate(chunks):
        orient_chunk = jnp.take(orientation, source * tiles + within)
        stats = correlate_chunk(spec_re, spec_im, got_re, got_im, forward, inverse, orient_chunk,
                                orient_total, stats, n == len(chunks) - 1)
    top_map, mean_map, var_map, peak = stats
    return (top_map, mean_map, var_map, peak[:, 0, :orient_total])


def body(patches, owner_of_patch, group_of_patch, defocus, templ_re, templ_im, orientation):
    sources = lax.axis_size("patch")
    my_index = lax.axis_index("patch")
    number, extent = (patches.shape[0], patches.shape[1])
    cosine, sine = dft_tables(extent)
    row_owner = owner_of_patch.reshape(sources, number)
    take_idx, pieces, slot_row = route_patches(patches, row_owner, my_index)
    groups = jnp.take(jnp.concatenate([group_of_patch, jnp.zeros((1,), jnp.int32)]), slot_row)
    focus_values = jnp.take(defocus, groups)
    scale = ctf_scale(focus_values, extent)
    forward = jnp.concatenate(
        [jnp.concatenate([cosine, sine], axis=1), jnp.concatenate([-sine, cosine], axis=1)], axis=0
    )
    half_table = jnp.concatenate([cosine, -sine], axis=1)
    inverse = half_table * jnp.asarray(1.0 / extent, jnp.bfloat16)
    spec_re, spec_im = make_spectra(take_idx, *pieces, scale, half_table, forward)
    return correlate_all(spec_re, spec_im, templ_re, templ_im, orientation, forward, inverse)


def solution(mesh):
    placed = (
        P(("blk", "patch"), None, None),
        P("blk"),
        P("blk"),
        P(),
        P("blk", None, None),
        P("blk", None, None),
        P(),
    )
    return jax.shard_map(
        body,
        mesh=mesh,
        in_specs=placed,
        out_specs=(
            P(("blk", "patch"), None, None),
            P(("blk", "patch"), None, None),
            P(("blk", "patch"), None, None),
            P(("blk", "patch"), None),
        ),
        check_vma=False,
    )
```

```python
import functools
import math

import jax
import jax.numpy as jnp
from jax import lax
from jax.experimental import pallas as pl
from jax.experimental.pallas import tpu as pltpu
from jax.sharding import PartitionSpec as P

SLOT = 2
CAP = 4
TILE_T = 4


AMPLITUDE = 0.07


def dft_tables(extent):
    indices = jnp.arange(extent, dtype=jnp.int32)
    turn_count = indices[:, None] * indices[None, :] % extent
    angles = turn_count.astype(jnp.float32) * (2.0 * math.pi / extent)
    return (jnp.cos(angles).astype(jnp.bfloat16), jnp.sin(angles).astype(jnp.bfloat16))


def ctf_filter(defocus_values, extent):
    indices = jnp.arange(extent, dtype=jnp.int32)
    signed = (
        jnp.where(indices < extent // 2, indices, indices - extent).astype(jnp.float32) / extent
    )
    radius = signed[:, None] * signed[:, None] + signed[None, :] * signed[None, :]
    phases = math.pi * defocus_values[:, None, None] * radius[None, :, :] - AMPLITUDE
    return -jnp.sin(phases)


def ctf_scale(defocus_values, extent):
    indices = jnp.arange(extent, dtype=jnp.int32)
    signed = (
        jnp.where(indices < extent // 2, indices, indices - extent).astype(jnp.float32) / extent
    )
    square = signed * signed
    turn = math.pi * defocus_values[:, None]
    row_phase = turn * square[None, :] - AMPLITUDE
    col_phase = turn * square[None, :]
    row_sin, row_cos = jnp.sin(row_phase), jnp.cos(row_phase)
    col_sin, col_cos = jnp.sin(col_phase), jnp.cos(col_phase)
    ctf = -(row_sin[:, :, None] * col_cos[:, None, :] + row_cos[:, :, None] * col_sin[:, None, :])
    return ctf / extent


def xor_pairs(count, shift):
    return [(d, d ^ shift) for d in range(count)]


def route_patches(patches, row_owner, my_index):
    sources, number = row_owner.shape
    extent = patches.shape[-1]
    chips = sources // 2
    devs = jnp.arange(sources, dtype=jnp.int32)
    chip_of = devs // 2
    owner_chip = row_owner // 2
    masks = [row_owner == (devs ^ 1)[:, None]]
    for m in range(1, chips):
        masks.append(owner_chip == (chip_of ^ m)[:, None])
    match = jnp.stack(masks, axis=1)
    first = jnp.where(match[..., 0], 0, jnp.where(match[..., 1], 1, number))
    second = jnp.where(match[..., 0] & match[..., 1], 1, number)
    send_sel = jnp.stack([first, second], axis=-1)
    send_pid = jnp.where(send_sel < number, devs[:, None, None] * number + send_sel, -1)
    padded = jnp.concatenate([patches, jnp.zeros((1, extent, extent), patches.dtype)], axis=0)
    my_sel = lax.dynamic_index_in_dim(send_sel, my_index, 0, keepdims=False)
    outgoing = jnp.take(padded, my_sel.reshape(-1), axis=0).reshape(chips, 2, extent, extent)
    partner = my_index ^ 1
    my_chip = my_index // 2
    direct = lax.ppermute(outgoing[0], "patch", xor_pairs(sources, 1))
    received = []
    for m in range(1, chips):
        received.append(lax.ppermute(outgoing[m], "patch", xor_pairs(sources, 2 * m)))
    received = jnp.concatenate(received, axis=0)
    forwarded = lax.ppermute(received, "patch", xor_pairs(sources, 1))
    cand_pid = [my_index * number + jnp.arange(number, dtype=jnp.int32)]
    cand_pid.append(lax.dynamic_index_in_dim(send_pid, partner, 0, keepdims=False)[0])
    for core in (my_index % 2, partner % 2):
        for m in range(1, chips):
            source = (my_chip ^ m) * 2 + core
            cand_pid.append(lax.dynamic_index_in_dim(send_pid, source, 0, keepdims=False)[m])
    cand_pid = jnp.concatenate(cand_pid)
    flat_owner = row_owner.reshape(-1)
    hits = (flat_owner == my_index).astype(jnp.int32)
    rank_in = jnp.cumsum(hits) - hits
    slot_ids = jnp.arange(CAP, dtype=jnp.int32)
    wanted = (hits[None, :] == 1) & (rank_in[None, :] == slot_ids[:, None])
    patch_ids = jnp.arange(sources * number, dtype=jnp.int32)
    slot_pid = jnp.sum(jnp.where(wanted, patch_ids[None, :], 0), axis=1)
    present = jnp.any(wanted, axis=1)
    cand_ids = jnp.arange(cand_pid.shape[0], dtype=jnp.int32)
    found = cand_pid[None, :] == slot_pid[:, None]
    take_idx = jnp.sum(jnp.where(found, cand_ids[None, :], 0), axis=1)
    take_idx = jnp.where(present, take_idx, cand_pid.shape[0])
    pieces = (patches, direct, received, forwarded)
    return take_idx, pieces, jnp.where(present, slot_pid, sources * number)


def spectra_kernel(rows, take_ref, own_ref, direct_ref, recv_ref, fwd_ref, scale_ref, half_ref,
                   full_ref, re_ref, im_ref):
    s = pl.program_id(0)
    idx = take_ref[s]
    number = own_ref.shape[0]
    pick_own = own_ref[jnp.clip(idx, 0, number - 1)]
    pick_direct = direct_ref[jnp.clip(idx - number, 0, number - 1)]
    pick_recv = recv_ref[jnp.clip(idx - 2 * number, 0, rows - 1)]
    pick_fwd = fwd_ref[jnp.clip(idx - 2 * number - rows, 0, rows - 1)]
    zero = jnp.zeros_like(pick_own)
    image = jnp.where(
        idx < number, pick_own,
        jnp.where(idx < 2 * number, pick_direct,
                  jnp.where(idx < 2 * number + rows, pick_recv,
                            jnp.where(idx < 2 * number + 2 * rows, pick_fwd, zero))))
    extent = image.shape[-1]
    half = jnp.dot(image, half_ref[...], preferred_element_type=jnp.float32).astype(jnp.bfloat16)
    half_stack = jnp.concatenate([half[:, :extent], half[:, extent:]], axis=0)
    spec = jnp.dot(full_ref[...], half_stack, preferred_element_type=jnp.float32)
    scale = scale_ref[0]
    re_ref[0] = (spec[:extent] * scale).astype(jnp.bfloat16)
    im_ref[0] = (spec[extent:] * scale).astype(jnp.bfloat16)


def make_spectra(take_idx, own, direct, received, forwarded, scale, half_table, full_table):
    count, extent = (scale.shape[0], scale.shape[-1])
    rows = received.shape[0]
    whole = pl.BlockSpec(memory_space=pltpu.VMEM)
    plane = pl.BlockSpec((1, extent, extent), lambda s: (s, 0, 0))
    spec_shape = jax.ShapeDtypeStruct((count, extent, extent), jnp.bfloat16)
    return pl.pallas_call(
        functools.partial(spectra_kernel, rows),
        grid=(count,),
        in_specs=[pl.BlockSpec(memory_space=pltpu.SMEM), whole, whole, whole, whole, plane,
                  pl.BlockSpec(half_table.shape, lambda s: (0, 0)),
                  pl.BlockSpec(full_table.shape, lambda s: (0, 0))],
        out_specs=[plane, plane],
        out_shape=[spec_shape, spec_shape],
        compiler_params=pltpu.CompilerParams(dimension_semantics=("arbitrary",)),
        cost_estimate=pl.CostEstimate(
            flops=3 * count * 6 * extent * extent * extent, transcendentals=0,
            bytes_accessed=count * 10 * extent * extent),
    )(take_idx, own, direct, received, forwarded, scale, half_table, full_table)


def corr_kernel(first, last, counts, orient_total, *refs):
    groups = len(counts)
    orient_ref, sr_ref, si_ref = refs[:3]
    templ_refs = refs[3:3 + groups]
    fw_ref, inv_ref = refs[3 + groups:5 + groups]
    rest = refs[5 + groups:]
    if first:
        top_ref, sum_ref, sq_ref, peak_ref = rest
    else:
        top_in, sum_in, sq_in, peak_in, top_ref, sum_ref, sq_ref, peak_ref = rest
    extent = sr_ref.shape[-1]
    sr = sr_ref[0].astype(jnp.float32)
    si = si_ref[0].astype(jnp.float32)
    forward = fw_ref[...]
    inverse = inv_ref[...]
    lanes = lax.broadcasted_iota(jnp.int32, peak_ref.shape[1:], 1)
    peak_row = jnp.zeros(peak_ref.shape[1:], jnp.float32) if first else peak_in[0]
    top = total = square = None
    position = 0
    for templ_ref, count in zip(templ_refs, counts):
        for t in range(count):
            tr = templ_ref[t].astype(jnp.float32)
            ti = templ_ref[count + t].astype(jnp.float32)
            pre = (sr * tr + si * ti).astype(jnp.bfloat16)
            pim = (si * tr - sr * ti).astype(jnp.bfloat16)
            prod = jnp.concatenate([pre, pim], axis=1)
            q = jnp.dot(prod, forward, preferred_element_type=jnp.float32).astype(jnp.bfloat16)
            q_stack = jnp.concatenate([q[:, :extent], q[:, extent:]], axis=0)
            corr = jnp.dot(inverse, q_stack, preferred_element_type=jnp.float32)
            peak_row = jnp.where(lanes == orient_ref[position], jnp.max(corr), peak_row)
            position += 1
            if top is None:
                top, total, square = corr, corr, corr * corr
            else:
                top = jnp.maximum(top, corr)
                total = total + corr
                square = square + corr * corr
    if not first:
        top = jnp.maximum(top_in[0], top)
        total = sum_in[0] + total
        square = sq_in[0] + square
    top_ref[0] = top
    peak_ref[0] = peak_row
    if last:
        mean = total / orient_total
        sum_ref[0] = mean
        sq_ref[0] = square / orient_total - mean * mean
    else:
        sum_ref[0] = total
        sq_ref[0] = square


def correlate_chunk(spec_re, spec_im, templ_groups, forward, inverse, orient_chunk,
                    orient_total, stats, last):
    count, extent = (spec_re.shape[0], spec_re.shape[-1])
    counts = tuple(group.shape[0] // 2 for group in templ_groups)
    tiles = sum(counts)
    first = stats is None
    lanes = 128 * ((orient_total + 127) // 128)
    plane = pl.BlockSpec((1, extent, extent), lambda s: (s, 0, 0))
    peak_spec = pl.BlockSpec((1, 8, lanes), lambda s: (s, 0, 0))
    templ_specs = [pl.BlockSpec(group.shape, lambda s: (0, 0, 0)) for group in templ_groups]
    fw_spec = pl.BlockSpec(forward.shape, lambda s: (0, 0))
    inv_spec = pl.BlockSpec(inverse.shape, lambda s: (0, 0))
    in_specs = [pl.BlockSpec(memory_space=pltpu.SMEM), plane, plane] + templ_specs + [
        fw_spec, inv_spec]
    operands = [orient_chunk, spec_re, spec_im] + list(templ_groups) + [forward, inverse]
    aliases = {}
    if not first:
        base = len(operands)
        in_specs += [plane, plane, plane, peak_spec]
        operands += list(stats)
        aliases = {base: 0, base + 1: 1, base + 2: 2, base + 3: 3}
    map_shape = jax.ShapeDtypeStruct((count, extent, extent), jnp.float32)
    flops = 3 * tiles * count * 12 * extent * extent * extent
    return pl.pallas_call(
        functools.partial(corr_kernel, first, last, counts, orient_total),
        grid=(count,),
        in_specs=in_specs,
        out_specs=[plane, plane, plane, peak_spec],
        out_shape=[map_shape, map_shape, map_shape,
                   jax.ShapeDtypeStruct((count, 8, lanes), jnp.float32)],
        input_output_aliases=aliases,
        compiler_params=pltpu.CompilerParams(dimension_semantics=("arbitrary",)),
        cost_estimate=pl.CostEstimate(
            flops=flops, transcendentals=0,
            bytes_accessed=tiles * 4 * extent * extent * 2 + count * 10 * extent * extent * 4),
    )(*operands)


def correlate_all(spec_re, spec_im, templ_re, templ_im, orientation, forward, inverse):
    blocks = lax.axis_size("blk")
    me = lax.axis_index("blk")
    sources = lax.axis_size("patch")
    core = lax.axis_index("patch") % 2
    tiles = templ_re.shape[0]
    half = tiles // 2
    orient_total = orientation.shape[0]
    local = jnp.concatenate([templ_re, templ_im], axis=0)
    mine = jnp.concatenate(
        [lax.dynamic_slice_in_dim(templ_re, core * half, half, 0),
         lax.dynamic_slice_in_dim(templ_im, core * half, half, 0)], axis=0)
    within = jnp.arange(half, dtype=jnp.int32)
    chunks = [([local], me * tiles + jnp.arange(tiles, dtype=jnp.int32))]
    for k in range(1, blocks):
        source = me ^ k
        got = lax.ppermute(mine, "blk", [(b, b ^ k) for b in range(blocks)])
        passed = lax.ppermute(got, "patch", xor_pairs(sources, 1))
        index = jnp.concatenate(
            [source * tiles + core * half + within, source * tiles + (1 - core) * half + within])
        chunks.append(([got, passed], index))
    stats = None
    for n, (groups, index) in enumerate(chunks):
        orient_chunk = jnp.take(orientation, index)
        stats = correlate_chunk(spec_re, spec_im, groups, forward, inverse, orient_chunk,
                                orient_total, stats, n == len(chunks) - 1)
    top_map, mean_map, var_map, peak = stats
    return (top_map, mean_map, var_map, peak[:, 0, :orient_total])


def body(patches, owner_of_patch, group_of_patch, defocus, templ_re, templ_im, orientation):
    sources = lax.axis_size("patch")
    my_index = lax.axis_index("patch")
    number, extent = (patches.shape[0], patches.shape[1])
    cosine, sine = dft_tables(extent)
    row_owner = owner_of_patch.reshape(sources, number)
    take_idx, pieces, slot_row = route_patches(patches, row_owner, my_index)
    groups = jnp.take(jnp.concatenate([group_of_patch, jnp.zeros((1,), jnp.int32)]), slot_row)
    focus_values = jnp.take(defocus, groups)
    scale = ctf_scale(focus_values, extent)
    forward = jnp.concatenate(
        [jnp.concatenate([cosine, sine], axis=1), jnp.concatenate([-sine, cosine], axis=1)], axis=0
    )
    half_table = jnp.concatenate([cosine, -sine], axis=1)
    inverse = half_table * jnp.asarray(1.0 / extent, jnp.bfloat16)
    spec_re, spec_im = make_spectra(take_idx, *pieces, scale, half_table, forward)
    return correlate_all(spec_re, spec_im, templ_re, templ_im, orientation, forward, inverse)


def solution(mesh):
    placed = (
        P(("blk", "patch"), None, None),
        P("blk"),
        P("blk"),
        P(),
        P("blk", None, None),
        P("blk", None, None),
        P(),
    )
    return jax.shard_map(
        body,
        mesh=mesh,
        in_specs=placed,
        out_specs=(
            P(("blk", "patch"), None, None),
            P(("blk", "patch"), None, None),
            P(("blk", "patch"), None, None),
            P(("blk", "patch"), None),
        ),
        check_vma=False,
    )
```

```python
import functools
import math

import jax
import ml_dtypes
import numpy as np
import jax.numpy as jnp
from jax import lax
from jax.experimental import pallas as pl
from jax.experimental.pallas import tpu as pltpu
from jax.sharding import PartitionSpec as P

SLOT = 2
CAP = 4
TILE_T = 4


AMPLITUDE = 0.07


def dft_tables(extent):
    indices = np.arange(extent, dtype=np.int64)
    turn_count = indices[:, None] * indices[None, :] % extent
    angles = turn_count.astype(np.float32) * np.float32(2.0 * math.pi / extent)
    cosine = np.cos(angles).astype(ml_dtypes.bfloat16)
    sine = np.sin(angles).astype(ml_dtypes.bfloat16)
    forward = np.concatenate(
        [np.concatenate([cosine, sine], axis=1), np.concatenate([-sine, cosine], axis=1)], axis=0
    )
    half_table = np.concatenate([cosine, -sine], axis=1)
    inverse = (half_table.astype(np.float32) / extent).astype(ml_dtypes.bfloat16)
    return forward, half_table, inverse


def ctf_filter(defocus_values, extent):
    indices = jnp.arange(extent, dtype=jnp.int32)
    signed = (
        jnp.where(indices < extent // 2, indices, indices - extent).astype(jnp.float32) / extent
    )
    radius = signed[:, None] * signed[:, None] + signed[None, :] * signed[None, :]
    phases = math.pi * defocus_values[:, None, None] * radius[None, :, :] - AMPLITUDE
    return -jnp.sin(phases)


def ctf_scale(defocus_values, extent):
    indices = jnp.arange(extent, dtype=jnp.int32)
    signed = (
        jnp.where(indices < extent // 2, indices, indices - extent).astype(jnp.float32) / extent
    )
    square = signed * signed
    turn = math.pi * defocus_values[:, None]
    row_phase = turn * square[None, :] - AMPLITUDE
    col_phase = turn * square[None, :]
    row_sin, row_cos = jnp.sin(row_phase), jnp.cos(row_phase)
    col_sin, col_cos = jnp.sin(col_phase), jnp.cos(col_phase)
    ctf = -(row_sin[:, :, None] * col_cos[:, None, :] + row_cos[:, :, None] * col_sin[:, None, :])
    return ctf / extent


def xor_pairs(count, shift):
    return [(d, d ^ shift) for d in range(count)]


def route_patches(patches, row_owner, my_index):
    sources, number = row_owner.shape
    extent = patches.shape[-1]
    chips = sources // 2
    devs = jnp.arange(sources, dtype=jnp.int32)
    chip_of = devs // 2
    owner_chip = row_owner // 2
    masks = [row_owner == (devs ^ 1)[:, None]]
    for m in range(1, chips):
        masks.append(owner_chip == (chip_of ^ m)[:, None])
    match = jnp.stack(masks, axis=1)
    first = jnp.where(match[..., 0], 0, jnp.where(match[..., 1], 1, number))
    second = jnp.where(match[..., 0] & match[..., 1], 1, number)
    send_sel = jnp.stack([first, second], axis=-1)
    send_pid = jnp.where(send_sel < number, devs[:, None, None] * number + send_sel, -1)
    padded = jnp.concatenate([patches, jnp.zeros((1, extent, extent), patches.dtype)], axis=0)
    my_sel = lax.dynamic_index_in_dim(send_sel, my_index, 0, keepdims=False)
    outgoing = jnp.take(padded, my_sel.reshape(-1), axis=0).reshape(chips, 2, extent, extent)
    partner = my_index ^ 1
    my_chip = my_index // 2
    direct = lax.ppermute(outgoing[0], "patch", xor_pairs(sources, 1))
    received = []
    for m in range(1, chips):
        received.append(lax.ppermute(outgoing[m], "patch", xor_pairs(sources, 2 * m)))
    received = jnp.concatenate(received, axis=0)
    forwarded = lax.ppermute(received, "patch", xor_pairs(sources, 1))
    cand_pid = [my_index * number + jnp.arange(number, dtype=jnp.int32)]
    cand_pid.append(lax.dynamic_index_in_dim(send_pid, partner, 0, keepdims=False)[0])
    for core in (my_index % 2, partner % 2):
        for m in range(1, chips):
            source = (my_chip ^ m) * 2 + core
            cand_pid.append(lax.dynamic_index_in_dim(send_pid, source, 0, keepdims=False)[m])
    cand_pid = jnp.concatenate(cand_pid)
    flat_owner = row_owner.reshape(-1)
    hits = (flat_owner == my_index).astype(jnp.int32)
    rank_in = jnp.cumsum(hits) - hits
    slot_ids = jnp.arange(CAP, dtype=jnp.int32)
    wanted = (hits[None, :] == 1) & (rank_in[None, :] == slot_ids[:, None])
    patch_ids = jnp.arange(sources * number, dtype=jnp.int32)
    slot_pid = jnp.sum(jnp.where(wanted, patch_ids[None, :], 0), axis=1)
    present = jnp.any(wanted, axis=1)
    cand_ids = jnp.arange(cand_pid.shape[0], dtype=jnp.int32)
    found = cand_pid[None, :] == slot_pid[:, None]
    take_idx = jnp.sum(jnp.where(found, cand_ids[None, :], 0), axis=1)
    take_idx = jnp.where(present, take_idx, cand_pid.shape[0])
    pieces = (patches, direct, received, forwarded)
    return take_idx, pieces, jnp.where(present, slot_pid, sources * number), outgoing


def spectra_kernel(rows, take_ref, own_ref, direct_ref, recv_ref, fwd_ref, scale_ref, half_ref,
                   full_ref, re_ref, im_ref):
    s = pl.program_id(0)
    idx = take_ref[s]
    number = own_ref.shape[0]
    pick_own = own_ref[jnp.clip(idx, 0, number - 1)]
    pick_direct = direct_ref[jnp.clip(idx - number, 0, number - 1)]
    pick_recv = recv_ref[jnp.clip(idx - 2 * number, 0, rows - 1)]
    pick_fwd = fwd_ref[jnp.clip(idx - 2 * number - rows, 0, rows - 1)]
    zero = jnp.zeros_like(pick_own)
    image = jnp.where(
        idx < number, pick_own,
        jnp.where(idx < 2 * number, pick_direct,
                  jnp.where(idx < 2 * number + rows, pick_recv,
                            jnp.where(idx < 2 * number + 2 * rows, pick_fwd, zero))))
    extent = image.shape[-1]
    half = jnp.dot(image, half_ref[...], preferred_element_type=jnp.float32).astype(jnp.bfloat16)
    half_stack = jnp.concatenate([half[:, :extent], half[:, extent:]], axis=0)
    spec = jnp.dot(full_ref[...], half_stack, preferred_element_type=jnp.float32)
    scale = scale_ref[0]
    re_ref[0] = (spec[:extent] * scale).astype(jnp.bfloat16)
    im_ref[0] = (spec[extent:] * scale).astype(jnp.bfloat16)


def make_spectra(take_idx, own, direct, received, forwarded, scale, half_table, full_table):
    count, extent = (scale.shape[0], scale.shape[-1])
    rows = received.shape[0]
    whole = pl.BlockSpec(memory_space=pltpu.VMEM)
    plane = pl.BlockSpec((1, extent, extent), lambda s: (s, 0, 0))
    spec_shape = jax.ShapeDtypeStruct((count, extent, extent), jnp.bfloat16)
    return pl.pallas_call(
        functools.partial(spectra_kernel, rows),
        grid=(count,),
        in_specs=[pl.BlockSpec(memory_space=pltpu.SMEM), whole, whole, whole, whole, plane,
                  pl.BlockSpec(half_table.shape, lambda s: (0, 0)),
                  pl.BlockSpec(full_table.shape, lambda s: (0, 0))],
        out_specs=[plane, plane],
        out_shape=[spec_shape, spec_shape],
        compiler_params=pltpu.CompilerParams(dimension_semantics=("arbitrary",)),
        cost_estimate=pl.CostEstimate(
            flops=3 * count * 6 * extent * extent * extent, transcendentals=0,
            bytes_accessed=count * 10 * extent * extent),
    )(take_idx, own, direct, received, forwarded, scale, half_table, full_table)


def corr_kernel(first, last, counts, orient_total, *refs):
    groups = len(counts)
    orient_ref, sr_ref, si_ref = refs[:3]
    templ_refs = refs[3:3 + groups]
    fw_ref, inv_ref = refs[3 + groups:5 + groups]
    rest = refs[5 + groups:]
    if first:
        top_ref, sum_ref, sq_ref, peak_ref = rest
    else:
        top_in, sum_in, sq_in, peak_in, top_ref, sum_ref, sq_ref, peak_ref = rest
    extent = sr_ref.shape[-1]
    sr = sr_ref[0].astype(jnp.float32)
    si = si_ref[0].astype(jnp.float32)
    forward = fw_ref[...]
    inverse = inv_ref[...]
    lanes = lax.broadcasted_iota(jnp.int32, peak_ref.shape[1:], 1)
    peak_row = jnp.zeros(peak_ref.shape[1:], jnp.float32) if first else peak_in[0]
    top = total = square = None
    position = 0
    for templ_ref, count in zip(templ_refs, counts):
        for t in range(count):
            tr = templ_ref[t].astype(jnp.float32)
            ti = templ_ref[count + t].astype(jnp.float32)
            pre = (sr * tr + si * ti).astype(jnp.bfloat16)
            pim = (si * tr - sr * ti).astype(jnp.bfloat16)
            prod = jnp.concatenate([pre, pim], axis=1)
            q = jnp.dot(prod, forward, preferred_element_type=jnp.float32).astype(jnp.bfloat16)
            q_stack = jnp.concatenate([q[:, :extent], q[:, extent:]], axis=0)
            corr = jnp.dot(inverse, q_stack, preferred_element_type=jnp.float32)
            peak_row = jnp.where(lanes == orient_ref[position], jnp.max(corr), peak_row)
            position += 1
            if top is None:
                top, total, square = corr, corr, corr * corr
            else:
                top = jnp.maximum(top, corr)
                total = total + corr
                square = square + corr * corr
    if not first:
        top = jnp.maximum(top_in[0], top)
        total = sum_in[0] + total
        square = sq_in[0] + square
    top_ref[0] = top
    peak_ref[0] = peak_row
    if last:
        mean = total / orient_total
        sum_ref[0] = mean
        sq_ref[0] = square / orient_total - mean * mean
    else:
        sum_ref[0] = total
        sq_ref[0] = square


def correlate_chunk(spec_re, spec_im, templ_groups, forward, inverse, orient_chunk,
                    orient_total, stats, last):
    count, extent = (spec_re.shape[0], spec_re.shape[-1])
    counts = tuple(group.shape[0] // 2 for group in templ_groups)
    tiles = sum(counts)
    first = stats is None
    lanes = 128 * ((orient_total + 127) // 128)
    plane = pl.BlockSpec((1, extent, extent), lambda s: (s, 0, 0))
    peak_spec = pl.BlockSpec((1, 8, lanes), lambda s: (s, 0, 0))
    templ_specs = [pl.BlockSpec(group.shape, lambda s: (0, 0, 0)) for group in templ_groups]
    fw_spec = pl.BlockSpec(forward.shape, lambda s: (0, 0))
    inv_spec = pl.BlockSpec(inverse.shape, lambda s: (0, 0))
    in_specs = [pl.BlockSpec(memory_space=pltpu.SMEM), plane, plane] + templ_specs + [
        fw_spec, inv_spec]
    operands = [orient_chunk, spec_re, spec_im] + list(templ_groups) + [forward, inverse]
    aliases = {}
    if not first:
        base = len(operands)
        in_specs += [plane, plane, plane, peak_spec]
        operands += list(stats)
        aliases = {base: 0, base + 1: 1, base + 2: 2, base + 3: 3}
    map_shape = jax.ShapeDtypeStruct((count, extent, extent), jnp.float32)
    flops = 3 * tiles * count * 12 * extent * extent * extent
    return pl.pallas_call(
        functools.partial(corr_kernel, first, last, counts, orient_total),
        grid=(count,),
        in_specs=in_specs,
        out_specs=[plane, plane, plane, peak_spec],
        out_shape=[map_shape, map_shape, map_shape,
                   jax.ShapeDtypeStruct((count, 8, lanes), jnp.float32)],
        input_output_aliases=aliases,
        compiler_params=pltpu.CompilerParams(dimension_semantics=("arbitrary",)),
        cost_estimate=pl.CostEstimate(
            flops=flops, transcendentals=0,
            bytes_accessed=tiles * 4 * extent * extent * 2 + count * 10 * extent * extent * 4),
    )(*operands)


def correlate_all(spec_re, spec_im, templ_re, templ_im, orientation, forward, inverse):
    blocks = lax.axis_size("blk")
    me = lax.axis_index("blk")
    sources = lax.axis_size("patch")
    core = lax.axis_index("patch") % 2
    tiles = templ_re.shape[0]
    half = tiles // 2
    orient_total = orientation.shape[0]
    local = jnp.concatenate([templ_re, templ_im], axis=0)
    mine = jnp.concatenate(
        [lax.dynamic_slice_in_dim(templ_re, core * half, half, 0),
         lax.dynamic_slice_in_dim(templ_im, core * half, half, 0)], axis=0)
    within = jnp.arange(half, dtype=jnp.int32)
    chunks = [([local], me * tiles + jnp.arange(tiles, dtype=jnp.int32))]
    for k in range(1, blocks):
        source = me ^ k
        got = lax.ppermute(mine, "blk", [(b, b ^ k) for b in range(blocks)])
        passed = lax.ppermute(got, "patch", xor_pairs(sources, 1))
        index = jnp.concatenate(
            [source * tiles + core * half + within, source * tiles + (1 - core) * half + within])
        chunks.append(([got, passed], index))
    stats = None
    for n, (groups, index) in enumerate(chunks):
        orient_chunk = jnp.take(orientation, index)
        stats = correlate_chunk(spec_re, spec_im, groups, forward, inverse, orient_chunk,
                                orient_total, stats, n == len(chunks) - 1)
    top_map, mean_map, var_map, peak = stats
    return (top_map, mean_map, var_map, peak[:, 0, :orient_total])


def body(patches, owner_of_patch, group_of_patch, defocus, templ_re, templ_im, orientation):
    sources = lax.axis_size("patch")
    my_index = lax.axis_index("patch")
    number, extent = (patches.shape[0], patches.shape[1])
    forward, half_table, inverse = (jnp.asarray(table) for table in dft_tables(extent))
    row_owner = owner_of_patch.reshape(sources, number)
    take_idx, pieces, slot_row, outgoing = route_patches(patches, row_owner, my_index)
    templ_re, templ_im, unused = lax.optimization_barrier((templ_re, templ_im, outgoing))
    groups = jnp.take(jnp.concatenate([group_of_patch, jnp.zeros((1,), jnp.int32)]), slot_row)
    focus_values = jnp.take(defocus, groups)
    scale = ctf_scale(focus_values, extent)
    spec_re, spec_im = make_spectra(take_idx, *pieces, scale, half_table, forward)
    return correlate_all(spec_re, spec_im, templ_re, templ_im, orientation, forward, inverse)


def solution(mesh):
    placed = (
        P(("blk", "patch"), None, None),
        P("blk"),
        P("blk"),
        P(),
        P("blk", None, None),
        P("blk", None, None),
        P(),
    )
    return jax.shard_map(
        body,
        mesh=mesh,
        in_specs=placed,
        out_specs=(
            P(("blk", "patch"), None, None),
            P(("blk", "patch"), None, None),
            P(("blk", "patch"), None, None),
            P(("blk", "patch"), None),
        ),
        check_vma=False,
    )
```

```python
import functools
import math

import jax
import ml_dtypes
import numpy as np
import jax.numpy as jnp
from jax import lax
from jax.experimental import pallas as pl
from jax.experimental.pallas import tpu as pltpu
from jax.sharding import PartitionSpec as P

SLOT = 2
CAP = 4
TILE_T = 4


AMPLITUDE = 0.07


def dft_tables(extent):
    indices = np.arange(extent, dtype=np.int64)
    turn_count = indices[:, None] * indices[None, :] % extent
    angles = turn_count.astype(np.float32) * np.float32(2.0 * math.pi / extent)
    cosine = np.cos(angles).astype(ml_dtypes.bfloat16)
    sine = np.sin(angles).astype(ml_dtypes.bfloat16)
    forward = np.concatenate(
        [np.concatenate([cosine, sine], axis=1), np.concatenate([-sine, cosine], axis=1)], axis=0
    )
    half_table = np.concatenate([cosine, -sine], axis=1)
    inverse = (half_table.astype(np.float32) / extent).astype(ml_dtypes.bfloat16)
    return forward, half_table, inverse


def ctf_filter(defocus_values, extent):
    indices = jnp.arange(extent, dtype=jnp.int32)
    signed = (
        jnp.where(indices < extent // 2, indices, indices - extent).astype(jnp.float32) / extent
    )
    radius = signed[:, None] * signed[:, None] + signed[None, :] * signed[None, :]
    phases = math.pi * defocus_values[:, None, None] * radius[None, :, :] - AMPLITUDE
    return -jnp.sin(phases)


def ctf_scale(defocus_values, extent):
    indices = jnp.arange(extent, dtype=jnp.int32)
    signed = (
        jnp.where(indices < extent // 2, indices, indices - extent).astype(jnp.float32) / extent
    )
    square = signed * signed
    turn = math.pi * defocus_values[:, None]
    row_phase = turn * square[None, :] - AMPLITUDE
    col_phase = turn * square[None, :]
    row_sin, row_cos = jnp.sin(row_phase), jnp.cos(row_phase)
    col_sin, col_cos = jnp.sin(col_phase), jnp.cos(col_phase)
    ctf = -(row_sin[:, :, None] * col_cos[:, None, :] + row_cos[:, :, None] * col_sin[:, None, :])
    return ctf / extent


def xor_pairs(count, shift):
    return [(d, d ^ shift) for d in range(count)]


def route_patches(patches, row_owner, my_index):
    sources, number = row_owner.shape
    extent = patches.shape[-1]
    chips = sources // 2
    devs = jnp.arange(sources, dtype=jnp.int32)
    chip_of = devs // 2
    owner_chip = row_owner // 2
    masks = [row_owner == (devs ^ 1)[:, None]]
    for m in range(1, chips):
        masks.append(owner_chip == (chip_of ^ m)[:, None])
    match = jnp.stack(masks, axis=1)
    first = jnp.where(match[..., 0], 0, jnp.where(match[..., 1], 1, number))
    second = jnp.where(match[..., 0] & match[..., 1], 1, number)
    send_sel = jnp.stack([first, second], axis=-1)
    send_pid = jnp.where(send_sel < number, devs[:, None, None] * number + send_sel, -1)
    padded = jnp.concatenate([patches, jnp.zeros((1, extent, extent), patches.dtype)], axis=0)
    my_sel = lax.dynamic_index_in_dim(send_sel, my_index, 0, keepdims=False)
    outgoing = jnp.take(padded, my_sel.reshape(-1), axis=0).reshape(chips, 2, extent, extent)
    partner = my_index ^ 1
    my_chip = my_index // 2
    direct = lax.ppermute(outgoing[0], "patch", xor_pairs(sources, 1))
    received = []
    for m in range(1, chips):
        received.append(lax.ppermute(outgoing[m], "patch", xor_pairs(sources, 2 * m)))
    received = jnp.concatenate(received, axis=0)
    forwarded = lax.ppermute(received, "patch", xor_pairs(sources, 1))
    cand_pid = [my_index * number + jnp.arange(number, dtype=jnp.int32)]
    cand_pid.append(lax.dynamic_index_in_dim(send_pid, partner, 0, keepdims=False)[0])
    for core in (my_index % 2, partner % 2):
        for m in range(1, chips):
            source = (my_chip ^ m) * 2 + core
            cand_pid.append(lax.dynamic_index_in_dim(send_pid, source, 0, keepdims=False)[m])
    cand_pid = jnp.concatenate(cand_pid)
    flat_owner = row_owner.reshape(-1)
    hits = (flat_owner == my_index).astype(jnp.int32)
    rank_in = jnp.cumsum(hits) - hits
    slot_ids = jnp.arange(CAP, dtype=jnp.int32)
    wanted = (hits[None, :] == 1) & (rank_in[None, :] == slot_ids[:, None])
    patch_ids = jnp.arange(sources * number, dtype=jnp.int32)
    slot_pid = jnp.sum(jnp.where(wanted, patch_ids[None, :], 0), axis=1)
    present = jnp.any(wanted, axis=1)
    cand_ids = jnp.arange(cand_pid.shape[0], dtype=jnp.int32)
    found = cand_pid[None, :] == slot_pid[:, None]
    take_idx = jnp.sum(jnp.where(found, cand_ids[None, :], 0), axis=1)
    take_idx = jnp.where(present, take_idx, cand_pid.shape[0])
    pieces = (patches, direct, received, forwarded)
    return take_idx, pieces, jnp.where(present, slot_pid, sources * number), outgoing


def spectra_kernel(rows, take_ref, own_ref, direct_ref, recv_ref, fwd_ref, scale_ref, half_ref,
                   full_ref, re_ref, im_ref):
    number = own_ref.shape[0]
    extent = own_ref.shape[-1]
    half_table = half_ref[...]
    full_table = full_ref[...]
    for s in range(re_ref.shape[0]):
        idx = take_ref[s]
        pick_own = own_ref[jnp.clip(idx, 0, number - 1)]
        pick_direct = direct_ref[jnp.clip(idx - number, 0, number - 1)]
        pick_recv = recv_ref[jnp.clip(idx - 2 * number, 0, rows - 1)]
        pick_fwd = fwd_ref[jnp.clip(idx - 2 * number - rows, 0, rows - 1)]
        zero = jnp.zeros_like(pick_own)
        image = jnp.where(
            idx < number, pick_own,
            jnp.where(idx < 2 * number, pick_direct,
                      jnp.where(idx < 2 * number + rows, pick_recv,
                                jnp.where(idx < 2 * number + 2 * rows, pick_fwd, zero))))
        half = jnp.dot(image, half_table, preferred_element_type=jnp.float32).astype(jnp.bfloat16)
        half_stack = jnp.concatenate([half[:, :extent], half[:, extent:]], axis=0)
        spec = jnp.dot(full_table, half_stack, preferred_element_type=jnp.float32)
        scale = scale_ref[s]
        re_ref[s] = (spec[:extent] * scale).astype(jnp.bfloat16)
        im_ref[s] = (spec[extent:] * scale).astype(jnp.bfloat16)


def make_spectra(take_idx, own, direct, received, forwarded, scale, half_table, full_table):
    count, extent = (scale.shape[0], scale.shape[-1])
    rows = received.shape[0]
    whole = pl.BlockSpec(memory_space=pltpu.VMEM)
    spec_shape = jax.ShapeDtypeStruct((count, extent, extent), jnp.bfloat16)
    return pl.pallas_call(
        functools.partial(spectra_kernel, rows),
        in_specs=[pl.BlockSpec(memory_space=pltpu.SMEM)] + [whole] * 7,
        out_specs=[whole, whole],
        out_shape=[spec_shape, spec_shape],
        cost_estimate=pl.CostEstimate(
            flops=3 * count * 6 * extent * extent * extent, transcendentals=0,
            bytes_accessed=count * 10 * extent * extent),
    )(take_idx, own, direct, received, forwarded, scale, half_table, full_table)


def corr_kernel(first, last, counts, orient_total, *refs):
    groups = len(counts)
    orient_ref, sr_ref, si_ref = refs[:3]
    templ_refs = refs[3:3 + groups]
    fw_ref, inv_ref = refs[3 + groups:5 + groups]
    rest = refs[5 + groups:]
    if first:
        top_ref, sum_ref, sq_ref, peak_ref = rest
    else:
        top_in, sum_in, sq_in, peak_in, top_ref, sum_ref, sq_ref, peak_ref = rest
    extent = sr_ref.shape[-1]
    sr = sr_ref[0].astype(jnp.float32)
    si = si_ref[0].astype(jnp.float32)
    forward = fw_ref[...]
    inverse = inv_ref[...]
    lanes = lax.broadcasted_iota(jnp.int32, peak_ref.shape[1:], 1)
    peak_row = jnp.zeros(peak_ref.shape[1:], jnp.float32) if first else peak_in[0]
    top = total = square = None
    prods = []
    for templ_ref, count in zip(templ_refs, counts):
        for t in range(count):
            tr = templ_ref[t].astype(jnp.float32)
            ti = templ_ref[count + t].astype(jnp.float32)
            pre = (sr * tr + si * ti).astype(jnp.bfloat16)
            pim = (si * tr - sr * ti).astype(jnp.bfloat16)
            prods.append(jnp.concatenate([pre, pim], axis=1))
    q_all = jnp.dot(jnp.concatenate(prods, axis=0), forward,
                    preferred_element_type=jnp.float32).astype(jnp.bfloat16)
    for position in range(len(prods)):
        q = q_all[position * extent:(position + 1) * extent]
        q_stack = jnp.concatenate([q[:, :extent], q[:, extent:]], axis=0)
        corr = jnp.dot(inverse, q_stack, preferred_element_type=jnp.float32)
        peak_row = jnp.where(lanes == orient_ref[position], jnp.max(corr), peak_row)
        if top is None:
            top, total, square = corr, corr, corr * corr
        else:
            top = jnp.maximum(top, corr)
            total = total + corr
            square = square + corr * corr
    if not first:
        top = jnp.maximum(top_in[0], top)
        total = sum_in[0] + total
        square = sq_in[0] + square
    top_ref[0] = top
    peak_ref[0] = peak_row
    if last:
        mean = total / orient_total
        sum_ref[0] = mean
        sq_ref[0] = square / orient_total - mean * mean
    else:
        sum_ref[0] = total
        sq_ref[0] = square


def correlate_chunk(spec_re, spec_im, templ_groups, forward, inverse, orient_chunk,
                    orient_total, stats, last):
    count, extent = (spec_re.shape[0], spec_re.shape[-1])
    counts = tuple(group.shape[0] // 2 for group in templ_groups)
    tiles = sum(counts)
    first = stats is None
    lanes = 128 * ((orient_total + 127) // 128)
    plane = pl.BlockSpec((1, extent, extent), lambda s: (s, 0, 0))
    peak_spec = pl.BlockSpec((1, 8, lanes), lambda s: (s, 0, 0))
    templ_specs = [pl.BlockSpec(group.shape, lambda s: (0, 0, 0)) for group in templ_groups]
    fw_spec = pl.BlockSpec(forward.shape, lambda s: (0, 0))
    inv_spec = pl.BlockSpec(inverse.shape, lambda s: (0, 0))
    in_specs = [pl.BlockSpec(memory_space=pltpu.SMEM), plane, plane] + templ_specs + [
        fw_spec, inv_spec]
    operands = [orient_chunk, spec_re, spec_im] + list(templ_groups) + [forward, inverse]
    aliases = {}
    if not first:
        base = len(operands)
        in_specs += [plane, plane, plane, peak_spec]
        operands += list(stats)
        aliases = {base: 0, base + 1: 1, base + 2: 2, base + 3: 3}
    map_shape = jax.ShapeDtypeStruct((count, extent, extent), jnp.float32)
    flops = 3 * tiles * count * 12 * extent * extent * extent
    return pl.pallas_call(
        functools.partial(corr_kernel, first, last, counts, orient_total),
        grid=(count,),
        in_specs=in_specs,
        out_specs=[plane, plane, plane, peak_spec],
        out_shape=[map_shape, map_shape, map_shape,
                   jax.ShapeDtypeStruct((count, 8, lanes), jnp.float32)],
        input_output_aliases=aliases,
        compiler_params=pltpu.CompilerParams(dimension_semantics=("arbitrary",)),
        cost_estimate=pl.CostEstimate(
            flops=flops, transcendentals=0,
            bytes_accessed=tiles * 4 * extent * extent * 2 + count * 10 * extent * extent * 4),
    )(*operands)


def correlate_all(spec_re, spec_im, templ_re, templ_im, orientation, forward, inverse):
    blocks = lax.axis_size("blk")
    me = lax.axis_index("blk")
    sources = lax.axis_size("patch")
    core = lax.axis_index("patch") % 2
    tiles = templ_re.shape[0]
    half = tiles // 2
    orient_total = orientation.shape[0]
    local = jnp.concatenate([templ_re, templ_im], axis=0)
    mine = jnp.concatenate(
        [lax.dynamic_slice_in_dim(templ_re, core * half, half, 0),
         lax.dynamic_slice_in_dim(templ_im, core * half, half, 0)], axis=0)
    within = jnp.arange(half, dtype=jnp.int32)
    chunks = [([local], me * tiles + jnp.arange(tiles, dtype=jnp.int32))]
    for k in range(1, blocks):
        source = me ^ k
        got = lax.ppermute(mine, "blk", [(b, b ^ k) for b in range(blocks)])
        passed = lax.ppermute(got, "patch", xor_pairs(sources, 1))
        index = jnp.concatenate(
            [source * tiles + core * half + within, source * tiles + (1 - core) * half + within])
        chunks.append(([got, passed], index))
    stats = None
    for n, (groups, index) in enumerate(chunks):
        orient_chunk = jnp.take(orientation, index)
        stats = correlate_chunk(spec_re, spec_im, groups, forward, inverse, orient_chunk,
                                orient_total, stats, n == len(chunks) - 1)
    top_map, mean_map, var_map, peak = stats
    return (top_map, mean_map, var_map, peak[:, 0, :orient_total])


def body(patches, owner_of_patch, group_of_patch, defocus, templ_re, templ_im, orientation):
    sources = lax.axis_size("patch")
    my_index = lax.axis_index("patch")
    number, extent = (patches.shape[0], patches.shape[1])
    forward, half_table, inverse = (jnp.asarray(table) for table in dft_tables(extent))
    row_owner = owner_of_patch.reshape(sources, number)
    take_idx, pieces, slot_row, outgoing = route_patches(patches, row_owner, my_index)
    templ_re, templ_im, unused = lax.optimization_barrier((templ_re, templ_im, outgoing))
    groups = jnp.take(jnp.concatenate([group_of_patch, jnp.zeros((1,), jnp.int32)]), slot_row)
    focus_values = jnp.take(defocus, groups)
    scale = ctf_scale(focus_values, extent)
    spec_re, spec_im = make_spectra(take_idx, *pieces, scale, half_table, forward)
    return correlate_all(spec_re, spec_im, templ_re, templ_im, orientation, forward, inverse)


def solution(mesh):
    placed = (
        P(("blk", "patch"), None, None),
        P("blk"),
        P("blk"),
        P(),
        P("blk", None, None),
        P("blk", None, None),
        P(),
    )
    return jax.shard_map(
        body,
        mesh=mesh,
        in_specs=placed,
        out_specs=(
            P(("blk", "patch"), None, None),
            P(("blk", "patch"), None, None),
            P(("blk", "patch"), None, None),
            P(("blk", "patch"), None),
        ),
        check_vma=False,
    )
```

```python
import functools
import math

import jax
import ml_dtypes
import numpy as np
import jax.numpy as jnp
from jax import lax
from jax.experimental import pallas as pl
from jax.experimental.pallas import tpu as pltpu
from jax.sharding import PartitionSpec as P

SLOT = 2
CAP = 4
TILE_T = 4


AMPLITUDE = 0.07


def dft_tables(extent):
    indices = np.arange(extent, dtype=np.int64)
    turn_count = indices[:, None] * indices[None, :] % extent
    angles = turn_count.astype(np.float32) * np.float32(2.0 * math.pi / extent)
    cosine = np.cos(angles).astype(ml_dtypes.bfloat16)
    sine = np.sin(angles).astype(ml_dtypes.bfloat16)
    forward = np.concatenate(
        [np.concatenate([cosine, sine], axis=1), np.concatenate([-sine, cosine], axis=1)], axis=0
    )
    half_table = np.concatenate([cosine, -sine], axis=1)
    inverse = (half_table.astype(np.float32) / extent).astype(ml_dtypes.bfloat16)
    return forward, half_table, inverse


def ctf_filter(defocus_values, extent):
    indices = jnp.arange(extent, dtype=jnp.int32)
    signed = (
        jnp.where(indices < extent // 2, indices, indices - extent).astype(jnp.float32) / extent
    )
    radius = signed[:, None] * signed[:, None] + signed[None, :] * signed[None, :]
    phases = math.pi * defocus_values[:, None, None] * radius[None, :, :] - AMPLITUDE
    return -jnp.sin(phases)


def ctf_scale(defocus_values, extent):
    indices = jnp.arange(extent, dtype=jnp.int32)
    signed = (
        jnp.where(indices < extent // 2, indices, indices - extent).astype(jnp.float32) / extent
    )
    square = signed * signed
    turn = math.pi * defocus_values[:, None]
    row_phase = turn * square[None, :] - AMPLITUDE
    col_phase = turn * square[None, :]
    row_sin, row_cos = jnp.sin(row_phase), jnp.cos(row_phase)
    col_sin, col_cos = jnp.sin(col_phase), jnp.cos(col_phase)
    ctf = -(row_sin[:, :, None] * col_cos[:, None, :] + row_cos[:, :, None] * col_sin[:, None, :])
    return ctf / extent


def xor_pairs(count, shift):
    return [(d, d ^ shift) for d in range(count)]


def route_patches(patches, row_owner, my_index):
    sources, number = row_owner.shape
    extent = patches.shape[-1]
    chips = sources // 2
    devs = jnp.arange(sources, dtype=jnp.int32)
    chip_of = devs // 2
    owner_chip = row_owner // 2
    masks = [row_owner == (devs ^ 1)[:, None]]
    for m in range(1, chips):
        masks.append(owner_chip == (chip_of ^ m)[:, None])
    match = jnp.stack(masks, axis=1)
    first = jnp.where(match[..., 0], 0, jnp.where(match[..., 1], 1, number))
    second = jnp.where(match[..., 0] & match[..., 1], 1, number)
    send_sel = jnp.stack([first, second], axis=-1)
    send_pid = jnp.where(send_sel < number, devs[:, None, None] * number + send_sel, -1)
    padded = jnp.concatenate([patches, jnp.zeros((1, extent, extent), patches.dtype)], axis=0)
    my_sel = lax.dynamic_index_in_dim(send_sel, my_index, 0, keepdims=False)
    outgoing = jnp.take(padded, my_sel.reshape(-1), axis=0).reshape(chips, 2, extent, extent)
    partner = my_index ^ 1
    my_chip = my_index // 2
    direct = lax.ppermute(outgoing[0], "patch", xor_pairs(sources, 1))
    received = []
    for m in range(1, chips):
        received.append(lax.ppermute(outgoing[m], "patch", xor_pairs(sources, 2 * m)))
    received = jnp.concatenate(received, axis=0)
    forwarded = lax.ppermute(received, "patch", xor_pairs(sources, 1))
    cand_pid = [my_index * number + jnp.arange(number, dtype=jnp.int32)]
    cand_pid.append(lax.dynamic_index_in_dim(send_pid, partner, 0, keepdims=False)[0])
    for core in (my_index % 2, partner % 2):
        for m in range(1, chips):
            source = (my_chip ^ m) * 2 + core
            cand_pid.append(lax.dynamic_index_in_dim(send_pid, source, 0, keepdims=False)[m])
    cand_pid = jnp.concatenate(cand_pid)
    flat_owner = row_owner.reshape(-1)
    hits = (flat_owner == my_index).astype(jnp.int32)
    rank_in = jnp.cumsum(hits) - hits
    slot_ids = jnp.arange(CAP, dtype=jnp.int32)
    wanted = (hits[None, :] == 1) & (rank_in[None, :] == slot_ids[:, None])
    patch_ids = jnp.arange(sources * number, dtype=jnp.int32)
    slot_pid = jnp.sum(jnp.where(wanted, patch_ids[None, :], 0), axis=1)
    present = jnp.any(wanted, axis=1)
    cand_ids = jnp.arange(cand_pid.shape[0], dtype=jnp.int32)
    found = cand_pid[None, :] == slot_pid[:, None]
    take_idx = jnp.sum(jnp.where(found, cand_ids[None, :], 0), axis=1)
    take_idx = jnp.where(present, take_idx, cand_pid.shape[0])
    pieces = (patches, direct, received, forwarded)
    return take_idx, pieces, jnp.where(present, slot_pid, sources * number), outgoing


def spectra_kernel(rows, take_ref, own_hbm, direct_hbm, recv_hbm, fwd_hbm, scale_ref, half_ref,
                   full_ref, re_ref, im_ref, buf, sems):
    number = own_hbm.shape[0]
    extent = own_hbm.shape[-1]
    count = re_ref.shape[0]
    pieces = ((own_hbm, 0, number), (direct_hbm, number, number),
              (recv_hbm, 2 * number, rows), (fwd_hbm, 2 * number + rows, rows))
    limit = 2 * number + 2 * rows

    def copies(s):
        idx = take_ref[s]
        found = []
        for piece, base, size in pieces:
            inside = (idx >= base) & (idx < base + size)
            local = jnp.clip(idx - base, 0, size - 1)
            found.append((inside, pltpu.make_async_copy(piece.at[local], buf.at[s], sems.at[s])))
        return idx, found

    for s in range(count):
        idx, found = copies(s)
        for inside, copy in found:
            pl.when(inside)(copy.start)

        @pl.when(idx >= limit)
        def _():
            buf[s] = jnp.zeros((extent, extent), buf.dtype)

    half_table = half_ref[...]
    full_table = full_ref[...]
    for s in range(count):
        idx, found = copies(s)
        for inside, copy in found:
            pl.when(inside)(copy.wait)
        image = buf[s]
        half = jnp.dot(image, half_table, preferred_element_type=jnp.float32).astype(jnp.bfloat16)
        half_stack = jnp.concatenate([half[:, :extent], half[:, extent:]], axis=0)
        spec = jnp.dot(full_table, half_stack, preferred_element_type=jnp.float32)
        scale = scale_ref[s]
        re_ref[s] = (spec[:extent] * scale).astype(jnp.bfloat16)
        im_ref[s] = (spec[extent:] * scale).astype(jnp.bfloat16)


def make_spectra(take_idx, own, direct, received, forwarded, scale, half_table, full_table):
    count, extent = (scale.shape[0], scale.shape[-1])
    rows = received.shape[0]
    whole = pl.BlockSpec(memory_space=pltpu.VMEM)
    far = pl.BlockSpec(memory_space=pl.ANY)
    spec_shape = jax.ShapeDtypeStruct((count, extent, extent), jnp.bfloat16)
    return pl.pallas_call(
        functools.partial(spectra_kernel, rows),
        in_specs=[pl.BlockSpec(memory_space=pltpu.SMEM), far, far, far, far, whole, whole, whole],
        out_specs=[whole, whole],
        out_shape=[spec_shape, spec_shape],
        scratch_shapes=[pltpu.VMEM((count, extent, extent), own.dtype),
                        pltpu.SemaphoreType.DMA((count,))],
        cost_estimate=pl.CostEstimate(
            flops=3 * count * 6 * extent * extent * extent, transcendentals=0,
            bytes_accessed=count * 10 * extent * extent),
    )(take_idx, own, direct, received, forwarded, scale, half_table, full_table)


def corr_kernel(first, last, counts, orient_total, *refs):
    groups = len(counts)
    orient_ref, sr_ref, si_ref = refs[:3]
    templ_refs = refs[3:3 + groups]
    fw_ref, inv_ref = refs[3 + groups:5 + groups]
    rest = refs[5 + groups:]
    if first:
        top_ref, sum_ref, sq_ref, peak_ref = rest
    else:
        top_in, sum_in, sq_in, peak_in, top_ref, sum_ref, sq_ref, peak_ref = rest
    extent = sr_ref.shape[-1]
    sr = sr_ref[0].astype(jnp.float32)
    si = si_ref[0].astype(jnp.float32)
    forward = fw_ref[...]
    inverse = inv_ref[...]
    row_shape = (8, 128 * ((orient_total + 127) // 128))
    lanes = lax.broadcasted_iota(jnp.int32, row_shape, 1)
    peak_row = jnp.zeros(row_shape, jnp.float32) if first else peak_in[0]
    top = total = square = None
    prods = []
    for templ_ref, count in zip(templ_refs, counts):
        for t in range(count):
            tr = templ_ref[t].astype(jnp.float32)
            ti = templ_ref[count + t].astype(jnp.float32)
            pre = (sr * tr + si * ti).astype(jnp.bfloat16)
            pim = (si * tr - sr * ti).astype(jnp.bfloat16)
            prods.append(jnp.concatenate([pre, pim], axis=1))
    q_all = jnp.dot(jnp.concatenate(prods, axis=0), forward,
                    preferred_element_type=jnp.float32).astype(jnp.bfloat16)
    for position in range(len(prods)):
        q = q_all[position * extent:(position + 1) * extent]
        q_stack = jnp.concatenate([q[:, :extent], q[:, extent:]], axis=0)
        corr = jnp.dot(inverse, q_stack, preferred_element_type=jnp.float32)
        peak_row = jnp.where(lanes == orient_ref[position], jnp.max(corr), peak_row)
        if top is None:
            top, total, square = corr, corr, corr * corr
        else:
            top = jnp.maximum(top, corr)
            total = total + corr
            square = square + corr * corr
    if not first:
        top = jnp.maximum(top_in[0], top)
        total = sum_in[0] + total
        square = sq_in[0] + square
    top_ref[0] = top
    if last:
        s = pl.program_id(0)
        peak_ref[pl.ds(s, 1), :] = peak_row[0:1, :orient_total]
    else:
        peak_ref[0] = peak_row
    if last:
        mean = total / orient_total
        sum_ref[0] = mean
        sq_ref[0] = square / orient_total - mean * mean
    else:
        sum_ref[0] = total
        sq_ref[0] = square


def correlate_chunk(spec_re, spec_im, templ_groups, forward, inverse, orient_chunk,
                    orient_total, stats, last):
    count, extent = (spec_re.shape[0], spec_re.shape[-1])
    counts = tuple(group.shape[0] // 2 for group in templ_groups)
    tiles = sum(counts)
    first = stats is None
    lanes = 128 * ((orient_total + 127) // 128)
    plane = pl.BlockSpec((1, extent, extent), lambda s: (s, 0, 0))
    peak_spec = pl.BlockSpec((1, 8, lanes), lambda s: (s, 0, 0))
    templ_specs = [pl.BlockSpec(group.shape, lambda s: (0, 0, 0)) for group in templ_groups]
    fw_spec = pl.BlockSpec(forward.shape, lambda s: (0, 0))
    inv_spec = pl.BlockSpec(inverse.shape, lambda s: (0, 0))
    in_specs = [pl.BlockSpec(memory_space=pltpu.SMEM), plane, plane] + templ_specs + [
        fw_spec, inv_spec]
    operands = [orient_chunk, spec_re, spec_im] + list(templ_groups) + [forward, inverse]
    aliases = {}
    if not first:
        base = len(operands)
        in_specs += [plane, plane, plane, peak_spec]
        operands += list(stats)
        aliases = {base: 0, base + 1: 1, base + 2: 2}
        if not last:
            aliases[base + 3] = 3
    map_shape = jax.ShapeDtypeStruct((count, extent, extent), jnp.float32)
    flops = 3 * tiles * count * 12 * extent * extent * extent
    return pl.pallas_call(
        functools.partial(corr_kernel, first, last, counts, orient_total),
        grid=(count,),
        in_specs=in_specs,
        out_specs=[plane, plane, plane,
                   pl.BlockSpec((count, orient_total), lambda s: (0, 0)) if last else peak_spec],
        out_shape=[map_shape, map_shape, map_shape,
                   jax.ShapeDtypeStruct((count, orient_total) if last else (count, 8, lanes),
                                        jnp.float32)],
        input_output_aliases=aliases,
        compiler_params=pltpu.CompilerParams(dimension_semantics=("arbitrary",)),
        cost_estimate=pl.CostEstimate(
            flops=flops, transcendentals=0,
            bytes_accessed=tiles * 4 * extent * extent * 2 + count * 10 * extent * extent * 4),
    )(*operands)


def correlate_all(spec_re, spec_im, templ_re, templ_im, orientation, forward, inverse):
    blocks = lax.axis_size("blk")
    me = lax.axis_index("blk")
    sources = lax.axis_size("patch")
    core = lax.axis_index("patch") % 2
    tiles = templ_re.shape[0]
    half = tiles // 2
    orient_total = orientation.shape[0]
    local = jnp.concatenate([templ_re, templ_im], axis=0)
    mine = jnp.concatenate(
        [lax.dynamic_slice_in_dim(templ_re, core * half, half, 0),
         lax.dynamic_slice_in_dim(templ_im, core * half, half, 0)], axis=0)
    within = jnp.arange(half, dtype=jnp.int32)
    chunks = [([local], me * tiles + jnp.arange(tiles, dtype=jnp.int32))]
    for k in range(1, blocks):
        source = me ^ k
        got = lax.ppermute(mine, "blk", [(b, b ^ k) for b in range(blocks)])
        passed = lax.ppermute(got, "patch", xor_pairs(sources, 1))
        index = jnp.concatenate(
            [source * tiles + core * half + within, source * tiles + (1 - core) * half + within])
        chunks.append(([got, passed], index))
    stats = None
    for n, (groups, index) in enumerate(chunks):
        orient_chunk = jnp.take(orientation, index)
        stats = correlate_chunk(spec_re, spec_im, groups, forward, inverse, orient_chunk,
                                orient_total, stats, n == len(chunks) - 1)
    top_map, mean_map, var_map, peak = stats
    return (top_map, mean_map, var_map, peak)


def body(patches, owner_of_patch, group_of_patch, defocus, templ_re, templ_im, orientation):
    sources = lax.axis_size("patch")
    my_index = lax.axis_index("patch")
    number, extent = (patches.shape[0], patches.shape[1])
    forward, half_table, inverse = (jnp.asarray(table) for table in dft_tables(extent))
    row_owner = owner_of_patch.reshape(sources, number)
    take_idx, pieces, slot_row, outgoing = route_patches(patches, row_owner, my_index)
    templ_re, templ_im, unused = lax.optimization_barrier((templ_re, templ_im, outgoing))
    groups = jnp.take(jnp.concatenate([group_of_patch, jnp.zeros((1,), jnp.int32)]), slot_row)
    focus_values = jnp.take(defocus, groups)
    scale = ctf_scale(focus_values, extent)
    spec_re, spec_im = make_spectra(take_idx, *pieces, scale, half_table, forward)
    return correlate_all(spec_re, spec_im, templ_re, templ_im, orientation, forward, inverse)


def solution(mesh):
    placed = (
        P(("blk", "patch"), None, None),
        P("blk"),
        P("blk"),
        P(),
        P("blk", None, None),
        P("blk", None, None),
        P(),
    )
    return jax.shard_map(
        body,
        mesh=mesh,
        in_specs=placed,
        out_specs=(
            P(("blk", "patch"), None, None),
            P(("blk", "patch"), None, None),
            P(("blk", "patch"), None, None),
            P(("blk", "patch"), None),
        ),
        check_vma=False,
    )
```

```python
import functools
import math

import jax
import ml_dtypes
import numpy as np
import jax.numpy as jnp
from jax import lax
from jax.experimental import pallas as pl
from jax.experimental.pallas import tpu as pltpu
from jax.sharding import PartitionSpec as P

SLOT = 2
CAP = 4
TILE_T = 4


AMPLITUDE = 0.07


def dft_tables(extent):
    indices = np.arange(extent, dtype=np.int64)
    turn_count = indices[:, None] * indices[None, :] % extent
    angles = turn_count.astype(np.float32) * np.float32(2.0 * math.pi / extent)
    cosine = np.cos(angles).astype(ml_dtypes.bfloat16)
    sine = np.sin(angles).astype(ml_dtypes.bfloat16)
    forward = np.concatenate(
        [np.concatenate([cosine, sine], axis=1), np.concatenate([-sine, cosine], axis=1)], axis=0
    )
    half_table = np.concatenate([cosine, -sine], axis=1)
    inverse = (half_table.astype(np.float32) / extent).astype(ml_dtypes.bfloat16)
    return forward, half_table, inverse


def ctf_filter(defocus_values, extent):
    indices = jnp.arange(extent, dtype=jnp.int32)
    signed = (
        jnp.where(indices < extent // 2, indices, indices - extent).astype(jnp.float32) / extent
    )
    radius = signed[:, None] * signed[:, None] + signed[None, :] * signed[None, :]
    phases = math.pi * defocus_values[:, None, None] * radius[None, :, :] - AMPLITUDE
    return -jnp.sin(phases)


def ctf_scale(defocus_values, extent):
    indices = jnp.arange(extent, dtype=jnp.int32)
    signed = (
        jnp.where(indices < extent // 2, indices, indices - extent).astype(jnp.float32) / extent
    )
    square = signed * signed
    turn = math.pi * defocus_values[:, None]
    row_phase = turn * square[None, :] - AMPLITUDE
    col_phase = turn * square[None, :]
    row_sin, row_cos = jnp.sin(row_phase), jnp.cos(row_phase)
    col_sin, col_cos = jnp.sin(col_phase), jnp.cos(col_phase)
    ctf = -(row_sin[:, :, None] * col_cos[:, None, :] + row_cos[:, :, None] * col_sin[:, None, :])
    return ctf / extent


def xor_pairs(count, shift):
    return [(d, d ^ shift) for d in range(count)]


def route_patches(patches, row_owner, my_index):
    sources, number = row_owner.shape
    extent = patches.shape[-1]
    chips = sources // 2
    devs = jnp.arange(sources, dtype=jnp.int32)
    chip_of = devs // 2
    owner_chip = row_owner // 2
    masks = [row_owner == (devs ^ 1)[:, None]]
    for m in range(1, chips):
        masks.append(owner_chip == (chip_of ^ m)[:, None])
    match = jnp.stack(masks, axis=1)
    first = jnp.where(match[..., 0], 0, jnp.where(match[..., 1], 1, number))
    second = jnp.where(match[..., 0] & match[..., 1], 1, number)
    send_sel = jnp.stack([first, second], axis=-1)
    send_pid = jnp.where(send_sel < number, devs[:, None, None] * number + send_sel, -1)
    padded = jnp.concatenate([patches, jnp.zeros((1, extent, extent), patches.dtype)], axis=0)
    my_sel = lax.dynamic_index_in_dim(send_sel, my_index, 0, keepdims=False)
    outgoing = jnp.take(padded, my_sel.reshape(-1), axis=0).reshape(chips, 2, extent, extent)
    partner = my_index ^ 1
    my_chip = my_index // 2
    direct = lax.ppermute(outgoing[0], "patch", xor_pairs(sources, 1))
    received = []
    for m in range(1, chips):
        received.append(lax.ppermute(outgoing[m], "patch", xor_pairs(sources, 2 * m)))
    received = jnp.concatenate(received, axis=0)
    forwarded = lax.ppermute(received, "patch", xor_pairs(sources, 1))
    cand_pid = [my_index * number + jnp.arange(number, dtype=jnp.int32)]
    cand_pid.append(lax.dynamic_index_in_dim(send_pid, partner, 0, keepdims=False)[0])
    for core in (my_index % 2, partner % 2):
        for m in range(1, chips):
            source = (my_chip ^ m) * 2 + core
            cand_pid.append(lax.dynamic_index_in_dim(send_pid, source, 0, keepdims=False)[m])
    cand_pid = jnp.concatenate(cand_pid)
    flat_owner = row_owner.reshape(-1)
    hits = (flat_owner == my_index).astype(jnp.int32)
    rank_in = jnp.cumsum(hits) - hits
    slot_ids = jnp.arange(CAP, dtype=jnp.int32)
    wanted = (hits[None, :] == 1) & (rank_in[None, :] == slot_ids[:, None])
    patch_ids = jnp.arange(sources * number, dtype=jnp.int32)
    slot_pid = jnp.sum(jnp.where(wanted, patch_ids[None, :], 0), axis=1)
    present = jnp.any(wanted, axis=1)
    cand_ids = jnp.arange(cand_pid.shape[0], dtype=jnp.int32)
    found = cand_pid[None, :] == slot_pid[:, None]
    take_idx = jnp.sum(jnp.where(found, cand_ids[None, :], 0), axis=1)
    take_idx = jnp.where(present, take_idx, cand_pid.shape[0])
    pieces = (patches, direct, received, forwarded)
    return take_idx, pieces, jnp.where(present, slot_pid, sources * number), outgoing


def spectra_kernel(rows, take_ref, own_ref, direct_ref, recv_ref, fwd_ref, scale_ref, half_ref,
                   full_ref, re_ref, im_ref):
    number = own_ref.shape[0]
    extent = own_ref.shape[-1]
    half_table = half_ref[...]
    full_table = full_ref[...]
    for s in range(re_ref.shape[0]):
        idx = take_ref[s]
        pick_own = own_ref[jnp.clip(idx, 0, number - 1)]
        pick_direct = direct_ref[jnp.clip(idx - number, 0, number - 1)]
        pick_recv = recv_ref[jnp.clip(idx - 2 * number, 0, rows - 1)]
        pick_fwd = fwd_ref[jnp.clip(idx - 2 * number - rows, 0, rows - 1)]
        zero = jnp.zeros_like(pick_own)
        image = jnp.where(
            idx < number, pick_own,
            jnp.where(idx < 2 * number, pick_direct,
                      jnp.where(idx < 2 * number + rows, pick_recv,
                                jnp.where(idx < 2 * number + 2 * rows, pick_fwd, zero))))
        half = jnp.dot(image, half_table, preferred_element_type=jnp.float32).astype(jnp.bfloat16)
        half_stack = jnp.concatenate([half[:, :extent], half[:, extent:]], axis=0)
        spec = jnp.dot(full_table, half_stack, preferred_element_type=jnp.float32)
        scale = scale_ref[s]
        re_ref[s] = (spec[:extent] * scale).astype(jnp.bfloat16)
        im_ref[s] = (spec[extent:] * scale).astype(jnp.bfloat16)


def make_spectra(take_idx, own, direct, received, forwarded, scale, half_table, full_table):
    count, extent = (scale.shape[0], scale.shape[-1])
    rows = received.shape[0]
    whole = pl.BlockSpec(memory_space=pltpu.VMEM)
    spec_shape = jax.ShapeDtypeStruct((count, extent, extent), jnp.bfloat16)
    return pl.pallas_call(
        functools.partial(spectra_kernel, rows),
        in_specs=[pl.BlockSpec(memory_space=pltpu.SMEM)] + [whole] * 7,
        out_specs=[whole, whole],
        out_shape=[spec_shape, spec_shape],
        cost_estimate=pl.CostEstimate(
            flops=3 * count * 6 * extent * extent * extent, transcendentals=0,
            bytes_accessed=count * 10 * extent * extent),
    )(take_idx, own, direct, received, forwarded, scale, half_table, full_table)


def corr_kernel(first, last, counts, orient_total, *refs):
    groups = len(counts)
    orient_ref, sr_ref, si_ref = refs[:3]
    templ_refs = refs[3:3 + groups]
    fw_ref, inv_ref = refs[3 + groups:5 + groups]
    rest = refs[5 + groups:]
    if first:
        top_ref, sum_ref, sq_ref, peak_ref = rest
    else:
        top_in, sum_in, sq_in, peak_in, top_ref, sum_ref, sq_ref, peak_ref = rest
    extent = sr_ref.shape[-1]
    sr = sr_ref[0].astype(jnp.float32)
    si = si_ref[0].astype(jnp.float32)
    forward = fw_ref[...]
    inverse = inv_ref[...]
    row_shape = (8, 128 * ((orient_total + 127) // 128))
    lanes = lax.broadcasted_iota(jnp.int32, row_shape, 1)
    peak_row = jnp.zeros(row_shape, jnp.float32) if first else peak_in[0]
    top = total = square = None
    prods = []
    for templ_ref, count in zip(templ_refs, counts):
        for t in range(count):
            tr = templ_ref[t].astype(jnp.float32)
            ti = templ_ref[count + t].astype(jnp.float32)
            pre = (sr * tr + si * ti).astype(jnp.bfloat16)
            pim = (si * tr - sr * ti).astype(jnp.bfloat16)
            prods.append(jnp.concatenate([pre, pim], axis=1))
    q_all = jnp.dot(jnp.concatenate(prods, axis=0), forward,
                    preferred_element_type=jnp.float32).astype(jnp.bfloat16)
    for position in range(len(prods)):
        q = q_all[position * extent:(position + 1) * extent]
        q_stack = jnp.concatenate([q[:, :extent], q[:, extent:]], axis=0)
        corr = jnp.dot(inverse, q_stack, preferred_element_type=jnp.float32)
        peak_row = jnp.where(lanes == orient_ref[position], jnp.max(corr), peak_row)
        if top is None:
            top, total, square = corr, corr, corr * corr
        else:
            top = jnp.maximum(top, corr)
            total = total + corr
            square = square + corr * corr
    if not first:
        top = jnp.maximum(top_in[0], top)
        total = sum_in[0] + total
        square = sq_in[0] + square
    top_ref[0] = top
    if last:
        s = pl.program_id(0)
        peak_ref[pl.ds(s, 1), :] = peak_row[0:1, :orient_total]
    else:
        peak_ref[0] = peak_row
    if last:
        mean = total / orient_total
        sum_ref[0] = mean
        sq_ref[0] = square / orient_total - mean * mean
    else:
        sum_ref[0] = total
        sq_ref[0] = square


def correlate_chunk(spec_re, spec_im, templ_groups, forward, inverse, orient_chunk,
                    orient_total, stats, last):
    count, extent = (spec_re.shape[0], spec_re.shape[-1])
    counts = tuple(group.shape[0] // 2 for group in templ_groups)
    tiles = sum(counts)
    first = stats is None
    lanes = 128 * ((orient_total + 127) // 128)
    plane = pl.BlockSpec((1, extent, extent), lambda s: (s, 0, 0))
    peak_spec = pl.BlockSpec((1, 8, lanes), lambda s: (s, 0, 0))
    templ_specs = [pl.BlockSpec(group.shape, lambda s: (0, 0, 0)) for group in templ_groups]
    fw_spec = pl.BlockSpec(forward.shape, lambda s: (0, 0))
    inv_spec = pl.BlockSpec(inverse.shape, lambda s: (0, 0))
    in_specs = [pl.BlockSpec(memory_space=pltpu.SMEM), plane, plane] + templ_specs + [
        fw_spec, inv_spec]
    operands = [orient_chunk, spec_re, spec_im] + list(templ_groups) + [forward, inverse]
    aliases = {}
    if not first:
        base = len(operands)
        in_specs += [plane, plane, plane, peak_spec]
        operands += list(stats)
        aliases = {base: 0, base + 1: 1, base + 2: 2}
        if not last:
            aliases[base + 3] = 3
    map_shape = jax.ShapeDtypeStruct((count, extent, extent), jnp.float32)
    flops = 3 * tiles * count * 12 * extent * extent * extent
    return pl.pallas_call(
        functools.partial(corr_kernel, first, last, counts, orient_total),
        grid=(count,),
        in_specs=in_specs,
        out_specs=[plane, plane, plane,
                   pl.BlockSpec((count, orient_total), lambda s: (0, 0)) if last else peak_spec],
        out_shape=[map_shape, map_shape, map_shape,
                   jax.ShapeDtypeStruct((count, orient_total) if last else (count, 8, lanes),
                                        jnp.float32)],
        input_output_aliases=aliases,
        compiler_params=pltpu.CompilerParams(dimension_semantics=("arbitrary",)),
        cost_estimate=pl.CostEstimate(
            flops=flops, transcendentals=0,
            bytes_accessed=tiles * 4 * extent * extent * 2 + count * 10 * extent * extent * 4),
    )(*operands)


def correlate_all(spec_re, spec_im, templ_re, templ_im, orientation, forward, inverse):
    blocks = lax.axis_size("blk")
    me = lax.axis_index("blk")
    sources = lax.axis_size("patch")
    core = lax.axis_index("patch") % 2
    tiles = templ_re.shape[0]
    half = tiles // 2
    orient_total = orientation.shape[0]
    local = jnp.concatenate([templ_re, templ_im], axis=0)
    mine = jnp.concatenate(
        [lax.dynamic_slice_in_dim(templ_re, core * half, half, 0),
         lax.dynamic_slice_in_dim(templ_im, core * half, half, 0)], axis=0)
    within = jnp.arange(half, dtype=jnp.int32)
    chunks = [([local], me * tiles + jnp.arange(tiles, dtype=jnp.int32))]
    for k in range(1, blocks):
        source = me ^ k
        got = lax.ppermute(mine, "blk", [(b, b ^ k) for b in range(blocks)])
        passed = lax.ppermute(got, "patch", xor_pairs(sources, 1))
        index = jnp.concatenate(
            [source * tiles + core * half + within, source * tiles + (1 - core) * half + within])
        chunks.append(([got, passed], index))
    stats = None
    for n, (groups, index) in enumerate(chunks):
        orient_chunk = jnp.take(orientation, index)
        stats = correlate_chunk(spec_re, spec_im, groups, forward, inverse, orient_chunk,
                                orient_total, stats, n == len(chunks) - 1)
    top_map, mean_map, var_map, peak = stats
    return (top_map, mean_map, var_map, peak)


def body(patches, owner_of_patch, group_of_patch, defocus, templ_re, templ_im, orientation):
    sources = lax.axis_size("patch")
    my_index = lax.axis_index("patch")
    number, extent = (patches.shape[0], patches.shape[1])
    forward, half_table, inverse = (jnp.asarray(table) for table in dft_tables(extent))
    row_owner = owner_of_patch.reshape(sources, number)
    take_idx, pieces, slot_row, outgoing = route_patches(patches, row_owner, my_index)
    templ_re, templ_im, unused = lax.optimization_barrier((templ_re, templ_im, outgoing))
    groups = jnp.take(jnp.concatenate([group_of_patch, jnp.zeros((1,), jnp.int32)]), slot_row)
    focus_values = jnp.take(defocus, groups)
    scale = ctf_scale(focus_values, extent)
    spec_re, spec_im = make_spectra(take_idx, *pieces, scale, half_table, forward)
    return correlate_all(spec_re, spec_im, templ_re, templ_im, orientation, forward, inverse)


def solution(mesh):
    placed = (
        P(("blk", "patch"), None, None),
        P("blk"),
        P("blk"),
        P(),
        P("blk", None, None),
        P("blk", None, None),
        P(),
    )
    return jax.shard_map(
        body,
        mesh=mesh,
        in_specs=placed,
        out_specs=(
            P(("blk", "patch"), None, None),
            P(("blk", "patch"), None, None),
            P(("blk", "patch"), None, None),
            P(("blk", "patch"), None),
        ),
        check_vma=False,
    )
```

```python
import functools
import math

import jax
import ml_dtypes
import numpy as np
import jax.numpy as jnp
from jax import lax
from jax.experimental import pallas as pl
from jax.experimental.pallas import tpu as pltpu
from jax.sharding import PartitionSpec as P

SLOT = 2
CAP = 4
TILE_T = 4


AMPLITUDE = 0.07


def dft_tables(extent):
    indices = np.arange(extent, dtype=np.int64)
    turn_count = indices[:, None] * indices[None, :] % extent
    angles = turn_count.astype(np.float32) * np.float32(2.0 * math.pi / extent)
    cosine = np.cos(angles).astype(ml_dtypes.bfloat16)
    sine = np.sin(angles).astype(ml_dtypes.bfloat16)
    forward = np.concatenate(
        [np.concatenate([cosine, sine], axis=1), np.concatenate([-sine, cosine], axis=1)], axis=0
    )
    half_table = np.concatenate([cosine, -sine], axis=1)
    inverse = (half_table.astype(np.float32) / extent).astype(ml_dtypes.bfloat16)
    return forward, half_table, inverse


def ctf_filter(defocus_values, extent):
    indices = jnp.arange(extent, dtype=jnp.int32)
    signed = (
        jnp.where(indices < extent // 2, indices, indices - extent).astype(jnp.float32) / extent
    )
    radius = signed[:, None] * signed[:, None] + signed[None, :] * signed[None, :]
    phases = math.pi * defocus_values[:, None, None] * radius[None, :, :] - AMPLITUDE
    return -jnp.sin(phases)


def ctf_scale(defocus_values, extent):
    indices = jnp.arange(extent, dtype=jnp.int32)
    signed = (
        jnp.where(indices < extent // 2, indices, indices - extent).astype(jnp.float32) / extent
    )
    square = signed * signed
    turn = math.pi * defocus_values[:, None]
    row_phase = turn * square[None, :] - AMPLITUDE
    col_phase = turn * square[None, :]
    row_sin, row_cos = jnp.sin(row_phase), jnp.cos(row_phase)
    col_sin, col_cos = jnp.sin(col_phase), jnp.cos(col_phase)
    ctf = -(row_sin[:, :, None] * col_cos[:, None, :] + row_cos[:, :, None] * col_sin[:, None, :])
    return ctf / extent


def xor_pairs(count, shift):
    return [(d, d ^ shift) for d in range(count)]


def two_matches(match, empty):
    first = jnp.where(match[..., 0], 0, jnp.where(match[..., 1], 1, empty))
    second = jnp.where(match[..., 0] & match[..., 1], 1, empty)
    return jnp.stack([first, second], axis=-1)


def route_relay(patches, row_owner, my_index):
    sources, number = row_owner.shape
    extent = patches.shape[-1]
    devs = jnp.arange(sources, dtype=jnp.int32)
    chip_of = devs // 2
    flat_owner = row_owner.reshape(-1)
    own_pid = devs[:, None] * number + jnp.arange(number, dtype=jnp.int32)[None, :]
    owner_chip = row_owner // 2
    sel_p = two_matches(row_owner == (devs ^ 1)[:, None], number)
    sel_n = two_matches(owner_chip == (chip_of ^ 1)[:, None], number)
    sel_f = two_matches((owner_chip ^ chip_of[:, None]) >= 2, number)

    def pids_of(sel, base):
        picked = jnp.take_along_axis(base, jnp.minimum(sel, number - 1), axis=1)
        return jnp.where(sel < number, picked, -1)

    pid_p = pids_of(sel_p, own_pid)
    pid_n = pids_of(sel_n, own_pid)
    pid_f = pids_of(sel_f, own_pid)
    far_got = jnp.take(pid_f, devs ^ 4, axis=0)
    far_chip = jnp.where(far_got >= 0, jnp.take(flat_owner, jnp.maximum(far_got, 0)) // 2, -1)
    sel_r = two_matches(far_chip == (chip_of ^ 1)[:, None], number)
    pid_r = pids_of(sel_r, far_got)
    padded = jnp.concatenate([patches, jnp.zeros((1, extent, extent), patches.dtype)], axis=0)
    my_sel = jnp.concatenate([lax.dynamic_index_in_dim(sel, my_index, 0, keepdims=False)
                              for sel in (sel_p, sel_n, sel_f)])
    outgoing = jnp.take(padded, my_sel, axis=0)
    direct = lax.ppermute(outgoing[0:2], "patch", xor_pairs(sources, 1))
    near_got = lax.ppermute(outgoing[2:4], "patch", xor_pairs(sources, 2))
    far_slots = lax.ppermute(outgoing[4:6], "patch", xor_pairs(sources, 4))
    far_padded = jnp.concatenate([far_slots, jnp.zeros((1, extent, extent), patches.dtype)], axis=0)
    my_relay = lax.dynamic_index_in_dim(sel_r, my_index, 0, keepdims=False)
    relay_got = lax.ppermute(jnp.take(far_padded, my_relay, axis=0), "patch",
                             xor_pairs(sources, 2))
    received = jnp.concatenate([near_got, far_slots, relay_got], axis=0)
    forwarded = lax.ppermute(received, "patch", xor_pairs(sources, 1))
    partner = my_index ^ 1

    def row(table, device):
        return lax.dynamic_index_in_dim(table, device, 0, keepdims=False)

    cand_pid = jnp.concatenate([
        row(own_pid, my_index), row(pid_p, partner),
        row(pid_n, my_index ^ 2), row(pid_f, my_index ^ 4), row(pid_r, my_index ^ 2),
        row(pid_n, partner ^ 2), row(pid_f, partner ^ 4), row(pid_r, partner ^ 2)])
    hits = (flat_owner == my_index).astype(jnp.int32)
    rank_in = jnp.cumsum(hits) - hits
    slot_ids = jnp.arange(CAP, dtype=jnp.int32)
    wanted = (hits[None, :] == 1) & (rank_in[None, :] == slot_ids[:, None])
    patch_ids = jnp.arange(sources * number, dtype=jnp.int32)
    slot_pid = jnp.sum(jnp.where(wanted, patch_ids[None, :], 0), axis=1)
    present = jnp.any(wanted, axis=1)
    cand_ids = jnp.arange(cand_pid.shape[0], dtype=jnp.int32)
    found = cand_pid[None, :] == slot_pid[:, None]
    take_idx = jnp.sum(jnp.where(found, cand_ids[None, :], 0), axis=1)
    take_idx = jnp.where(present, take_idx, cand_pid.shape[0])
    pieces = (patches, direct, received, forwarded)
    return take_idx, pieces, jnp.where(present, slot_pid, sources * number), outgoing


def route_patches(patches, row_owner, my_index):
    sources, number = row_owner.shape
    extent = patches.shape[-1]
    chips = sources // 2
    devs = jnp.arange(sources, dtype=jnp.int32)
    chip_of = devs // 2
    owner_chip = row_owner // 2
    masks = [row_owner == (devs ^ 1)[:, None]]
    for m in range(1, chips):
        masks.append(owner_chip == (chip_of ^ m)[:, None])
    match = jnp.stack(masks, axis=1)
    first = jnp.where(match[..., 0], 0, jnp.where(match[..., 1], 1, number))
    second = jnp.where(match[..., 0] & match[..., 1], 1, number)
    send_sel = jnp.stack([first, second], axis=-1)
    send_pid = jnp.where(send_sel < number, devs[:, None, None] * number + send_sel, -1)
    padded = jnp.concatenate([patches, jnp.zeros((1, extent, extent), patches.dtype)], axis=0)
    my_sel = lax.dynamic_index_in_dim(send_sel, my_index, 0, keepdims=False)
    outgoing = jnp.take(padded, my_sel.reshape(-1), axis=0).reshape(chips, 2, extent, extent)
    partner = my_index ^ 1
    my_chip = my_index // 2
    direct = lax.ppermute(outgoing[0], "patch", xor_pairs(sources, 1))
    received = []
    for m in range(1, chips):
        received.append(lax.ppermute(outgoing[m], "patch", xor_pairs(sources, 2 * m)))
    received = jnp.concatenate(received, axis=0)
    forwarded = lax.ppermute(received, "patch", xor_pairs(sources, 1))
    cand_pid = [my_index * number + jnp.arange(number, dtype=jnp.int32)]
    cand_pid.append(lax.dynamic_index_in_dim(send_pid, partner, 0, keepdims=False)[0])
    for core in (my_index % 2, partner % 2):
        for m in range(1, chips):
            source = (my_chip ^ m) * 2 + core
            cand_pid.append(lax.dynamic_index_in_dim(send_pid, source, 0, keepdims=False)[m])
    cand_pid = jnp.concatenate(cand_pid)
    flat_owner = row_owner.reshape(-1)
    hits = (flat_owner == my_index).astype(jnp.int32)
    rank_in = jnp.cumsum(hits) - hits
    slot_ids = jnp.arange(CAP, dtype=jnp.int32)
    wanted = (hits[None, :] == 1) & (rank_in[None, :] == slot_ids[:, None])
    patch_ids = jnp.arange(sources * number, dtype=jnp.int32)
    slot_pid = jnp.sum(jnp.where(wanted, patch_ids[None, :], 0), axis=1)
    present = jnp.any(wanted, axis=1)
    cand_ids = jnp.arange(cand_pid.shape[0], dtype=jnp.int32)
    found = cand_pid[None, :] == slot_pid[:, None]
    take_idx = jnp.sum(jnp.where(found, cand_ids[None, :], 0), axis=1)
    take_idx = jnp.where(present, take_idx, cand_pid.shape[0])
    pieces = (patches, direct, received, forwarded)
    return take_idx, pieces, jnp.where(present, slot_pid, sources * number), outgoing


def spectra_kernel(rows, take_ref, own_ref, direct_ref, recv_ref, fwd_ref, scale_ref, half_ref,
                   full_ref, re_ref, im_ref):
    number = own_ref.shape[0]
    extent = own_ref.shape[-1]
    half_table = half_ref[...]
    full_table = full_ref[...]
    for s in range(re_ref.shape[0]):
        idx = take_ref[s]
        pick_own = own_ref[jnp.clip(idx, 0, number - 1)]
        pick_direct = direct_ref[jnp.clip(idx - number, 0, number - 1)]
        pick_recv = recv_ref[jnp.clip(idx - 2 * number, 0, rows - 1)]
        pick_fwd = fwd_ref[jnp.clip(idx - 2 * number - rows, 0, rows - 1)]
        zero = jnp.zeros_like(pick_own)
        image = jnp.where(
            idx < number, pick_own,
            jnp.where(idx < 2 * number, pick_direct,
                      jnp.where(idx < 2 * number + rows, pick_recv,
                                jnp.where(idx < 2 * number + 2 * rows, pick_fwd, zero))))
        half = jnp.dot(image, half_table, preferred_element_type=jnp.float32).astype(jnp.bfloat16)
        half_stack = jnp.concatenate([half[:, :extent], half[:, extent:]], axis=0)
        spec = jnp.dot(full_table, half_stack, preferred_element_type=jnp.float32)
        scale = scale_ref[s]
        re_ref[s] = (spec[:extent] * scale).astype(jnp.bfloat16)
        im_ref[s] = (spec[extent:] * scale).astype(jnp.bfloat16)


def make_spectra(take_idx, own, direct, received, forwarded, scale, half_table, full_table):
    count, extent = (scale.shape[0], scale.shape[-1])
    rows = received.shape[0]
    whole = pl.BlockSpec(memory_space=pltpu.VMEM)
    spec_shape = jax.ShapeDtypeStruct((count, extent, extent), jnp.bfloat16)
    return pl.pallas_call(
        functools.partial(spectra_kernel, rows),
        in_specs=[pl.BlockSpec(memory_space=pltpu.SMEM)] + [whole] * 7,
        out_specs=[whole, whole],
        out_shape=[spec_shape, spec_shape],
        cost_estimate=pl.CostEstimate(
            flops=3 * count * 6 * extent * extent * extent, transcendentals=0,
            bytes_accessed=count * 10 * extent * extent),
    )(take_idx, own, direct, received, forwarded, scale, half_table, full_table)


def corr_kernel(first, last, counts, orient_total, *refs):
    groups = len(counts)
    orient_ref, sr_ref, si_ref = refs[:3]
    templ_refs = refs[3:3 + groups]
    fw_ref, inv_ref = refs[3 + groups:5 + groups]
    rest = refs[5 + groups:]
    if first:
        top_ref, sum_ref, sq_ref, peak_ref = rest
    else:
        top_in, sum_in, sq_in, peak_in, top_ref, sum_ref, sq_ref, peak_ref = rest
    extent = sr_ref.shape[-1]
    sr = sr_ref[0].astype(jnp.float32)
    si = si_ref[0].astype(jnp.float32)
    forward = fw_ref[...]
    inverse = inv_ref[...]
    row_shape = (8, 128 * ((orient_total + 127) // 128))
    lanes = lax.broadcasted_iota(jnp.int32, row_shape, 1)
    peak_row = jnp.zeros(row_shape, jnp.float32) if first else peak_in[0]
    top = total = square = None
    prods = []
    for templ_ref, count in zip(templ_refs, counts):
        for t in range(count):
            tr = templ_ref[t].astype(jnp.float32)
            ti = templ_ref[count + t].astype(jnp.float32)
            pre = (sr * tr + si * ti).astype(jnp.bfloat16)
            pim = (si * tr - sr * ti).astype(jnp.bfloat16)
            prods.append(jnp.concatenate([pre, pim], axis=1))
    q_all = jnp.dot(jnp.concatenate(prods, axis=0), forward,
                    preferred_element_type=jnp.float32).astype(jnp.bfloat16)
    for position in range(len(prods)):
        q = q_all[position * extent:(position + 1) * extent]
        q_stack = jnp.concatenate([q[:, :extent], q[:, extent:]], axis=0)
        corr = jnp.dot(inverse, q_stack, preferred_element_type=jnp.float32)
        peak_row = jnp.where(lanes == orient_ref[position], jnp.max(corr), peak_row)
        if top is None:
            top, total, square = corr, corr, corr * corr
        else:
            top = jnp.maximum(top, corr)
            total = total + corr
            square = square + corr * corr
    if not first:
        top = jnp.maximum(top_in[0], top)
        total = sum_in[0] + total
        square = sq_in[0] + square
    top_ref[0] = top
    if last:
        s = pl.program_id(0)
        peak_ref[pl.ds(s, 1), :] = peak_row[0:1, :orient_total]
    else:
        peak_ref[0] = peak_row
    if last:
        mean = total / orient_total
        sum_ref[0] = mean
        sq_ref[0] = square / orient_total - mean * mean
    else:
        sum_ref[0] = total
        sq_ref[0] = square


def correlate_chunk(spec_re, spec_im, templ_groups, forward, inverse, orient_chunk,
                    orient_total, stats, last):
    count, extent = (spec_re.shape[0], spec_re.shape[-1])
    counts = tuple(group.shape[0] // 2 for group in templ_groups)
    tiles = sum(counts)
    first = stats is None
    lanes = 128 * ((orient_total + 127) // 128)
    plane = pl.BlockSpec((1, extent, extent), lambda s: (s, 0, 0))
    peak_spec = pl.BlockSpec((1, 8, lanes), lambda s: (s, 0, 0))
    templ_specs = [pl.BlockSpec(group.shape, lambda s: (0, 0, 0)) for group in templ_groups]
    fw_spec = pl.BlockSpec(forward.shape, lambda s: (0, 0))
    inv_spec = pl.BlockSpec(inverse.shape, lambda s: (0, 0))
    in_specs = [pl.BlockSpec(memory_space=pltpu.SMEM), plane, plane] + templ_specs + [
        fw_spec, inv_spec]
    operands = [orient_chunk, spec_re, spec_im] + list(templ_groups) + [forward, inverse]
    aliases = {}
    if not first:
        base = len(operands)
        in_specs += [plane, plane, plane, peak_spec]
        operands += list(stats)
        aliases = {base: 0, base + 1: 1, base + 2: 2}
        if not last:
            aliases[base + 3] = 3
    map_shape = jax.ShapeDtypeStruct((count, extent, extent), jnp.float32)
    flops = 3 * tiles * count * 12 * extent * extent * extent
    return pl.pallas_call(
        functools.partial(corr_kernel, first, last, counts, orient_total),
        grid=(count,),
        in_specs=in_specs,
        out_specs=[plane, plane, plane,
                   pl.BlockSpec((count, orient_total), lambda s: (0, 0)) if last else peak_spec],
        out_shape=[map_shape, map_shape, map_shape,
                   jax.ShapeDtypeStruct((count, orient_total) if last else (count, 8, lanes),
                                        jnp.float32)],
        input_output_aliases=aliases,
        compiler_params=pltpu.CompilerParams(dimension_semantics=("arbitrary",)),
        cost_estimate=pl.CostEstimate(
            flops=flops, transcendentals=0,
            bytes_accessed=tiles * 4 * extent * extent * 2 + count * 10 * extent * extent * 4),
    )(*operands)


def correlate_all(spec_re, spec_im, templ_re, templ_im, orientation, forward, inverse):
    blocks = lax.axis_size("blk")
    me = lax.axis_index("blk")
    sources = lax.axis_size("patch")
    core = lax.axis_index("patch") % 2
    tiles = templ_re.shape[0]
    half = tiles // 2
    orient_total = orientation.shape[0]
    local = jnp.concatenate([templ_re, templ_im], axis=0)
    mine = jnp.concatenate(
        [lax.dynamic_slice_in_dim(templ_re, core * half, half, 0),
         lax.dynamic_slice_in_dim(templ_im, core * half, half, 0)], axis=0)
    within = jnp.arange(half, dtype=jnp.int32)
    chunks = [([local], me * tiles + jnp.arange(tiles, dtype=jnp.int32))]
    for k in range(1, blocks):
        source = me ^ k
        got = lax.ppermute(mine, "blk", [(b, b ^ k) for b in range(blocks)])
        passed = lax.ppermute(got, "patch", xor_pairs(sources, 1))
        index = jnp.concatenate(
            [source * tiles + core * half + within, source * tiles + (1 - core) * half + within])
        chunks.append(([got, passed], index))
    stats = None
    for n, (groups, index) in enumerate(chunks):
        orient_chunk = jnp.take(orientation, index)
        stats = correlate_chunk(spec_re, spec_im, groups, forward, inverse, orient_chunk,
                                orient_total, stats, n == len(chunks) - 1)
    top_map, mean_map, var_map, peak = stats
    return (top_map, mean_map, var_map, peak)


def body(patches, owner_of_patch, group_of_patch, defocus, templ_re, templ_im, orientation):
    sources = lax.axis_size("patch")
    my_index = lax.axis_index("patch")
    number, extent = (patches.shape[0], patches.shape[1])
    forward, half_table, inverse = (jnp.asarray(table) for table in dft_tables(extent))
    row_owner = owner_of_patch.reshape(sources, number)
    if sources == 8 and number == 2:
        take_idx, pieces, slot_row, outgoing = route_relay(patches, row_owner, my_index)
    else:
        take_idx, pieces, slot_row, outgoing = route_patches(patches, row_owner, my_index)
    templ_re, templ_im, unused = lax.optimization_barrier((templ_re, templ_im, outgoing))
    groups = jnp.take(jnp.concatenate([group_of_patch, jnp.zeros((1,), jnp.int32)]), slot_row)
    focus_values = jnp.take(defocus, groups)
    scale = ctf_scale(focus_values, extent)
    spec_re, spec_im = make_spectra(take_idx, *pieces, scale, half_table, forward)
    return correlate_all(spec_re, spec_im, templ_re, templ_im, orientation, forward, inverse)


def solution(mesh):
    placed = (
        P(("blk", "patch"), None, None),
        P("blk"),
        P("blk"),
        P(),
        P("blk", None, None),
        P("blk", None, None),
        P(),
    )
    return jax.shard_map(
        body,
        mesh=mesh,
        in_specs=placed,
        out_specs=(
            P(("blk", "patch"), None, None),
            P(("blk", "patch"), None, None),
            P(("blk", "patch"), None, None),
            P(("blk", "patch"), None),
        ),
        check_vma=False,
    )
```

```python
import functools
import math

import jax
import ml_dtypes
import numpy as np
import jax.numpy as jnp
from jax import lax
from jax.experimental import pallas as pl
from jax.experimental.pallas import tpu as pltpu
from jax.sharding import PartitionSpec as P

SLOT = 2
CAP = 4
TILE_T = 4
PER_STEP = 2


AMPLITUDE = 0.07


def dft_tables(extent):
    indices = np.arange(extent, dtype=np.int64)
    turn_count = indices[:, None] * indices[None, :] % extent
    angles = turn_count.astype(np.float32) * np.float32(2.0 * math.pi / extent)
    cosine = np.cos(angles).astype(ml_dtypes.bfloat16)
    sine = np.sin(angles).astype(ml_dtypes.bfloat16)
    forward = np.concatenate(
        [np.concatenate([cosine, sine], axis=1), np.concatenate([-sine, cosine], axis=1)], axis=0
    )
    half_table = np.concatenate([cosine, -sine], axis=1)
    inverse = (half_table.astype(np.float32) / extent).astype(ml_dtypes.bfloat16)
    return forward, half_table, inverse


def ctf_filter(defocus_values, extent):
    indices = jnp.arange(extent, dtype=jnp.int32)
    signed = (
        jnp.where(indices < extent // 2, indices, indices - extent).astype(jnp.float32) / extent
    )
    radius = signed[:, None] * signed[:, None] + signed[None, :] * signed[None, :]
    phases = math.pi * defocus_values[:, None, None] * radius[None, :, :] - AMPLITUDE
    return -jnp.sin(phases)


def ctf_scale(defocus_values, extent):
    indices = jnp.arange(extent, dtype=jnp.int32)
    signed = (
        jnp.where(indices < extent // 2, indices, indices - extent).astype(jnp.float32) / extent
    )
    square = signed * signed
    turn = math.pi * defocus_values[:, None]
    row_phase = turn * square[None, :] - AMPLITUDE
    col_phase = turn * square[None, :]
    row_sin, row_cos = jnp.sin(row_phase), jnp.cos(row_phase)
    col_sin, col_cos = jnp.sin(col_phase), jnp.cos(col_phase)
    ctf = -(row_sin[:, :, None] * col_cos[:, None, :] + row_cos[:, :, None] * col_sin[:, None, :])
    return ctf / extent


def xor_pairs(count, shift):
    return [(d, d ^ shift) for d in range(count)]


def route_patches(patches, row_owner, my_index):
    sources, number = row_owner.shape
    extent = patches.shape[-1]
    chips = sources // 2
    devs = jnp.arange(sources, dtype=jnp.int32)
    chip_of = devs // 2
    owner_chip = row_owner // 2
    masks = [row_owner == (devs ^ 1)[:, None]]
    for m in range(1, chips):
        masks.append(owner_chip == (chip_of ^ m)[:, None])
    match = jnp.stack(masks, axis=1)
    first = jnp.where(match[..., 0], 0, jnp.where(match[..., 1], 1, number))
    second = jnp.where(match[..., 0] & match[..., 1], 1, number)
    send_sel = jnp.stack([first, second], axis=-1)
    send_pid = jnp.where(send_sel < number, devs[:, None, None] * number + send_sel, -1)
    padded = jnp.concatenate([patches, jnp.zeros((1, extent, extent), patches.dtype)], axis=0)
    my_sel = lax.dynamic_index_in_dim(send_sel, my_index, 0, keepdims=False)
    outgoing = jnp.take(padded, my_sel.reshape(-1), axis=0).reshape(chips, 2, extent, extent)
    partner = my_index ^ 1
    my_chip = my_index // 2
    direct = lax.ppermute(outgoing[0], "patch", xor_pairs(sources, 1))
    received = []
    for m in range(1, chips):
        received.append(lax.ppermute(outgoing[m], "patch", xor_pairs(sources, 2 * m)))
    received = jnp.concatenate(received, axis=0)
    forwarded = lax.ppermute(received, "patch", xor_pairs(sources, 1))
    cand_pid = [my_index * number + jnp.arange(number, dtype=jnp.int32)]
    cand_pid.append(lax.dynamic_index_in_dim(send_pid, partner, 0, keepdims=False)[0])
    for core in (my_index % 2, partner % 2):
        for m in range(1, chips):
            source = (my_chip ^ m) * 2 + core
            cand_pid.append(lax.dynamic_index_in_dim(send_pid, source, 0, keepdims=False)[m])
    cand_pid = jnp.concatenate(cand_pid)
    flat_owner = row_owner.reshape(-1)
    hits = (flat_owner == my_index).astype(jnp.int32)
    rank_in = jnp.cumsum(hits) - hits
    slot_ids = jnp.arange(CAP, dtype=jnp.int32)
    wanted = (hits[None, :] == 1) & (rank_in[None, :] == slot_ids[:, None])
    patch_ids = jnp.arange(sources * number, dtype=jnp.int32)
    slot_pid = jnp.sum(jnp.where(wanted, patch_ids[None, :], 0), axis=1)
    present = jnp.any(wanted, axis=1)
    cand_ids = jnp.arange(cand_pid.shape[0], dtype=jnp.int32)
    found = cand_pid[None, :] == slot_pid[:, None]
    take_idx = jnp.sum(jnp.where(found, cand_ids[None, :], 0), axis=1)
    take_idx = jnp.where(present, take_idx, cand_pid.shape[0])
    pieces = (patches, direct, received, forwarded)
    return take_idx, pieces, jnp.where(present, slot_pid, sources * number), outgoing


def spectra_kernel(rows, take_ref, own_ref, direct_ref, recv_ref, fwd_ref, scale_ref, half_ref,
                   full_ref, re_ref, im_ref):
    number = own_ref.shape[0]
    extent = own_ref.shape[-1]
    half_table = half_ref[...]
    full_table = full_ref[...]
    for s in range(re_ref.shape[0]):
        idx = take_ref[s]
        pick_own = own_ref[jnp.clip(idx, 0, number - 1)]
        pick_direct = direct_ref[jnp.clip(idx - number, 0, number - 1)]
        pick_recv = recv_ref[jnp.clip(idx - 2 * number, 0, rows - 1)]
        pick_fwd = fwd_ref[jnp.clip(idx - 2 * number - rows, 0, rows - 1)]
        zero = jnp.zeros_like(pick_own)
        image = jnp.where(
            idx < number, pick_own,
            jnp.where(idx < 2 * number, pick_direct,
                      jnp.where(idx < 2 * number + rows, pick_recv,
                                jnp.where(idx < 2 * number + 2 * rows, pick_fwd, zero))))
        half = jnp.dot(image, half_table, preferred_element_type=jnp.float32).astype(jnp.bfloat16)
        half_stack = jnp.concatenate([half[:, :extent], half[:, extent:]], axis=0)
        spec = jnp.dot(full_table, half_stack, preferred_element_type=jnp.float32)
        scale = scale_ref[s]
        re_ref[s] = (spec[:extent] * scale).astype(jnp.bfloat16)
        im_ref[s] = (spec[extent:] * scale).astype(jnp.bfloat16)


def make_spectra(take_idx, own, direct, received, forwarded, scale, half_table, full_table):
    count, extent = (scale.shape[0], scale.shape[-1])
    rows = received.shape[0]
    whole = pl.BlockSpec(memory_space=pltpu.VMEM)
    spec_shape = jax.ShapeDtypeStruct((count, extent, extent), jnp.bfloat16)
    return pl.pallas_call(
        functools.partial(spectra_kernel, rows),
        in_specs=[pl.BlockSpec(memory_space=pltpu.SMEM)] + [whole] * 7,
        out_specs=[whole, whole],
        out_shape=[spec_shape, spec_shape],
        cost_estimate=pl.CostEstimate(
            flops=3 * count * 6 * extent * extent * extent, transcendentals=0,
            bytes_accessed=count * 10 * extent * extent),
    )(take_idx, own, direct, received, forwarded, scale, half_table, full_table)


def corr_kernel(first, last, counts, orient_total, *refs):
    groups = len(counts)
    orient_ref, sr_ref, si_ref = refs[:3]
    templ_refs = refs[3:3 + groups]
    fw_ref, inv_ref = refs[3 + groups:5 + groups]
    rest = refs[5 + groups:]
    if first:
        top_ref, sum_ref, sq_ref, peak_ref = rest
    else:
        top_in, sum_in, sq_in, peak_in, top_ref, sum_ref, sq_ref, peak_ref = rest
    extent = sr_ref.shape[-1]
    per_step = sr_ref.shape[0]
    forward = fw_ref[...]
    inverse = inv_ref[...]
    row_shape = (8, 128 * ((orient_total + 127) // 128))
    lanes = lax.broadcasted_iota(jnp.int32, row_shape, 1)
    templs = []
    for templ_ref, count in zip(templ_refs, counts):
        for t in range(count):
            templs.append((templ_ref[t].astype(jnp.float32), templ_ref[count + t].astype(jnp.float32)))
    prods = []
    for j in range(per_step):
        sr = sr_ref[j].astype(jnp.float32)
        si = si_ref[j].astype(jnp.float32)
        for tr, ti in templs:
            pre = (sr * tr + si * ti).astype(jnp.bfloat16)
            pim = (si * tr - sr * ti).astype(jnp.bfloat16)
            prods.append(jnp.concatenate([pre, pim], axis=1))
    q_all = jnp.dot(jnp.concatenate(prods, axis=0), forward,
                    preferred_element_type=jnp.float32).astype(jnp.bfloat16)
    tiles = len(templs)
    for j in range(per_step):
        peak_row = jnp.zeros(row_shape, jnp.float32) if first else peak_in[j]
        top = total = square = None
        for position in range(tiles):
            row = (j * tiles + position) * extent
            q = q_all[row:row + extent]
            q_stack = jnp.concatenate([q[:, :extent], q[:, extent:]], axis=0)
            corr = jnp.dot(inverse, q_stack, preferred_element_type=jnp.float32)
            peak_row = jnp.where(lanes == orient_ref[position], jnp.max(corr), peak_row)
            if top is None:
                top, total, square = corr, corr, corr * corr
            else:
                top = jnp.maximum(top, corr)
                total = total + corr
                square = square + corr * corr
        if not first:
            top = jnp.maximum(top_in[j], top)
            total = sum_in[j] + total
            square = sq_in[j] + square
        top_ref[j] = top
        if last:
            s = pl.program_id(0) * per_step + j
            peak_ref[pl.ds(s, 1), :] = peak_row[0:1, :orient_total]
        else:
            peak_ref[j] = peak_row
        if last:
            mean = total / orient_total
            sum_ref[j] = mean
            sq_ref[j] = square / orient_total - mean * mean
        else:
            sum_ref[j] = total
            sq_ref[j] = square


def correlate_chunk(spec_re, spec_im, templ_groups, forward, inverse, orient_chunk,
                    orient_total, stats, last):
    count, extent = (spec_re.shape[0], spec_re.shape[-1])
    counts = tuple(group.shape[0] // 2 for group in templ_groups)
    tiles = sum(counts)
    first = stats is None
    lanes = 128 * ((orient_total + 127) // 128)
    per_step = PER_STEP if count % PER_STEP == 0 else 1
    plane = pl.BlockSpec((per_step, extent, extent), lambda s: (s, 0, 0))
    peak_spec = pl.BlockSpec((per_step, 8, lanes), lambda s: (s, 0, 0))
    templ_specs = [pl.BlockSpec(group.shape, lambda s: (0, 0, 0)) for group in templ_groups]
    fw_spec = pl.BlockSpec(forward.shape, lambda s: (0, 0))
    inv_spec = pl.BlockSpec(inverse.shape, lambda s: (0, 0))
    in_specs = [pl.BlockSpec(memory_space=pltpu.SMEM), plane, plane] + templ_specs + [
        fw_spec, inv_spec]
    operands = [orient_chunk, spec_re, spec_im] + list(templ_groups) + [forward, inverse]
    aliases = {}
    if not first:
        base = len(operands)
        in_specs += [plane, plane, plane, peak_spec]
        operands += list(stats)
        aliases = {base: 0, base + 1: 1, base + 2: 2}
        if not last:
            aliases[base + 3] = 3
    map_shape = jax.ShapeDtypeStruct((count, extent, extent), jnp.float32)
    flops = 3 * tiles * count * 12 * extent * extent * extent
    return pl.pallas_call(
        functools.partial(corr_kernel, first, last, counts, orient_total),
        grid=(count // per_step,),
        in_specs=in_specs,
        out_specs=[plane, plane, plane,
                   pl.BlockSpec((count, orient_total), lambda s: (0, 0)) if last else peak_spec],
        out_shape=[map_shape, map_shape, map_shape,
                   jax.ShapeDtypeStruct((count, orient_total) if last else (count, 8, lanes),
                                        jnp.float32)],
        input_output_aliases=aliases,
        compiler_params=pltpu.CompilerParams(dimension_semantics=("arbitrary",)),
        cost_estimate=pl.CostEstimate(
            flops=flops, transcendentals=0,
            bytes_accessed=tiles * 4 * extent * extent * 2 + count * 10 * extent * extent * 4),
    )(*operands)


def correlate_all(spec_re, spec_im, templ_re, templ_im, orientation, forward, inverse):
    blocks = lax.axis_size("blk")
    me = lax.axis_index("blk")
    sources = lax.axis_size("patch")
    core = lax.axis_index("patch") % 2
    tiles = templ_re.shape[0]
    half = tiles // 2
    orient_total = orientation.shape[0]
    local = jnp.concatenate([templ_re, templ_im], axis=0)
    mine = jnp.concatenate(
        [lax.dynamic_slice_in_dim(templ_re, core * half, half, 0),
         lax.dynamic_slice_in_dim(templ_im, core * half, half, 0)], axis=0)
    within = jnp.arange(half, dtype=jnp.int32)
    chunks = [([local], me * tiles + jnp.arange(tiles, dtype=jnp.int32))]
    for k in range(1, blocks):
        source = me ^ k
        got = lax.ppermute(mine, "blk", [(b, b ^ k) for b in range(blocks)])
        passed = lax.ppermute(got, "patch", xor_pairs(sources, 1))
        index = jnp.concatenate(
            [source * tiles + core * half + within, source * tiles + (1 - core) * half + within])
        chunks.append(([got, passed], index))
    stats = None
    for n, (groups, index) in enumerate(chunks):
        orient_chunk = jnp.take(orientation, index)
        stats = correlate_chunk(spec_re, spec_im, groups, forward, inverse, orient_chunk,
                                orient_total, stats, n == len(chunks) - 1)
    top_map, mean_map, var_map, peak = stats
    return (top_map, mean_map, var_map, peak)


def body(patches, owner_of_patch, group_of_patch, defocus, templ_re, templ_im, orientation):
    sources = lax.axis_size("patch")
    my_index = lax.axis_index("patch")
    number, extent = (patches.shape[0], patches.shape[1])
    forward, half_table, inverse = (jnp.asarray(table) for table in dft_tables(extent))
    row_owner = owner_of_patch.reshape(sources, number)
    take_idx, pieces, slot_row, outgoing = route_patches(patches, row_owner, my_index)
    templ_re, templ_im, unused = lax.optimization_barrier((templ_re, templ_im, outgoing))
    groups = jnp.take(jnp.concatenate([group_of_patch, jnp.zeros((1,), jnp.int32)]), slot_row)
    focus_values = jnp.take(defocus, groups)
    scale = ctf_scale(focus_values, extent)
    spec_re, spec_im = make_spectra(take_idx, *pieces, scale, half_table, forward)
    return correlate_all(spec_re, spec_im, templ_re, templ_im, orientation, forward, inverse)


def solution(mesh):
    placed = (
        P(("blk", "patch"), None, None),
        P("blk"),
        P("blk"),
        P(),
        P("blk", None, None),
        P("blk", None, None),
        P(),
    )
    return jax.shard_map(
        body,
        mesh=mesh,
        in_specs=placed,
        out_specs=(
            P(("blk", "patch"), None, None),
            P(("blk", "patch"), None, None),
            P(("blk", "patch"), None, None),
            P(("blk", "patch"), None),
        ),
        check_vma=False,
    )
```

```python
import functools
import math

import jax
import ml_dtypes
import numpy as np
import jax.numpy as jnp
from jax import lax
from jax.experimental import pallas as pl
from jax.experimental.pallas import tpu as pltpu
from jax.sharding import PartitionSpec as P

SLOT = 2
CAP = 4
TILE_T = 4


AMPLITUDE = 0.07


def dft_tables(extent):
    indices = np.arange(extent, dtype=np.int64)
    turn_count = indices[:, None] * indices[None, :] % extent
    angles = turn_count.astype(np.float32) * np.float32(2.0 * math.pi / extent)
    cosine = np.cos(angles).astype(ml_dtypes.bfloat16)
    sine = np.sin(angles).astype(ml_dtypes.bfloat16)
    forward = np.concatenate(
        [np.concatenate([cosine, sine], axis=1), np.concatenate([-sine, cosine], axis=1)], axis=0
    )
    half_table = np.concatenate([cosine, -sine], axis=1)
    inverse = (half_table.astype(np.float32) / extent).astype(ml_dtypes.bfloat16)
    return forward, half_table, inverse


def ctf_filter(defocus_values, extent):
    indices = jnp.arange(extent, dtype=jnp.int32)
    signed = (
        jnp.where(indices < extent // 2, indices, indices - extent).astype(jnp.float32) / extent
    )
    radius = signed[:, None] * signed[:, None] + signed[None, :] * signed[None, :]
    phases = math.pi * defocus_values[:, None, None] * radius[None, :, :] - AMPLITUDE
    return -jnp.sin(phases)


def ctf_scale(defocus_values, extent):
    indices = jnp.arange(extent, dtype=jnp.int32)
    signed = (
        jnp.where(indices < extent // 2, indices, indices - extent).astype(jnp.float32) / extent
    )
    square = signed * signed
    turn = math.pi * defocus_values[:, None]
    row_phase = turn * square[None, :] - AMPLITUDE
    col_phase = turn * square[None, :]
    row_sin, row_cos = jnp.sin(row_phase), jnp.cos(row_phase)
    col_sin, col_cos = jnp.sin(col_phase), jnp.cos(col_phase)
    ctf = -(row_sin[:, :, None] * col_cos[:, None, :] + row_cos[:, :, None] * col_sin[:, None, :])
    return ctf / extent


def xor_pairs(count, shift):
    return [(d, d ^ shift) for d in range(count)]


def route_patches(patches, row_owner, my_index):
    sources, number = row_owner.shape
    extent = patches.shape[-1]
    chips = sources // 2
    devs = jnp.arange(sources, dtype=jnp.int32)
    chip_of = devs // 2
    owner_chip = row_owner // 2
    masks = [row_owner == (devs ^ 1)[:, None]]
    for m in range(1, chips):
        masks.append(owner_chip == (chip_of ^ m)[:, None])
    match = jnp.stack(masks, axis=1)
    first = jnp.where(match[..., 0], 0, jnp.where(match[..., 1], 1, number))
    second = jnp.where(match[..., 0] & match[..., 1], 1, number)
    send_sel = jnp.stack([first, second], axis=-1)
    send_pid = jnp.where(send_sel < number, devs[:, None, None] * number + send_sel, -1)
    padded = jnp.concatenate([patches, jnp.zeros((1, extent, extent), patches.dtype)], axis=0)
    my_sel = lax.dynamic_index_in_dim(send_sel, my_index, 0, keepdims=False)
    outgoing = jnp.take(padded, my_sel.reshape(-1), axis=0).reshape(chips, 2, extent, extent)
    partner = my_index ^ 1
    my_chip = my_index // 2
    direct = lax.ppermute(outgoing[0], "patch", xor_pairs(sources, 1))
    received = []
    for m in range(1, chips):
        received.append(lax.ppermute(outgoing[m], "patch", xor_pairs(sources, 2 * m)))
    received = jnp.concatenate(received, axis=0)
    forwarded = lax.ppermute(received, "patch", xor_pairs(sources, 1))
    cand_pid = [my_index * number + jnp.arange(number, dtype=jnp.int32)]
    cand_pid.append(lax.dynamic_index_in_dim(send_pid, partner, 0, keepdims=False)[0])
    for core in (my_index % 2, partner % 2):
        for m in range(1, chips):
            source = (my_chip ^ m) * 2 + core
            cand_pid.append(lax.dynamic_index_in_dim(send_pid, source, 0, keepdims=False)[m])
    cand_pid = jnp.concatenate(cand_pid)
    flat_owner = row_owner.reshape(-1)
    hits = (flat_owner == my_index).astype(jnp.int32)
    rank_in = jnp.cumsum(hits) - hits
    slot_ids = jnp.arange(CAP, dtype=jnp.int32)
    wanted = (hits[None, :] == 1) & (rank_in[None, :] == slot_ids[:, None])
    patch_ids = jnp.arange(sources * number, dtype=jnp.int32)
    slot_pid = jnp.sum(jnp.where(wanted, patch_ids[None, :], 0), axis=1)
    present = jnp.any(wanted, axis=1)
    cand_ids = jnp.arange(cand_pid.shape[0], dtype=jnp.int32)
    found = cand_pid[None, :] == slot_pid[:, None]
    take_idx = jnp.sum(jnp.where(found, cand_ids[None, :], 0), axis=1)
    take_idx = jnp.where(present, take_idx, cand_pid.shape[0])
    pieces = (patches, direct, received, forwarded)
    return take_idx, pieces, jnp.where(present, slot_pid, sources * number), outgoing


def spectra_kernel(rows, take_ref, own_ref, direct_ref, recv_ref, fwd_ref, scale_ref, half_ref,
                   full_ref, re_ref, im_ref):
    number = own_ref.shape[0]
    extent = own_ref.shape[-1]
    half_table = half_ref[...]
    full_table = full_ref[...]
    for s in range(re_ref.shape[0]):
        idx = take_ref[s]
        pick_own = own_ref[jnp.clip(idx, 0, number - 1)]
        pick_direct = direct_ref[jnp.clip(idx - number, 0, number - 1)]
        pick_recv = recv_ref[jnp.clip(idx - 2 * number, 0, rows - 1)]
        pick_fwd = fwd_ref[jnp.clip(idx - 2 * number - rows, 0, rows - 1)]
        zero = jnp.zeros_like(pick_own)
        image = jnp.where(
            idx < number, pick_own,
            jnp.where(idx < 2 * number, pick_direct,
                      jnp.where(idx < 2 * number + rows, pick_recv,
                                jnp.where(idx < 2 * number + 2 * rows, pick_fwd, zero))))
        half = jnp.dot(image, half_table, preferred_element_type=jnp.float32).astype(jnp.bfloat16)
        half_stack = jnp.concatenate([half[:, :extent], half[:, extent:]], axis=0)
        spec = jnp.dot(full_table, half_stack, preferred_element_type=jnp.float32)
        scale = scale_ref[s]
        re_ref[s] = (spec[:extent] * scale).astype(jnp.bfloat16)
        im_ref[s] = (spec[extent:] * scale).astype(jnp.bfloat16)


def make_spectra(take_idx, own, direct, received, forwarded, scale, half_table, full_table):
    count, extent = (scale.shape[0], scale.shape[-1])
    rows = received.shape[0]
    whole = pl.BlockSpec(memory_space=pltpu.VMEM)
    spec_shape = jax.ShapeDtypeStruct((count, extent, extent), jnp.bfloat16)
    return pl.pallas_call(
        functools.partial(spectra_kernel, rows),
        in_specs=[pl.BlockSpec(memory_space=pltpu.SMEM)] + [whole] * 7,
        out_specs=[whole, whole],
        out_shape=[spec_shape, spec_shape],
        cost_estimate=pl.CostEstimate(
            flops=3 * count * 6 * extent * extent * extent, transcendentals=0,
            bytes_accessed=count * 10 * extent * extent),
    )(take_idx, own, direct, received, forwarded, scale, half_table, full_table)


def corr_kernel(first, last, counts, orient_total, *refs):
    groups = len(counts)
    orient_ref, sr_ref, si_ref = refs[:3]
    templ_refs = refs[3:3 + groups]
    fw_ref, inv_ref = refs[3 + groups:5 + groups]
    rest = refs[5 + groups:]
    if first:
        top_ref, sum_ref, sq_ref, peak_ref = rest
    else:
        top_in, sum_in, sq_in, peak_in, top_ref, sum_ref, sq_ref, peak_ref = rest
    extent = sr_ref.shape[-1]
    sr = sr_ref[0].astype(jnp.float32)
    si = si_ref[0].astype(jnp.float32)
    forward = fw_ref[...]
    inverse = inv_ref[...]
    row_shape = (8, 128 * ((orient_total + 127) // 128))
    lanes = lax.broadcasted_iota(jnp.int32, row_shape, 1)
    peak_row = jnp.zeros(row_shape, jnp.float32) if first else peak_in[0]
    top = total = square = None
    prods = []
    for templ_ref, count in zip(templ_refs, counts):
        for t in range(count):
            tr = templ_ref[t].astype(jnp.float32)
            ti = templ_ref[count + t].astype(jnp.float32)
            pre = (sr * tr + si * ti).astype(jnp.bfloat16)
            pim = (si * tr - sr * ti).astype(jnp.bfloat16)
            prods.append(jnp.concatenate([pre, pim], axis=1))
    q_all = jnp.dot(jnp.concatenate(prods, axis=0), forward,
                    preferred_element_type=jnp.float32).astype(jnp.bfloat16)
    for position in range(len(prods)):
        q = q_all[position * extent:(position + 1) * extent]
        q_stack = jnp.concatenate([q[:, :extent], q[:, extent:]], axis=0)
        corr = jnp.dot(inverse, q_stack, preferred_element_type=jnp.float32)
        peak_row = jnp.where(lanes == orient_ref[position], jnp.max(corr), peak_row)
        if top is None:
            top, total, square = corr, corr, corr * corr
        else:
            top = jnp.maximum(top, corr)
            total = total + corr
            square = square + corr * corr
    if not first:
        top = jnp.maximum(top_in[0], top)
        total = sum_in[0] + total
        square = sq_in[0] + square
    top_ref[0] = top
    if last:
        s = pl.program_id(0)
        peak_ref[pl.ds(s, 1), :] = peak_row[0:1, :orient_total]
    else:
        peak_ref[0] = peak_row
    if last:
        mean = total / orient_total
        sum_ref[0] = mean
        sq_ref[0] = square / orient_total - mean * mean
    else:
        sum_ref[0] = total
        sq_ref[0] = square


def correlate_chunk(spec_re, spec_im, templ_groups, forward, inverse, orient_chunk,
                    orient_total, stats, last):
    count, extent = (spec_re.shape[0], spec_re.shape[-1])
    counts = tuple(group.shape[0] // 2 for group in templ_groups)
    tiles = sum(counts)
    first = stats is None
    lanes = 128 * ((orient_total + 127) // 128)
    plane = pl.BlockSpec((1, extent, extent), lambda s: (s, 0, 0))
    peak_spec = pl.BlockSpec((1, 8, lanes), lambda s: (s, 0, 0))
    templ_specs = [pl.BlockSpec(group.shape, lambda s: (0, 0, 0)) for group in templ_groups]
    fw_spec = pl.BlockSpec(forward.shape, lambda s: (0, 0))
    inv_spec = pl.BlockSpec(inverse.shape, lambda s: (0, 0))
    in_specs = [pl.BlockSpec(memory_space=pltpu.SMEM), plane, plane] + templ_specs + [
        fw_spec, inv_spec]
    operands = [orient_chunk, spec_re, spec_im] + list(templ_groups) + [forward, inverse]
    aliases = {}
    if not first:
        base = len(operands)
        in_specs += [plane, plane, plane, peak_spec]
        operands += list(stats)
        aliases = {base: 0, base + 1: 1, base + 2: 2}
        if not last:
            aliases[base + 3] = 3
    map_shape = jax.ShapeDtypeStruct((count, extent, extent), jnp.float32)
    flops = 3 * tiles * count * 12 * extent * extent * extent
    return pl.pallas_call(
        functools.partial(corr_kernel, first, last, counts, orient_total),
        grid=(count,),
        in_specs=in_specs,
        out_specs=[plane, plane, plane,
                   pl.BlockSpec((count, orient_total), lambda s: (0, 0)) if last else peak_spec],
        out_shape=[map_shape, map_shape, map_shape,
                   jax.ShapeDtypeStruct((count, orient_total) if last else (count, 8, lanes),
                                        jnp.float32)],
        input_output_aliases=aliases,
        compiler_params=pltpu.CompilerParams(dimension_semantics=("arbitrary",)),
        cost_estimate=pl.CostEstimate(
            flops=flops, transcendentals=0,
            bytes_accessed=tiles * 4 * extent * extent * 2 + count * 10 * extent * extent * 4),
    )(*operands)


def correlate_all(spec_re, spec_im, templ_re, templ_im, orientation, forward, inverse):
    blocks = lax.axis_size("blk")
    me = lax.axis_index("blk")
    sources = lax.axis_size("patch")
    core = lax.axis_index("patch") % 2
    tiles = templ_re.shape[0]
    half = tiles // 2
    orient_total = orientation.shape[0]
    local = jnp.concatenate([templ_re, templ_im], axis=0)
    mine = jnp.concatenate(
        [lax.dynamic_slice_in_dim(templ_re, core * half, half, 0),
         lax.dynamic_slice_in_dim(templ_im, core * half, half, 0)], axis=0)
    within = jnp.arange(half, dtype=jnp.int32)
    chunks = [([local], me * tiles + jnp.arange(tiles, dtype=jnp.int32))]
    for k in range(1, blocks):
        source = me ^ k
        got = lax.ppermute(mine, "blk", [(b, b ^ k) for b in range(blocks)])
        passed = lax.ppermute(got, "patch", xor_pairs(sources, 1))
        index = jnp.concatenate(
            [source * tiles + core * half + within, source * tiles + (1 - core) * half + within])
        chunks.append(([got, passed], index))
    if len(chunks) > 2:
        merged = (chunks[0][0] + chunks[1][0], jnp.concatenate([chunks[0][1], chunks[1][1]]))
        chunks = [merged] + chunks[2:]
    stats = None
    for n, (groups, index) in enumerate(chunks):
        orient_chunk = jnp.take(orientation, index)
        stats = correlate_chunk(spec_re, spec_im, groups, forward, inverse, orient_chunk,
                                orient_total, stats, n == len(chunks) - 1)
    top_map, mean_map, var_map, peak = stats
    return (top_map, mean_map, var_map, peak)


def body(patches, owner_of_patch, group_of_patch, defocus, templ_re, templ_im, orientation):
    sources = lax.axis_size("patch")
    my_index = lax.axis_index("patch")
    number, extent = (patches.shape[0], patches.shape[1])
    forward, half_table, inverse = (jnp.asarray(table) for table in dft_tables(extent))
    row_owner = owner_of_patch.reshape(sources, number)
    take_idx, pieces, slot_row, outgoing = route_patches(patches, row_owner, my_index)
    templ_re, templ_im, unused = lax.optimization_barrier((templ_re, templ_im, outgoing))
    groups = jnp.take(jnp.concatenate([group_of_patch, jnp.zeros((1,), jnp.int32)]), slot_row)
    focus_values = jnp.take(defocus, groups)
    scale = ctf_scale(focus_values, extent)
    spec_re, spec_im = make_spectra(take_idx, *pieces, scale, half_table, forward)
    return correlate_all(spec_re, spec_im, templ_re, templ_im, orientation, forward, inverse)


def solution(mesh):
    placed = (
        P(("blk", "patch"), None, None),
        P("blk"),
        P("blk"),
        P(),
        P("blk", None, None),
        P("blk", None, None),
        P(),
    )
    return jax.shard_map(
        body,
        mesh=mesh,
        in_specs=placed,
        out_specs=(
            P(("blk", "patch"), None, None),
            P(("blk", "patch"), None, None),
            P(("blk", "patch"), None, None),
            P(("blk", "patch"), None),
        ),
        check_vma=False,
    )
```

```python
import functools
import math

import jax
import ml_dtypes
import numpy as np
import jax.numpy as jnp
from jax import lax
from jax.experimental import pallas as pl
from jax.experimental.pallas import tpu as pltpu
from jax.sharding import PartitionSpec as P

SLOT = 2
CAP = 4
TILE_T = 4


AMPLITUDE = 0.07


def dft_tables(extent):
    indices = np.arange(extent, dtype=np.int64)
    turn_count = indices[:, None] * indices[None, :] % extent
    angles = turn_count.astype(np.float32) * np.float32(2.0 * math.pi / extent)
    cosine = np.cos(angles).astype(ml_dtypes.bfloat16)
    sine = np.sin(angles).astype(ml_dtypes.bfloat16)
    forward = np.concatenate(
        [np.concatenate([cosine, sine], axis=1), np.concatenate([-sine, cosine], axis=1)], axis=0
    )
    half_table = np.concatenate([cosine, -sine], axis=1)
    inverse = (half_table.astype(np.float32) / extent).astype(ml_dtypes.bfloat16)
    return forward, half_table, inverse


def ctf_filter(defocus_values, extent):
    indices = jnp.arange(extent, dtype=jnp.int32)
    signed = (
        jnp.where(indices < extent // 2, indices, indices - extent).astype(jnp.float32) / extent
    )
    radius = signed[:, None] * signed[:, None] + signed[None, :] * signed[None, :]
    phases = math.pi * defocus_values[:, None, None] * radius[None, :, :] - AMPLITUDE
    return -jnp.sin(phases)


def ctf_scale(defocus_values, extent):
    indices = jnp.arange(extent, dtype=jnp.int32)
    signed = (
        jnp.where(indices < extent // 2, indices, indices - extent).astype(jnp.float32) / extent
    )
    square = signed * signed
    turn = math.pi * defocus_values[:, None]
    row_phase = turn * square[None, :] - AMPLITUDE
    col_phase = turn * square[None, :]
    row_sin, row_cos = jnp.sin(row_phase), jnp.cos(row_phase)
    col_sin, col_cos = jnp.sin(col_phase), jnp.cos(col_phase)
    ctf = -(row_sin[:, :, None] * col_cos[:, None, :] + row_cos[:, :, None] * col_sin[:, None, :])
    return ctf / extent


def xor_pairs(count, shift):
    return [(d, d ^ shift) for d in range(count)]


def route_patches(patches, row_owner, my_index):
    sources, number = row_owner.shape
    extent = patches.shape[-1]
    chips = sources // 2
    devs = jnp.arange(sources, dtype=jnp.int32)
    chip_of = devs // 2
    owner_chip = row_owner // 2
    masks = [row_owner == (devs ^ 1)[:, None]]
    for m in range(1, chips):
        masks.append(owner_chip == (chip_of ^ m)[:, None])
    match = jnp.stack(masks, axis=1)
    first = jnp.where(match[..., 0], 0, jnp.where(match[..., 1], 1, number))
    second = jnp.where(match[..., 0] & match[..., 1], 1, number)
    send_sel = jnp.stack([first, second], axis=-1)
    send_pid = jnp.where(send_sel < number, devs[:, None, None] * number + send_sel, -1)
    padded = jnp.concatenate([patches, jnp.zeros((1, extent, extent), patches.dtype)], axis=0)
    my_sel = lax.dynamic_index_in_dim(send_sel, my_index, 0, keepdims=False)
    outgoing = jnp.take(padded, my_sel.reshape(-1), axis=0).reshape(chips, 2, extent, extent)
    partner = my_index ^ 1
    my_chip = my_index // 2
    direct = lax.ppermute(outgoing[0], "patch", xor_pairs(sources, 1))
    received = []
    for m in range(1, chips):
        received.append(lax.ppermute(outgoing[m], "patch", xor_pairs(sources, 2 * m)))
    received = jnp.concatenate(received, axis=0)
    forwarded = lax.ppermute(received, "patch", xor_pairs(sources, 1))
    cand_pid = [my_index * number + jnp.arange(number, dtype=jnp.int32)]
    cand_pid.append(lax.dynamic_index_in_dim(send_pid, partner, 0, keepdims=False)[0])
    for core in (my_index % 2, partner % 2):
        for m in range(1, chips):
            source = (my_chip ^ m) * 2 + core
            cand_pid.append(lax.dynamic_index_in_dim(send_pid, source, 0, keepdims=False)[m])
    cand_pid = jnp.concatenate(cand_pid)
    flat_owner = row_owner.reshape(-1)
    hits = (flat_owner == my_index).astype(jnp.int32)
    rank_in = jnp.cumsum(hits) - hits
    slot_ids = jnp.arange(CAP, dtype=jnp.int32)
    wanted = (hits[None, :] == 1) & (rank_in[None, :] == slot_ids[:, None])
    patch_ids = jnp.arange(sources * number, dtype=jnp.int32)
    slot_pid = jnp.sum(jnp.where(wanted, patch_ids[None, :], 0), axis=1)
    present = jnp.any(wanted, axis=1)
    cand_ids = jnp.arange(cand_pid.shape[0], dtype=jnp.int32)
    found = cand_pid[None, :] == slot_pid[:, None]
    take_idx = jnp.sum(jnp.where(found, cand_ids[None, :], 0), axis=1)
    take_idx = jnp.where(present, take_idx, cand_pid.shape[0])
    pieces = (patches, direct, received, forwarded)
    return take_idx, pieces, jnp.where(present, slot_pid, sources * number), outgoing


def spectra_kernel(rows, take_ref, own_ref, direct_ref, recv_ref, fwd_ref, scale_ref, half_ref,
                   full_ref, re_ref, im_ref):
    number = own_ref.shape[0]
    extent = own_ref.shape[-1]
    half_table = half_ref[...]
    full_table = full_ref[...]
    for s in range(re_ref.shape[0]):
        idx = take_ref[s]
        pick_own = own_ref[jnp.clip(idx, 0, number - 1)]
        pick_direct = direct_ref[jnp.clip(idx - number, 0, number - 1)]
        pick_recv = recv_ref[jnp.clip(idx - 2 * number, 0, rows - 1)]
        pick_fwd = fwd_ref[jnp.clip(idx - 2 * number - rows, 0, rows - 1)]
        zero = jnp.zeros_like(pick_own)
        image = jnp.where(
            idx < number, pick_own,
            jnp.where(idx < 2 * number, pick_direct,
                      jnp.where(idx < 2 * number + rows, pick_recv,
                                jnp.where(idx < 2 * number + 2 * rows, pick_fwd, zero))))
        half = jnp.dot(image, half_table, preferred_element_type=jnp.float32).astype(jnp.bfloat16)
        half_stack = jnp.concatenate([half[:, :extent], half[:, extent:]], axis=0)
        spec = jnp.dot(full_table, half_stack, preferred_element_type=jnp.float32)
        scale = scale_ref[s]
        re_ref[s] = (spec[:extent] * scale).astype(jnp.bfloat16)
        im_ref[s] = (spec[extent:] * scale).astype(jnp.bfloat16)


def make_spectra(take_idx, own, direct, received, forwarded, scale, half_table, full_table):
    count, extent = (scale.shape[0], scale.shape[-1])
    rows = received.shape[0]
    whole = pl.BlockSpec(memory_space=pltpu.VMEM)
    spec_shape = jax.ShapeDtypeStruct((count, extent, extent), jnp.bfloat16)
    return pl.pallas_call(
        functools.partial(spectra_kernel, rows),
        in_specs=[pl.BlockSpec(memory_space=pltpu.SMEM)] + [whole] * 7,
        out_specs=[whole, whole],
        out_shape=[spec_shape, spec_shape],
        cost_estimate=pl.CostEstimate(
            flops=3 * count * 6 * extent * extent * extent, transcendentals=0,
            bytes_accessed=count * 10 * extent * extent),
    )(take_idx, own, direct, received, forwarded, scale, half_table, full_table)


def corr_kernel(first, last, counts, orient_total, *refs):
    groups = len(counts)
    orient_ref, sr_ref, si_ref = refs[:3]
    templ_refs = refs[3:3 + groups]
    fw_ref, inv_ref = refs[3 + groups:5 + groups]
    rest = refs[5 + groups:]
    if first:
        top_ref, sum_ref, sq_ref, peak_ref = rest
    else:
        top_in, sum_in, sq_in, peak_in, top_ref, sum_ref, sq_ref, peak_ref = rest
    extent = sr_ref.shape[-1]
    sr = sr_ref[0].astype(jnp.float32)
    si = si_ref[0].astype(jnp.float32)
    forward = fw_ref[...]
    inverse = inv_ref[...]
    row_shape = (8, 128 * ((orient_total + 127) // 128))
    lanes = lax.broadcasted_iota(jnp.int32, row_shape, 1)
    peak_row = jnp.zeros(row_shape, jnp.float32) if first else peak_in[0]
    top = total = square = None
    prods = []
    for templ_ref, count in zip(templ_refs, counts):
        for t in range(count):
            tr = templ_ref[t].astype(jnp.float32)
            ti = templ_ref[count + t].astype(jnp.float32)
            pre = (sr * tr + si * ti).astype(jnp.bfloat16)
            pim = (si * tr - sr * ti).astype(jnp.bfloat16)
            prods.append(jnp.concatenate([pre, pim], axis=1))
    q_all = jnp.dot(jnp.concatenate(prods, axis=0), forward,
                    preferred_element_type=jnp.float32).astype(jnp.bfloat16)
    for position in range(len(prods)):
        q = q_all[position * extent:(position + 1) * extent]
        q_stack = jnp.concatenate([q[:, :extent], q[:, extent:]], axis=0)
        corr = jnp.dot(inverse, q_stack, preferred_element_type=jnp.float32)
        peak_row = jnp.where(lanes == orient_ref[position], jnp.max(corr), peak_row)
        if top is None:
            top, total, square = corr, corr, corr * corr
        else:
            top = jnp.maximum(top, corr)
            total = total + corr
            square = square + corr * corr
    if not first:
        top = jnp.maximum(top_in[0], top)
        total = sum_in[0] + total
        square = sq_in[0] + square
    top_ref[0] = top
    if last:
        s = pl.program_id(0)
        peak_ref[pl.ds(s, 1), :] = peak_row[0:1, :orient_total]
    else:
        peak_ref[0] = peak_row
    if last:
        mean = total / orient_total
        sum_ref[0] = mean
        sq_ref[0] = square / orient_total - mean * mean
    else:
        sum_ref[0] = total
        sq_ref[0] = square


def correlate_chunk(spec_re, spec_im, templ_groups, forward, inverse, orient_chunk,
                    orient_total, stats, last):
    count, extent = (spec_re.shape[0], spec_re.shape[-1])
    counts = tuple(group.shape[0] // 2 for group in templ_groups)
    tiles = sum(counts)
    first = stats is None
    lanes = 128 * ((orient_total + 127) // 128)
    plane = pl.BlockSpec((1, extent, extent), lambda s: (s, 0, 0))
    peak_spec = pl.BlockSpec((1, 8, lanes), lambda s: (s, 0, 0))
    templ_specs = [pl.BlockSpec(group.shape, lambda s: (0, 0, 0)) for group in templ_groups]
    fw_spec = pl.BlockSpec(forward.shape, lambda s: (0, 0))
    inv_spec = pl.BlockSpec(inverse.shape, lambda s: (0, 0))
    in_specs = [pl.BlockSpec(memory_space=pltpu.SMEM), plane, plane] + templ_specs + [
        fw_spec, inv_spec]
    operands = [orient_chunk, spec_re, spec_im] + list(templ_groups) + [forward, inverse]
    aliases = {}
    if not first:
        base = len(operands)
        in_specs += [plane, plane, plane, peak_spec]
        operands += list(stats)
        aliases = {base: 0, base + 1: 1, base + 2: 2}
        if not last:
            aliases[base + 3] = 3
    map_shape = jax.ShapeDtypeStruct((count, extent, extent), jnp.float32)
    flops = 3 * tiles * count * 12 * extent * extent * extent
    return pl.pallas_call(
        functools.partial(corr_kernel, first, last, counts, orient_total),
        grid=(count,),
        in_specs=in_specs,
        out_specs=[plane, plane, plane,
                   pl.BlockSpec((count, orient_total), lambda s: (0, 0)) if last else peak_spec],
        out_shape=[map_shape, map_shape, map_shape,
                   jax.ShapeDtypeStruct((count, orient_total) if last else (count, 8, lanes),
                                        jnp.float32)],
        input_output_aliases=aliases,
        compiler_params=pltpu.CompilerParams(dimension_semantics=("arbitrary",)),
        cost_estimate=pl.CostEstimate(
            flops=flops, transcendentals=0,
            bytes_accessed=tiles * 4 * extent * extent * 2 + count * 10 * extent * extent * 4),
    )(*operands)


def correlate_all(spec_re, spec_im, templ_re, templ_im, orientation, forward, inverse):
    blocks = lax.axis_size("blk")
    me = lax.axis_index("blk")
    sources = lax.axis_size("patch")
    core = lax.axis_index("patch") % 2
    tiles = templ_re.shape[0]
    half = tiles // 2
    orient_total = orientation.shape[0]
    local = jnp.concatenate([templ_re, templ_im], axis=0)
    mine = jnp.concatenate(
        [lax.dynamic_slice_in_dim(templ_re, core * half, half, 0),
         lax.dynamic_slice_in_dim(templ_im, core * half, half, 0)], axis=0)
    within = jnp.arange(half, dtype=jnp.int32)
    first_groups = [local]
    first_index = [me * tiles + jnp.arange(tiles, dtype=jnp.int32)]
    late_groups, late_index = [], []
    for k in range(1, blocks):
        source = me ^ k
        got = lax.ppermute(mine, "blk", [(b, b ^ k) for b in range(blocks)])
        passed = lax.ppermute(got, "patch", xor_pairs(sources, 1))
        first_groups.append(got)
        first_index.append(source * tiles + core * half + within)
        if k == 1:
            first_groups.append(passed)
            first_index.append(source * tiles + (1 - core) * half + within)
        else:
            late_groups.append(passed)
            late_index.append(source * tiles + (1 - core) * half + within)
    chunks = [(first_groups, jnp.concatenate(first_index))]
    if late_groups:
        chunks.append((late_groups, jnp.concatenate(late_index)))
    stats = None
    for n, (groups, index) in enumerate(chunks):
        orient_chunk = jnp.take(orientation, index)
        stats = correlate_chunk(spec_re, spec_im, groups, forward, inverse, orient_chunk,
                                orient_total, stats, n == len(chunks) - 1)
    top_map, mean_map, var_map, peak = stats
    return (top_map, mean_map, var_map, peak)


def body(patches, owner_of_patch, group_of_patch, defocus, templ_re, templ_im, orientation):
    sources = lax.axis_size("patch")
    my_index = lax.axis_index("patch")
    number, extent = (patches.shape[0], patches.shape[1])
    forward, half_table, inverse = (jnp.asarray(table) for table in dft_tables(extent))
    row_owner = owner_of_patch.reshape(sources, number)
    take_idx, pieces, slot_row, outgoing = route_patches(patches, row_owner, my_index)
    templ_re, templ_im, unused = lax.optimization_barrier((templ_re, templ_im, outgoing))
    groups = jnp.take(jnp.concatenate([group_of_patch, jnp.zeros((1,), jnp.int32)]), slot_row)
    focus_values = jnp.take(defocus, groups)
    scale = ctf_scale(focus_values, extent)
    spec_re, spec_im = make_spectra(take_idx, *pieces, scale, half_table, forward)
    return correlate_all(spec_re, spec_im, templ_re, templ_im, orientation, forward, inverse)


def solution(mesh):
    placed = (
        P(("blk", "patch"), None, None),
        P("blk"),
        P("blk"),
        P(),
        P("blk", None, None),
        P("blk", None, None),
        P(),
    )
    return jax.shard_map(
        body,
        mesh=mesh,
        in_specs=placed,
        out_specs=(
            P(("blk", "patch"), None, None),
            P(("blk", "patch"), None, None),
            P(("blk", "patch"), None, None),
            P(("blk", "patch"), None),
        ),
        check_vma=False,
    )
```

```python
import functools
import math

import jax
import ml_dtypes
import numpy as np
import jax.numpy as jnp
from jax import lax
from jax.experimental import pallas as pl
from jax.experimental.pallas import tpu as pltpu
from jax.sharding import PartitionSpec as P

SLOT = 2
CAP = 4
TILE_T = 4


AMPLITUDE = 0.07


def dft_tables(extent):
    indices = np.arange(extent, dtype=np.int64)
    turn_count = indices[:, None] * indices[None, :] % extent
    angles = turn_count.astype(np.float32) * np.float32(2.0 * math.pi / extent)
    cosine = np.cos(angles).astype(ml_dtypes.bfloat16)
    sine = np.sin(angles).astype(ml_dtypes.bfloat16)
    forward = np.concatenate(
        [np.concatenate([cosine, sine], axis=1), np.concatenate([-sine, cosine], axis=1)], axis=0
    )
    half_table = np.concatenate([cosine, -sine], axis=1)
    inverse = (half_table.astype(np.float32) / extent).astype(ml_dtypes.bfloat16)
    return forward, half_table, inverse


def ctf_filter(defocus_values, extent):
    indices = jnp.arange(extent, dtype=jnp.int32)
    signed = (
        jnp.where(indices < extent // 2, indices, indices - extent).astype(jnp.float32) / extent
    )
    radius = signed[:, None] * signed[:, None] + signed[None, :] * signed[None, :]
    phases = math.pi * defocus_values[:, None, None] * radius[None, :, :] - AMPLITUDE
    return -jnp.sin(phases)


def ctf_scale(defocus_values, extent):
    indices = jnp.arange(extent, dtype=jnp.int32)
    signed = (
        jnp.where(indices < extent // 2, indices, indices - extent).astype(jnp.float32) / extent
    )
    square = signed * signed
    turn = math.pi * defocus_values[:, None]
    row_phase = turn * square[None, :] - AMPLITUDE
    col_phase = turn * square[None, :]
    row_sin, row_cos = jnp.sin(row_phase), jnp.cos(row_phase)
    col_sin, col_cos = jnp.sin(col_phase), jnp.cos(col_phase)
    ctf = -(row_sin[:, :, None] * col_cos[:, None, :] + row_cos[:, :, None] * col_sin[:, None, :])
    return ctf / extent


def xor_pairs(count, shift):
    return [(d, d ^ shift) for d in range(count)]


def route_patches(patches, row_owner, my_index):
    sources, number = row_owner.shape
    extent = patches.shape[-1]
    chips = sources // 2
    devs = jnp.arange(sources, dtype=jnp.int32)
    chip_of = devs // 2
    owner_chip = row_owner // 2
    masks = [row_owner == (devs ^ 1)[:, None]]
    for m in range(1, chips):
        masks.append(owner_chip == (chip_of ^ m)[:, None])
    match = jnp.stack(masks, axis=1)
    first = jnp.where(match[..., 0], 0, jnp.where(match[..., 1], 1, number))
    second = jnp.where(match[..., 0] & match[..., 1], 1, number)
    send_sel = jnp.stack([first, second], axis=-1)
    send_pid = jnp.where(send_sel < number, devs[:, None, None] * number + send_sel, -1)
    padded = jnp.concatenate([patches, jnp.zeros((1, extent, extent), patches.dtype)], axis=0)
    my_sel = lax.dynamic_index_in_dim(send_sel, my_index, 0, keepdims=False)
    outgoing = jnp.take(padded, my_sel.reshape(-1), axis=0).reshape(chips, 2, extent, extent)
    partner = my_index ^ 1
    my_chip = my_index // 2
    direct = lax.ppermute(outgoing[0], "patch", xor_pairs(sources, 1))
    received = []
    for m in range(1, chips):
        received.append(lax.ppermute(outgoing[m], "patch", xor_pairs(sources, 2 * m)))
    received = jnp.concatenate(received, axis=0)
    forwarded = lax.ppermute(received, "patch", xor_pairs(sources, 1))
    cand_pid = [my_index * number + jnp.arange(number, dtype=jnp.int32)]
    cand_pid.append(lax.dynamic_index_in_dim(send_pid, partner, 0, keepdims=False)[0])
    for core in (my_index % 2, partner % 2):
        for m in range(1, chips):
            source = (my_chip ^ m) * 2 + core
            cand_pid.append(lax.dynamic_index_in_dim(send_pid, source, 0, keepdims=False)[m])
    cand_pid = jnp.concatenate(cand_pid)
    flat_owner = row_owner.reshape(-1)
    hits = (flat_owner == my_index).astype(jnp.int32)
    rank_in = jnp.cumsum(hits) - hits
    slot_ids = jnp.arange(CAP, dtype=jnp.int32)
    wanted = (hits[None, :] == 1) & (rank_in[None, :] == slot_ids[:, None])
    patch_ids = jnp.arange(sources * number, dtype=jnp.int32)
    slot_pid = jnp.sum(jnp.where(wanted, patch_ids[None, :], 0), axis=1)
    present = jnp.any(wanted, axis=1)
    cand_ids = jnp.arange(cand_pid.shape[0], dtype=jnp.int32)
    found = cand_pid[None, :] == slot_pid[:, None]
    take_idx = jnp.sum(jnp.where(found, cand_ids[None, :], 0), axis=1)
    take_idx = jnp.where(present, take_idx, cand_pid.shape[0])
    pieces = (patches, direct, received, forwarded)
    return take_idx, pieces, jnp.where(present, slot_pid, sources * number), outgoing


def spectra_kernel(rows, take_ref, own_ref, direct_ref, recv_ref, fwd_ref, scale_ref, half_ref,
                   full_ref, re_ref, im_ref):
    number = own_ref.shape[0]
    extent = own_ref.shape[-1]
    half_table = half_ref[...]
    full_table = full_ref[...]
    for s in range(re_ref.shape[0]):
        idx = take_ref[s]
        pick_own = own_ref[jnp.clip(idx, 0, number - 1)]
        pick_direct = direct_ref[jnp.clip(idx - number, 0, number - 1)]
        pick_recv = recv_ref[jnp.clip(idx - 2 * number, 0, rows - 1)]
        pick_fwd = fwd_ref[jnp.clip(idx - 2 * number - rows, 0, rows - 1)]
        zero = jnp.zeros_like(pick_own)
        image = jnp.where(
            idx < number, pick_own,
            jnp.where(idx < 2 * number, pick_direct,
                      jnp.where(idx < 2 * number + rows, pick_recv,
                                jnp.where(idx < 2 * number + 2 * rows, pick_fwd, zero))))
        half = jnp.dot(image, half_table, preferred_element_type=jnp.float32).astype(jnp.bfloat16)
        half_stack = jnp.concatenate([half[:, :extent], half[:, extent:]], axis=0)
        spec = jnp.dot(full_table, half_stack, preferred_element_type=jnp.float32)
        scale = scale_ref[s]
        re_ref[s] = (spec[:extent] * scale).astype(jnp.bfloat16)
        im_ref[s] = (spec[extent:] * scale).astype(jnp.bfloat16)


def make_spectra(take_idx, own, direct, received, forwarded, scale, half_table, full_table):
    count, extent = (scale.shape[0], scale.shape[-1])
    rows = received.shape[0]
    whole = pl.BlockSpec(memory_space=pltpu.VMEM)
    spec_shape = jax.ShapeDtypeStruct((count, extent, extent), jnp.bfloat16)
    return pl.pallas_call(
        functools.partial(spectra_kernel, rows),
        in_specs=[pl.BlockSpec(memory_space=pltpu.SMEM)] + [whole] * 7,
        out_specs=[whole, whole],
        out_shape=[spec_shape, spec_shape],
        cost_estimate=pl.CostEstimate(
            flops=3 * count * 6 * extent * extent * extent, transcendentals=0,
            bytes_accessed=count * 10 * extent * extent),
    )(take_idx, own, direct, received, forwarded, scale, half_table, full_table)


def corr_kernel(first, last, counts, orient_total, *refs):
    groups = len(counts)
    orient_ref, sr_ref, si_ref = refs[:3]
    templ_refs = refs[3:3 + groups]
    fw_ref, inv_ref = refs[3 + groups:5 + groups]
    rest = refs[5 + groups:]
    if first:
        top_ref, sum_ref, sq_ref, peak_ref = rest
    else:
        top_in, sum_in, sq_in, peak_in, top_ref, sum_ref, sq_ref, peak_ref = rest
    extent = sr_ref.shape[-1]
    sr = sr_ref[0].astype(jnp.float32)
    si = si_ref[0].astype(jnp.float32)
    forward = fw_ref[...]
    inverse = inv_ref[...]
    row_shape = (8, 128 * ((orient_total + 127) // 128))
    lanes = lax.broadcasted_iota(jnp.int32, row_shape, 1)
    peak_row = jnp.zeros(row_shape, jnp.float32) if first else peak_in[0]
    top = total = square = None
    prods = []
    for templ_ref, (count, parts) in zip(templ_refs, counts):
        for part in range(parts):
            for t in range(count):
                tr = templ_ref[2 * count * part + t].astype(jnp.float32)
                ti = templ_ref[2 * count * part + count + t].astype(jnp.float32)
                pre = (sr * tr + si * ti).astype(jnp.bfloat16)
                pim = (si * tr - sr * ti).astype(jnp.bfloat16)
                prods.append(jnp.concatenate([pre, pim], axis=1))
    q_all = jnp.dot(jnp.concatenate(prods, axis=0), forward,
                    preferred_element_type=jnp.float32).astype(jnp.bfloat16)
    for position in range(len(prods)):
        q = q_all[position * extent:(position + 1) * extent]
        q_stack = jnp.concatenate([q[:, :extent], q[:, extent:]], axis=0)
        corr = jnp.dot(inverse, q_stack, preferred_element_type=jnp.float32)
        peak_row = jnp.where(lanes == orient_ref[position], jnp.max(corr), peak_row)
        if top is None:
            top, total, square = corr, corr, corr * corr
        else:
            top = jnp.maximum(top, corr)
            total = total + corr
            square = square + corr * corr
    if not first:
        top = jnp.maximum(top_in[0], top)
        total = sum_in[0] + total
        square = sq_in[0] + square
    top_ref[0] = top
    if last:
        s = pl.program_id(0)
        peak_ref[pl.ds(s, 1), :] = peak_row[0:1, :orient_total]
    else:
        peak_ref[0] = peak_row
    if last:
        mean = total / orient_total
        sum_ref[0] = mean
        sq_ref[0] = square / orient_total - mean * mean
    else:
        sum_ref[0] = total
        sq_ref[0] = square


def correlate_chunk(spec_re, spec_im, templ_groups, template_counts, forward, inverse,
                    orient_chunk, orient_total, stats, last):
    count, extent = (spec_re.shape[0], spec_re.shape[-1])
    counts = tuple(template_counts)
    tiles = sum(count * parts for count, parts in counts)
    first = stats is None
    lanes = 128 * ((orient_total + 127) // 128)
    plane = pl.BlockSpec((1, extent, extent), lambda s: (s, 0, 0))
    peak_spec = pl.BlockSpec((1, 8, lanes), lambda s: (s, 0, 0))
    templ_specs = [pl.BlockSpec(group.shape, lambda s: (0, 0, 0)) for group in templ_groups]
    fw_spec = pl.BlockSpec(forward.shape, lambda s: (0, 0))
    inv_spec = pl.BlockSpec(inverse.shape, lambda s: (0, 0))
    in_specs = [pl.BlockSpec(memory_space=pltpu.SMEM), plane, plane] + templ_specs + [
        fw_spec, inv_spec]
    operands = [orient_chunk, spec_re, spec_im] + list(templ_groups) + [forward, inverse]
    aliases = {}
    if not first:
        base = len(operands)
        in_specs += [plane, plane, plane, peak_spec]
        operands += list(stats)
        aliases = {base: 0, base + 1: 1, base + 2: 2}
        if not last:
            aliases[base + 3] = 3
    map_shape = jax.ShapeDtypeStruct((count, extent, extent), jnp.float32)
    flops = 3 * tiles * count * 12 * extent * extent * extent
    return pl.pallas_call(
        functools.partial(corr_kernel, first, last, counts, orient_total),
        grid=(count,),
        in_specs=in_specs,
        out_specs=[plane, plane, plane,
                   pl.BlockSpec((count, orient_total), lambda s: (0, 0)) if last else peak_spec],
        out_shape=[map_shape, map_shape, map_shape,
                   jax.ShapeDtypeStruct((count, orient_total) if last else (count, 8, lanes),
                                        jnp.float32)],
        input_output_aliases=aliases,
        compiler_params=pltpu.CompilerParams(dimension_semantics=("arbitrary",)),
        cost_estimate=pl.CostEstimate(
            flops=flops, transcendentals=0,
            bytes_accessed=tiles * 4 * extent * extent * 2 + count * 10 * extent * extent * 4),
    )(*operands)


def correlate_all(spec_re, spec_im, templ_re, templ_im, orientation, forward, inverse):
    blocks = lax.axis_size("blk")
    me = lax.axis_index("blk")
    sources = lax.axis_size("patch")
    core = lax.axis_index("patch") % 2
    tiles = templ_re.shape[0]
    half = tiles // 2
    orient_total = orientation.shape[0]
    local = jnp.concatenate([templ_re, templ_im], axis=0)
    mine = jnp.concatenate(
        [lax.dynamic_slice_in_dim(templ_re, core * half, half, 0),
         lax.dynamic_slice_in_dim(templ_im, core * half, half, 0)], axis=0)
    within = jnp.arange(half, dtype=jnp.int32)
    first_groups = [(local, 1)]
    first_index = [me * tiles + jnp.arange(tiles, dtype=jnp.int32)]
    late_got, late_index = [], []
    for k in range(1, blocks):
        source = me ^ k
        got = lax.ppermute(mine, "blk", [(b, b ^ k) for b in range(blocks)])
        first_groups.append((got, 1))
        first_index.append(source * tiles + core * half + within)
        if k == 1:
            first_groups.append((lax.ppermute(got, "patch", xor_pairs(sources, 1)), 1))
            first_index.append(source * tiles + (1 - core) * half + within)
        else:
            late_got.append(got)
            late_index.append(source * tiles + (1 - core) * half + within)
    chunks = [(first_groups, jnp.concatenate(first_index))]
    if late_got:
        passed = lax.ppermute(jnp.concatenate(late_got, axis=0), "patch", xor_pairs(sources, 1))
        chunks.append(([(passed, len(late_got))], jnp.concatenate(late_index)))
    stats = None
    for n, (groups, index) in enumerate(chunks):
        orient_chunk = jnp.take(orientation, index)
        counts = [(group.shape[0] // (2 * parts), parts) for group, parts in groups]
        stats = correlate_chunk(spec_re, spec_im, [group for group, parts in groups], counts,
                                forward, inverse, orient_chunk, orient_total, stats,
                                n == len(chunks) - 1)
    top_map, mean_map, var_map, peak = stats
    return (top_map, mean_map, var_map, peak)


def body(patches, owner_of_patch, group_of_patch, defocus, templ_re, templ_im, orientation):
    sources = lax.axis_size("patch")
    my_index = lax.axis_index("patch")
    number, extent = (patches.shape[0], patches.shape[1])
    forward, half_table, inverse = (jnp.asarray(table) for table in dft_tables(extent))
    row_owner = owner_of_patch.reshape(sources, number)
    take_idx, pieces, slot_row, outgoing = route_patches(patches, row_owner, my_index)
    templ_re, templ_im, unused = lax.optimization_barrier((templ_re, templ_im, outgoing))
    groups = jnp.take(jnp.concatenate([group_of_patch, jnp.zeros((1,), jnp.int32)]), slot_row)
    focus_values = jnp.take(defocus, groups)
    scale = ctf_scale(focus_values, extent)
    spec_re, spec_im = make_spectra(take_idx, *pieces, scale, half_table, forward)
    return correlate_all(spec_re, spec_im, templ_re, templ_im, orientation, forward, inverse)


def solution(mesh):
    placed = (
        P(("blk", "patch"), None, None),
        P("blk"),
        P("blk"),
        P(),
        P("blk", None, None),
        P("blk", None, None),
        P(),
    )
    return jax.shard_map(
        body,
        mesh=mesh,
        in_specs=placed,
        out_specs=(
            P(("blk", "patch"), None, None),
            P(("blk", "patch"), None, None),
            P(("blk", "patch"), None, None),
            P(("blk", "patch"), None),
        ),
        check_vma=False,
    )
```

```python
import functools
import math

import jax
import ml_dtypes
import numpy as np
import jax.numpy as jnp
from jax import lax
from jax.experimental import pallas as pl
from jax.experimental.pallas import tpu as pltpu
from jax.sharding import PartitionSpec as P

SLOT = 2
CAP = 4
TILE_T = 4


AMPLITUDE = 0.07


def dft_tables(extent):
    indices = np.arange(extent, dtype=np.int64)
    turn_count = indices[:, None] * indices[None, :] % extent
    angles = turn_count.astype(np.float32) * np.float32(2.0 * math.pi / extent)
    cosine = np.cos(angles).astype(ml_dtypes.bfloat16)
    sine = np.sin(angles).astype(ml_dtypes.bfloat16)
    forward = np.concatenate(
        [np.concatenate([cosine, sine], axis=1), np.concatenate([-sine, cosine], axis=1)], axis=0
    )
    half_table = np.concatenate([cosine, -sine], axis=1)
    inverse = (half_table.astype(np.float32) / extent).astype(ml_dtypes.bfloat16)
    return forward, half_table, inverse


def ctf_filter(defocus_values, extent):
    indices = jnp.arange(extent, dtype=jnp.int32)
    signed = (
        jnp.where(indices < extent // 2, indices, indices - extent).astype(jnp.float32) / extent
    )
    radius = signed[:, None] * signed[:, None] + signed[None, :] * signed[None, :]
    phases = math.pi * defocus_values[:, None, None] * radius[None, :, :] - AMPLITUDE
    return -jnp.sin(phases)


def ctf_scale(defocus_values, extent):
    indices = jnp.arange(extent, dtype=jnp.int32)
    signed = (
        jnp.where(indices < extent // 2, indices, indices - extent).astype(jnp.float32) / extent
    )
    square = signed * signed
    turn = math.pi * defocus_values[:, None]
    row_phase = turn * square[None, :] - AMPLITUDE
    col_phase = turn * square[None, :]
    row_sin, row_cos = jnp.sin(row_phase), jnp.cos(row_phase)
    col_sin, col_cos = jnp.sin(col_phase), jnp.cos(col_phase)
    ctf = -(row_sin[:, :, None] * col_cos[:, None, :] + row_cos[:, :, None] * col_sin[:, None, :])
    return ctf / extent


def xor_pairs(count, shift):
    return [(d, d ^ shift) for d in range(count)]


def route_patches(patches, row_owner, my_index):
    sources, number = row_owner.shape
    extent = patches.shape[-1]
    chips = sources // 2
    devs = jnp.arange(sources, dtype=jnp.int32)
    chip_of = devs // 2
    owner_chip = row_owner // 2
    masks = [row_owner == (devs ^ 1)[:, None]]
    for m in range(1, chips):
        masks.append(owner_chip == (chip_of ^ m)[:, None])
    match = jnp.stack(masks, axis=1)
    first = jnp.where(match[..., 0], 0, jnp.where(match[..., 1], 1, number))
    second = jnp.where(match[..., 0] & match[..., 1], 1, number)
    send_sel = jnp.stack([first, second], axis=-1)
    send_pid = jnp.where(send_sel < number, devs[:, None, None] * number + send_sel, -1)
    padded = jnp.concatenate([patches, jnp.zeros((1, extent, extent), patches.dtype)], axis=0)
    my_sel = lax.dynamic_index_in_dim(send_sel, my_index, 0, keepdims=False)
    outgoing = jnp.take(padded, my_sel.reshape(-1), axis=0).reshape(chips, 2, extent, extent)
    partner = my_index ^ 1
    my_chip = my_index // 2
    direct = lax.ppermute(outgoing[0], "patch", xor_pairs(sources, 1))
    received = []
    for m in range(1, chips):
        received.append(lax.ppermute(outgoing[m], "patch", xor_pairs(sources, 2 * m)))
    received = jnp.concatenate(received, axis=0)
    forwarded = lax.ppermute(received, "patch", xor_pairs(sources, 1))
    cand_pid = [my_index * number + jnp.arange(number, dtype=jnp.int32)]
    cand_pid.append(lax.dynamic_index_in_dim(send_pid, partner, 0, keepdims=False)[0])
    for core in (my_index % 2, partner % 2):
        for m in range(1, chips):
            source = (my_chip ^ m) * 2 + core
            cand_pid.append(lax.dynamic_index_in_dim(send_pid, source, 0, keepdims=False)[m])
    cand_pid = jnp.concatenate(cand_pid)
    flat_owner = row_owner.reshape(-1)
    hits = (flat_owner == my_index).astype(jnp.int32)
    rank_in = jnp.cumsum(hits) - hits
    slot_ids = jnp.arange(CAP, dtype=jnp.int32)
    wanted = (hits[None, :] == 1) & (rank_in[None, :] == slot_ids[:, None])
    patch_ids = jnp.arange(sources * number, dtype=jnp.int32)
    slot_pid = jnp.sum(jnp.where(wanted, patch_ids[None, :], 0), axis=1)
    present = jnp.any(wanted, axis=1)
    cand_ids = jnp.arange(cand_pid.shape[0], dtype=jnp.int32)
    found = cand_pid[None, :] == slot_pid[:, None]
    take_idx = jnp.sum(jnp.where(found, cand_ids[None, :], 0), axis=1)
    take_idx = jnp.where(present, take_idx, cand_pid.shape[0])
    pieces = (patches, direct, received, forwarded)
    return take_idx, pieces, jnp.where(present, slot_pid, sources * number), outgoing


def spectra_kernel(rows, take_ref, own_ref, direct_ref, recv_ref, fwd_ref, scale_ref, half_ref,
                   full_ref, re_ref, im_ref):
    number = own_ref.shape[0]
    extent = own_ref.shape[-1]
    half_table = half_ref[...]
    full_table = full_ref[...]
    for s in range(re_ref.shape[0]):
        idx = take_ref[s]
        pick_own = own_ref[jnp.clip(idx, 0, number - 1)]
        pick_direct = direct_ref[jnp.clip(idx - number, 0, number - 1)]
        pick_recv = recv_ref[jnp.clip(idx - 2 * number, 0, rows - 1)]
        pick_fwd = fwd_ref[jnp.clip(idx - 2 * number - rows, 0, rows - 1)]
        zero = jnp.zeros_like(pick_own)
        image = jnp.where(
            idx < number, pick_own,
            jnp.where(idx < 2 * number, pick_direct,
                      jnp.where(idx < 2 * number + rows, pick_recv,
                                jnp.where(idx < 2 * number + 2 * rows, pick_fwd, zero))))
        half = jnp.dot(image, half_table, preferred_element_type=jnp.float32).astype(jnp.bfloat16)
        half_stack = jnp.concatenate([half[:, :extent], half[:, extent:]], axis=0)
        spec = jnp.dot(full_table, half_stack, preferred_element_type=jnp.float32)
        scale = scale_ref[s]
        re_ref[s] = (spec[:extent] * scale).astype(jnp.bfloat16)
        im_ref[s] = (spec[extent:] * scale).astype(jnp.bfloat16)


def make_spectra(take_idx, own, direct, received, forwarded, scale, half_table, full_table):
    count, extent = (scale.shape[0], scale.shape[-1])
    rows = received.shape[0]
    whole = pl.BlockSpec(memory_space=pltpu.VMEM)
    spec_shape = jax.ShapeDtypeStruct((count, extent, extent), jnp.bfloat16)
    return pl.pallas_call(
        functools.partial(spectra_kernel, rows),
        in_specs=[pl.BlockSpec(memory_space=pltpu.SMEM)] + [whole] * 7,
        out_specs=[whole, whole],
        out_shape=[spec_shape, spec_shape],
        cost_estimate=pl.CostEstimate(
            flops=3 * count * 6 * extent * extent * extent, transcendentals=0,
            bytes_accessed=count * 10 * extent * extent),
    )(take_idx, own, direct, received, forwarded, scale, half_table, full_table)


def corr_kernel(first, last, counts, orient_total, *refs):
    groups = len(counts)
    orient_ref, sr_ref, si_ref = refs[:3]
    templ_refs = refs[3:3 + groups]
    fw_ref, inv_ref = refs[3 + groups:5 + groups]
    rest = refs[5 + groups:]
    if first:
        top_ref, sum_ref, sq_ref, peak_ref = rest
    else:
        top_in, sum_in, sq_in, peak_in, top_ref, sum_ref, sq_ref, peak_ref = rest
    extent = sr_ref.shape[-1]
    sr = sr_ref[0].astype(jnp.float32)
    si = si_ref[0].astype(jnp.float32)
    forward = fw_ref[...]
    inverse = inv_ref[...]
    row_shape = (8, 128 * ((orient_total + 127) // 128))
    lanes = lax.broadcasted_iota(jnp.int32, row_shape, 1)
    peak_row = jnp.zeros(row_shape, jnp.float32) if first else peak_in[0]
    top = total = square = None
    prods = []
    for templ_ref, (count, parts) in zip(templ_refs, counts):
        for part in range(parts):
            for t in range(count):
                tr = templ_ref[2 * count * part + t].astype(jnp.float32)
                ti = templ_ref[2 * count * part + count + t].astype(jnp.float32)
                pre = (sr * tr + si * ti).astype(jnp.bfloat16)
                pim = (si * tr - sr * ti).astype(jnp.bfloat16)
                prods.append(jnp.concatenate([pre, pim], axis=1))
    q_all = jnp.dot(jnp.concatenate(prods, axis=0), forward,
                    preferred_element_type=jnp.float32).astype(jnp.bfloat16)
    for position in range(len(prods)):
        q = q_all[position * extent:(position + 1) * extent]
        q_stack = jnp.concatenate([q[:, :extent], q[:, extent:]], axis=0)
        corr = jnp.dot(inverse, q_stack, preferred_element_type=jnp.float32)
        peak_row = jnp.where(lanes == orient_ref[position], jnp.max(corr), peak_row)
        if top is None:
            top, total, square = corr, corr, corr * corr
        else:
            top = jnp.maximum(top, corr)
            total = total + corr
            square = square + corr * corr
    if not first:
        top = jnp.maximum(top_in[0], top)
        total = sum_in[0] + total
        square = sq_in[0] + square
    top_ref[0] = top
    if last:
        s = pl.program_id(0)
        peak_ref[pl.ds(s, 1), :] = peak_row[0:1, :orient_total]
    else:
        peak_ref[0] = peak_row
    if last:
        mean = total / orient_total
        sum_ref[0] = mean
        sq_ref[0] = square / orient_total - mean * mean
    else:
        sum_ref[0] = total
        sq_ref[0] = square


def correlate_chunk(spec_re, spec_im, templ_groups, template_counts, forward, inverse,
                    orient_chunk, orient_total, stats, last):
    count, extent = (spec_re.shape[0], spec_re.shape[-1])
    counts = tuple(template_counts)
    tiles = sum(count * parts for count, parts in counts)
    first = stats is None
    lanes = 128 * ((orient_total + 127) // 128)
    plane = pl.BlockSpec((1, extent, extent), lambda s: (s, 0, 0))
    peak_spec = pl.BlockSpec((1, 8, lanes), lambda s: (s, 0, 0))
    templ_specs = [pl.BlockSpec(group.shape, lambda s: (0, 0, 0)) for group in templ_groups]
    fw_spec = pl.BlockSpec(forward.shape, lambda s: (0, 0))
    inv_spec = pl.BlockSpec(inverse.shape, lambda s: (0, 0))
    in_specs = [pl.BlockSpec(memory_space=pltpu.SMEM), plane, plane] + templ_specs + [
        fw_spec, inv_spec]
    operands = [orient_chunk, spec_re, spec_im] + list(templ_groups) + [forward, inverse]
    aliases = {}
    if not first:
        base = len(operands)
        in_specs += [plane, plane, plane, peak_spec]
        operands += list(stats)
        aliases = {base: 0, base + 1: 1, base + 2: 2}
        if not last:
            aliases[base + 3] = 3
    map_shape = jax.ShapeDtypeStruct((count, extent, extent), jnp.float32)
    flops = 3 * tiles * count * 12 * extent * extent * extent
    return pl.pallas_call(
        functools.partial(corr_kernel, first, last, counts, orient_total),
        grid=(count,),
        in_specs=in_specs,
        out_specs=[plane, plane, plane,
                   pl.BlockSpec((count, orient_total), lambda s: (0, 0)) if last else peak_spec],
        out_shape=[map_shape, map_shape, map_shape,
                   jax.ShapeDtypeStruct((count, orient_total) if last else (count, 8, lanes),
                                        jnp.float32)],
        input_output_aliases=aliases,
        compiler_params=pltpu.CompilerParams(dimension_semantics=("arbitrary",)),
        cost_estimate=pl.CostEstimate(
            flops=flops, transcendentals=0,
            bytes_accessed=tiles * 4 * extent * extent * 2 + count * 10 * extent * extent * 4),
    )(*operands)


def correlate_all(spec_re, spec_im, templ_re, templ_im, orientation, forward, inverse):
    blocks = lax.axis_size("blk")
    me = lax.axis_index("blk")
    sources = lax.axis_size("patch")
    core = lax.axis_index("patch") % 2
    tiles = templ_re.shape[0]
    half = tiles // 2
    orient_total = orientation.shape[0]
    local = jnp.concatenate([templ_re, templ_im], axis=0)
    mine = jnp.concatenate(
        [lax.dynamic_slice_in_dim(templ_re, core * half, half, 0),
         lax.dynamic_slice_in_dim(templ_im, core * half, half, 0)], axis=0)
    within = jnp.arange(half, dtype=jnp.int32)
    first_groups = [(local, 1)]
    first_index = [me * tiles + jnp.arange(tiles, dtype=jnp.int32)]
    late_got, late_index = [], []
    for k in range(1, blocks):
        source = me ^ k
        got = lax.ppermute(mine, "blk", [(b, b ^ k) for b in range(blocks)])
        first_groups.append((got, 1))
        first_index.append(source * tiles + core * half + within)
        late_got.append(got)
        late_index.append(source * tiles + (1 - core) * half + within)
    chunks = [(first_groups, jnp.concatenate(first_index))]
    if late_got:
        passed = lax.ppermute(jnp.concatenate(late_got, axis=0), "patch", xor_pairs(sources, 1))
        chunks.append(([(passed, len(late_got))], jnp.concatenate(late_index)))
    stats = None
    for n, (groups, index) in enumerate(chunks):
        orient_chunk = jnp.take(orientation, index)
        counts = [(group.shape[0] // (2 * parts), parts) for group, parts in groups]
        stats = correlate_chunk(spec_re, spec_im, [group for group, parts in groups], counts,
                                forward, inverse, orient_chunk, orient_total, stats,
                                n == len(chunks) - 1)
    top_map, mean_map, var_map, peak = stats
    return (top_map, mean_map, var_map, peak)


def body(patches, owner_of_patch, group_of_patch, defocus, templ_re, templ_im, orientation):
    sources = lax.axis_size("patch")
    my_index = lax.axis_index("patch")
    number, extent = (patches.shape[0], patches.shape[1])
    forward, half_table, inverse = (jnp.asarray(table) for table in dft_tables(extent))
    row_owner = owner_of_patch.reshape(sources, number)
    take_idx, pieces, slot_row, outgoing = route_patches(patches, row_owner, my_index)
    templ_re, templ_im, unused = lax.optimization_barrier((templ_re, templ_im, outgoing))
    groups = jnp.take(jnp.concatenate([group_of_patch, jnp.zeros((1,), jnp.int32)]), slot_row)
    focus_values = jnp.take(defocus, groups)
    scale = ctf_scale(focus_values, extent)
    spec_re, spec_im = make_spectra(take_idx, *pieces, scale, half_table, forward)
    return correlate_all(spec_re, spec_im, templ_re, templ_im, orientation, forward, inverse)


def solution(mesh):
    placed = (
        P(("blk", "patch"), None, None),
        P("blk"),
        P("blk"),
        P(),
        P("blk", None, None),
        P("blk", None, None),
        P(),
    )
    return jax.shard_map(
        body,
        mesh=mesh,
        in_specs=placed,
        out_specs=(
            P(("blk", "patch"), None, None),
            P(("blk", "patch"), None, None),
            P(("blk", "patch"), None, None),
            P(("blk", "patch"), None),
        ),
        check_vma=False,
    )
```

```python
import functools
import math

import jax
import ml_dtypes
import numpy as np
import jax.numpy as jnp
from jax import lax
from jax.experimental import pallas as pl
from jax.experimental.pallas import tpu as pltpu
from jax.sharding import PartitionSpec as P

SLOT = 2
CAP = 4
TILE_T = 4


AMPLITUDE = 0.07


def dft_tables(extent):
    indices = np.arange(extent, dtype=np.int64)
    turn_count = indices[:, None] * indices[None, :] % extent
    angles = turn_count.astype(np.float32) * np.float32(2.0 * math.pi / extent)
    cosine = np.cos(angles).astype(ml_dtypes.bfloat16)
    sine = np.sin(angles).astype(ml_dtypes.bfloat16)
    forward = np.concatenate(
        [np.concatenate([cosine, sine], axis=1), np.concatenate([-sine, cosine], axis=1)], axis=0
    )
    half_table = np.concatenate([cosine, -sine], axis=1)
    inverse = (half_table.astype(np.float32) / extent).astype(ml_dtypes.bfloat16)
    return forward, half_table, inverse


def ctf_filter(defocus_values, extent):
    indices = jnp.arange(extent, dtype=jnp.int32)
    signed = (
        jnp.where(indices < extent // 2, indices, indices - extent).astype(jnp.float32) / extent
    )
    radius = signed[:, None] * signed[:, None] + signed[None, :] * signed[None, :]
    phases = math.pi * defocus_values[:, None, None] * radius[None, :, :] - AMPLITUDE
    return -jnp.sin(phases)


def ctf_scale(defocus_values, extent):
    indices = jnp.arange(extent, dtype=jnp.int32)
    signed = (
        jnp.where(indices < extent // 2, indices, indices - extent).astype(jnp.float32) / extent
    )
    square = signed * signed
    turn = math.pi * defocus_values[:, None]
    row_phase = turn * square[None, :] - AMPLITUDE
    col_phase = turn * square[None, :]
    row_sin, row_cos = jnp.sin(row_phase), jnp.cos(row_phase)
    col_sin, col_cos = jnp.sin(col_phase), jnp.cos(col_phase)
    ctf = -(row_sin[:, :, None] * col_cos[:, None, :] + row_cos[:, :, None] * col_sin[:, None, :])
    return ctf / extent


def xor_pairs(count, shift):
    return [(d, d ^ shift) for d in range(count)]


def route_patches(patches, row_owner, my_index):
    sources, number = row_owner.shape
    extent = patches.shape[-1]
    chips = sources // 2
    devs = jnp.arange(sources, dtype=jnp.int32)
    chip_of = devs // 2
    owner_chip = row_owner // 2
    masks = [row_owner == (devs ^ 1)[:, None]]
    for m in range(1, chips):
        masks.append(owner_chip == (chip_of ^ m)[:, None])
    match = jnp.stack(masks, axis=1)
    first = jnp.where(match[..., 0], 0, jnp.where(match[..., 1], 1, number))
    second = jnp.where(match[..., 0] & match[..., 1], 1, number)
    send_sel = jnp.stack([first, second], axis=-1)
    send_pid = jnp.where(send_sel < number, devs[:, None, None] * number + send_sel, -1)
    padded = jnp.concatenate([patches, jnp.zeros((1, extent, extent), patches.dtype)], axis=0)
    my_sel = lax.dynamic_index_in_dim(send_sel, my_index, 0, keepdims=False)
    outgoing = jnp.take(padded, my_sel.reshape(-1), axis=0).reshape(chips, 2, extent, extent)
    partner = my_index ^ 1
    my_chip = my_index // 2
    direct = lax.ppermute(outgoing[0], "patch", xor_pairs(sources, 1))
    received = []
    for m in range(1, chips):
        received.append(lax.ppermute(outgoing[m], "patch", xor_pairs(sources, 2 * m)))
    received = jnp.concatenate(received, axis=0)
    recv_pid = jnp.concatenate(
        [jnp.take(send_pid[:, m], (chip_of ^ m) * 2 + devs % 2, axis=0) for m in range(1, chips)],
        axis=1)
    rows = recv_pid.shape[1]
    flat_owner = row_owner.reshape(-1)
    recv_owner = jnp.where(recv_pid >= 0, jnp.take(flat_owner, jnp.maximum(recv_pid, 0)), -1)
    for_partner = (recv_owner == (devs ^ 1)[:, None]).astype(jnp.int32)
    order = jnp.cumsum(for_partner, axis=1) - for_partner
    picks = jnp.arange(CAP, dtype=jnp.int32)
    chosen = (for_partner[:, None, :] == 1) & (order[:, None, :] == picks[None, :, None])
    fwd_sel = jnp.where(jnp.any(chosen, axis=2),
                        jnp.sum(jnp.where(chosen, jnp.arange(rows, dtype=jnp.int32), 0), axis=2), rows)
    fwd_pid = jnp.where(fwd_sel < rows,
                        jnp.take_along_axis(recv_pid, jnp.minimum(fwd_sel, rows - 1), axis=1), -1)
    recv_padded = jnp.concatenate([received, jnp.zeros((1, extent, extent), patches.dtype)], axis=0)
    my_fwd = lax.dynamic_index_in_dim(fwd_sel, my_index, 0, keepdims=False)
    forwarded = lax.ppermute(jnp.take(recv_padded, my_fwd, axis=0), "patch", xor_pairs(sources, 1))
    cand_pid = jnp.concatenate([
        my_index * number + jnp.arange(number, dtype=jnp.int32),
        lax.dynamic_index_in_dim(send_pid, partner, 0, keepdims=False)[0],
        lax.dynamic_index_in_dim(recv_pid, my_index, 0, keepdims=False),
        lax.dynamic_index_in_dim(fwd_pid, partner, 0, keepdims=False)])
    flat_owner = row_owner.reshape(-1)
    hits = (flat_owner == my_index).astype(jnp.int32)
    rank_in = jnp.cumsum(hits) - hits
    slot_ids = jnp.arange(CAP, dtype=jnp.int32)
    wanted = (hits[None, :] == 1) & (rank_in[None, :] == slot_ids[:, None])
    patch_ids = jnp.arange(sources * number, dtype=jnp.int32)
    slot_pid = jnp.sum(jnp.where(wanted, patch_ids[None, :], 0), axis=1)
    present = jnp.any(wanted, axis=1)
    cand_ids = jnp.arange(cand_pid.shape[0], dtype=jnp.int32)
    found = cand_pid[None, :] == slot_pid[:, None]
    take_idx = jnp.sum(jnp.where(found, cand_ids[None, :], 0), axis=1)
    take_idx = jnp.where(present, take_idx, cand_pid.shape[0])
    pieces = (patches, direct, received, forwarded)
    return take_idx, pieces, jnp.where(present, slot_pid, sources * number), outgoing


def spectra_kernel(rows, take_ref, own_ref, direct_ref, recv_ref, fwd_ref, scale_ref, half_ref,
                   full_ref, re_ref, im_ref):
    number = own_ref.shape[0]
    extent = own_ref.shape[-1]
    half_table = half_ref[...]
    full_table = full_ref[...]
    for s in range(re_ref.shape[0]):
        idx = take_ref[s]
        pick_own = own_ref[jnp.clip(idx, 0, number - 1)]
        pick_direct = direct_ref[jnp.clip(idx - number, 0, number - 1)]
        pick_recv = recv_ref[jnp.clip(idx - 2 * number, 0, rows - 1)]
        pick_fwd = fwd_ref[jnp.clip(idx - 2 * number - rows, 0, fwd_ref.shape[0] - 1)]
        zero = jnp.zeros_like(pick_own)
        image = jnp.where(
            idx < number, pick_own,
            jnp.where(idx < 2 * number, pick_direct,
                      jnp.where(idx < 2 * number + rows, pick_recv,
                                jnp.where(idx < 2 * number + rows + fwd_ref.shape[0], pick_fwd,
                                          zero))))
        half = jnp.dot(image, half_table, preferred_element_type=jnp.float32).astype(jnp.bfloat16)
        half_stack = jnp.concatenate([half[:, :extent], half[:, extent:]], axis=0)
        spec = jnp.dot(full_table, half_stack, preferred_element_type=jnp.float32)
        scale = scale_ref[s]
        re_ref[s] = (spec[:extent] * scale).astype(jnp.bfloat16)
        im_ref[s] = (spec[extent:] * scale).astype(jnp.bfloat16)


def make_spectra(take_idx, own, direct, received, forwarded, scale, half_table, full_table):
    count, extent = (scale.shape[0], scale.shape[-1])
    rows = received.shape[0]
    whole = pl.BlockSpec(memory_space=pltpu.VMEM)
    spec_shape = jax.ShapeDtypeStruct((count, extent, extent), jnp.bfloat16)
    return pl.pallas_call(
        functools.partial(spectra_kernel, rows),
        in_specs=[pl.BlockSpec(memory_space=pltpu.SMEM)] + [whole] * 7,
        out_specs=[whole, whole],
        out_shape=[spec_shape, spec_shape],
        cost_estimate=pl.CostEstimate(
            flops=3 * count * 6 * extent * extent * extent, transcendentals=0,
            bytes_accessed=count * 10 * extent * extent),
    )(take_idx, own, direct, received, forwarded, scale, half_table, full_table)


def corr_kernel(first, last, counts, orient_total, *refs):
    groups = len(counts)
    orient_ref, sr_ref, si_ref = refs[:3]
    templ_refs = refs[3:3 + groups]
    fw_ref, inv_ref = refs[3 + groups:5 + groups]
    rest = refs[5 + groups:]
    if first:
        top_ref, sum_ref, sq_ref, peak_ref = rest
    else:
        top_in, sum_in, sq_in, peak_in, top_ref, sum_ref, sq_ref, peak_ref = rest
    extent = sr_ref.shape[-1]
    sr = sr_ref[0].astype(jnp.float32)
    si = si_ref[0].astype(jnp.float32)
    forward = fw_ref[...]
    inverse = inv_ref[...]
    row_shape = (8, 128 * ((orient_total + 127) // 128))
    lanes = lax.broadcasted_iota(jnp.int32, row_shape, 1)
    peak_row = jnp.zeros(row_shape, jnp.float32) if first else peak_in[0]
    top = total = square = None
    prods = []
    for templ_ref, (count, parts) in zip(templ_refs, counts):
        for part in range(parts):
            for t in range(count):
                tr = templ_ref[2 * count * part + t].astype(jnp.float32)
                ti = templ_ref[2 * count * part + count + t].astype(jnp.float32)
                pre = (sr * tr + si * ti).astype(jnp.bfloat16)
                pim = (si * tr - sr * ti).astype(jnp.bfloat16)
                prods.append(jnp.concatenate([pre, pim], axis=1))
    q_all = jnp.dot(jnp.concatenate(prods, axis=0), forward,
                    preferred_element_type=jnp.float32).astype(jnp.bfloat16)
    for position in range(len(prods)):
        q = q_all[position * extent:(position + 1) * extent]
        q_stack = jnp.concatenate([q[:, :extent], q[:, extent:]], axis=0)
        corr = jnp.dot(inverse, q_stack, preferred_element_type=jnp.float32)
        peak_row = jnp.where(lanes == orient_ref[position], jnp.max(corr), peak_row)
        if top is None:
            top, total, square = corr, corr, corr * corr
        else:
            top = jnp.maximum(top, corr)
            total = total + corr
            square = square + corr * corr
    if not first:
        top = jnp.maximum(top_in[0], top)
        total = sum_in[0] + total
        square = sq_in[0] + square
    top_ref[0] = top
    if last:
        s = pl.program_id(0)
        peak_ref[pl.ds(s, 1), :] = peak_row[0:1, :orient_total]
    else:
        peak_ref[0] = peak_row
    if last:
        mean = total / orient_total
        sum_ref[0] = mean
        sq_ref[0] = square / orient_total - mean * mean
    else:
        sum_ref[0] = total
        sq_ref[0] = square


def correlate_chunk(spec_re, spec_im, templ_groups, template_counts, forward, inverse,
                    orient_chunk, orient_total, stats, last):
    count, extent = (spec_re.shape[0], spec_re.shape[-1])
    counts = tuple(template_counts)
    tiles = sum(count * parts for count, parts in counts)
    first = stats is None
    lanes = 128 * ((orient_total + 127) // 128)
    plane = pl.BlockSpec((1, extent, extent), lambda s: (s, 0, 0))
    peak_spec = pl.BlockSpec((1, 8, lanes), lambda s: (s, 0, 0))
    templ_specs = [pl.BlockSpec(group.shape, lambda s: (0, 0, 0)) for group in templ_groups]
    fw_spec = pl.BlockSpec(forward.shape, lambda s: (0, 0))
    inv_spec = pl.BlockSpec(inverse.shape, lambda s: (0, 0))
    in_specs = [pl.BlockSpec(memory_space=pltpu.SMEM), plane, plane] + templ_specs + [
        fw_spec, inv_spec]
    operands = [orient_chunk, spec_re, spec_im] + list(templ_groups) + [forward, inverse]
    aliases = {}
    if not first:
        base = len(operands)
        in_specs += [plane, plane, plane, peak_spec]
        operands += list(stats)
        aliases = {base: 0, base + 1: 1, base + 2: 2}
        if not last:
            aliases[base + 3] = 3
    map_shape = jax.ShapeDtypeStruct((count, extent, extent), jnp.float32)
    flops = 3 * tiles * count * 12 * extent * extent * extent
    return pl.pallas_call(
        functools.partial(corr_kernel, first, last, counts, orient_total),
        grid=(count,),
        in_specs=in_specs,
        out_specs=[plane, plane, plane,
                   pl.BlockSpec((count, orient_total), lambda s: (0, 0)) if last else peak_spec],
        out_shape=[map_shape, map_shape, map_shape,
                   jax.ShapeDtypeStruct((count, orient_total) if last else (count, 8, lanes),
                                        jnp.float32)],
        input_output_aliases=aliases,
        compiler_params=pltpu.CompilerParams(dimension_semantics=("arbitrary",)),
        cost_estimate=pl.CostEstimate(
            flops=flops, transcendentals=0,
            bytes_accessed=tiles * 4 * extent * extent * 2 + count * 10 * extent * extent * 4),
    )(*operands)


def correlate_all(spec_re, spec_im, templ_re, templ_im, orientation, forward, inverse):
    blocks = lax.axis_size("blk")
    me = lax.axis_index("blk")
    sources = lax.axis_size("patch")
    core = lax.axis_index("patch") % 2
    tiles = templ_re.shape[0]
    half = tiles // 2
    orient_total = orientation.shape[0]
    local = jnp.concatenate([templ_re, templ_im], axis=0)
    mine = jnp.concatenate(
        [lax.dynamic_slice_in_dim(templ_re, core * half, half, 0),
         lax.dynamic_slice_in_dim(templ_im, core * half, half, 0)], axis=0)
    within = jnp.arange(half, dtype=jnp.int32)
    first_groups = [(local, 1)]
    first_index = [me * tiles + jnp.arange(tiles, dtype=jnp.int32)]
    late_got, late_index = [], []
    for k in range(1, blocks):
        source = me ^ k
        got = lax.ppermute(mine, "blk", [(b, b ^ k) for b in range(blocks)])
        first_groups.append((got, 1))
        first_index.append(source * tiles + core * half + within)
        late_got.append(got)
        late_index.append(source * tiles + (1 - core) * half + within)
    chunks = [(first_groups, jnp.concatenate(first_index))]
    if late_got:
        passed = lax.ppermute(jnp.concatenate(late_got, axis=0), "patch", xor_pairs(sources, 1))
        chunks.append(([(passed, len(late_got))], jnp.concatenate(late_index)))
    stats = None
    for n, (groups, index) in enumerate(chunks):
        orient_chunk = jnp.take(orientation, index)
        counts = [(group.shape[0] // (2 * parts), parts) for group, parts in groups]
        stats = correlate_chunk(spec_re, spec_im, [group for group, parts in groups], counts,
                                forward, inverse, orient_chunk, orient_total, stats,
                                n == len(chunks) - 1)
    top_map, mean_map, var_map, peak = stats
    return (top_map, mean_map, var_map, peak)


def body(patches, owner_of_patch, group_of_patch, defocus, templ_re, templ_im, orientation):
    sources = lax.axis_size("patch")
    my_index = lax.axis_index("patch")
    number, extent = (patches.shape[0], patches.shape[1])
    forward, half_table, inverse = (jnp.asarray(table) for table in dft_tables(extent))
    row_owner = owner_of_patch.reshape(sources, number)
    take_idx, pieces, slot_row, outgoing = route_patches(patches, row_owner, my_index)
    templ_re, templ_im, unused = lax.optimization_barrier((templ_re, templ_im, outgoing))
    groups = jnp.take(jnp.concatenate([group_of_patch, jnp.zeros((1,), jnp.int32)]), slot_row)
    focus_values = jnp.take(defocus, groups)
    scale = ctf_scale(focus_values, extent)
    spec_re, spec_im = make_spectra(take_idx, *pieces, scale, half_table, forward)
    return correlate_all(spec_re, spec_im, templ_re, templ_im, orientation, forward, inverse)


def solution(mesh):
    placed = (
        P(("blk", "patch"), None, None),
        P("blk"),
        P("blk"),
        P(),
        P("blk", None, None),
        P("blk", None, None),
        P(),
    )
    return jax.shard_map(
        body,
        mesh=mesh,
        in_specs=placed,
        out_specs=(
            P(("blk", "patch"), None, None),
            P(("blk", "patch"), None, None),
            P(("blk", "patch"), None, None),
            P(("blk", "patch"), None),
        ),
        check_vma=False,
    )
```

```python
import functools
import math

import jax
import ml_dtypes
import numpy as np
import jax.numpy as jnp
from jax import lax
from jax.experimental import pallas as pl
from jax.experimental.pallas import tpu as pltpu
from jax.sharding import PartitionSpec as P

SLOT = 2
CAP = 4
TILE_T = 4


AMPLITUDE = 0.07


def dft_tables(extent):
    indices = np.arange(extent, dtype=np.int64)
    turn_count = indices[:, None] * indices[None, :] % extent
    angles = turn_count.astype(np.float32) * np.float32(2.0 * math.pi / extent)
    cosine = np.cos(angles).astype(ml_dtypes.bfloat16)
    sine = np.sin(angles).astype(ml_dtypes.bfloat16)
    forward = np.concatenate(
        [np.concatenate([cosine, sine], axis=1), np.concatenate([-sine, cosine], axis=1)], axis=0
    )
    half_table = np.concatenate([cosine, -sine], axis=1)
    inverse = (half_table.astype(np.float32) / extent).astype(ml_dtypes.bfloat16)
    return forward, half_table, inverse


def ctf_filter(defocus_values, extent):
    indices = jnp.arange(extent, dtype=jnp.int32)
    signed = (
        jnp.where(indices < extent // 2, indices, indices - extent).astype(jnp.float32) / extent
    )
    radius = signed[:, None] * signed[:, None] + signed[None, :] * signed[None, :]
    phases = math.pi * defocus_values[:, None, None] * radius[None, :, :] - AMPLITUDE
    return -jnp.sin(phases)


def ctf_scale(defocus_values, extent):
    indices = jnp.arange(extent, dtype=jnp.int32)
    signed = (
        jnp.where(indices < extent // 2, indices, indices - extent).astype(jnp.float32) / extent
    )
    square = signed * signed
    turn = math.pi * defocus_values[:, None]
    row_phase = turn * square[None, :] - AMPLITUDE
    col_phase = turn * square[None, :]
    row_sin, row_cos = jnp.sin(row_phase), jnp.cos(row_phase)
    col_sin, col_cos = jnp.sin(col_phase), jnp.cos(col_phase)
    ctf = -(row_sin[:, :, None] * col_cos[:, None, :] + row_cos[:, :, None] * col_sin[:, None, :])
    return ctf / extent


def xor_pairs(count, shift):
    return [(d, d ^ shift) for d in range(count)]


def route_patches(patches, row_owner, my_index):
    sources, number = row_owner.shape
    extent = patches.shape[-1]
    chips = sources // 2
    devs = jnp.arange(sources, dtype=jnp.int32)
    chip_of = devs // 2
    owner_chip = row_owner // 2
    masks = [row_owner == (devs ^ 1)[:, None]]
    for m in range(1, chips):
        masks.append(owner_chip == (chip_of ^ m)[:, None])
    match = jnp.stack(masks, axis=1)
    first = jnp.where(match[..., 0], 0, jnp.where(match[..., 1], 1, number))
    second = jnp.where(match[..., 0] & match[..., 1], 1, number)
    send_sel = jnp.stack([first, second], axis=-1)
    send_pid = jnp.where(send_sel < number, devs[:, None, None] * number + send_sel, -1)
    padded = jnp.concatenate([patches, jnp.zeros((1, extent, extent), patches.dtype)], axis=0)
    my_sel = lax.dynamic_index_in_dim(send_sel, my_index, 0, keepdims=False)
    outgoing = jnp.take(padded, my_sel.reshape(-1), axis=0).reshape(chips, 2, extent, extent)
    partner = my_index ^ 1
    my_chip = my_index // 2
    received = []
    for m in range(1, chips):
        received.append(lax.ppermute(outgoing[m], "patch", xor_pairs(sources, 2 * m)))
    received = jnp.concatenate(received, axis=0)
    forwarded = lax.ppermute(jnp.concatenate([outgoing[0], received], axis=0), "patch",
                             xor_pairs(sources, 1))
    cand_pid = [my_index * number + jnp.arange(number, dtype=jnp.int32)]
    for which, core in enumerate((my_index % 2, partner % 2)):
        if which == 1:
            cand_pid.append(lax.dynamic_index_in_dim(send_pid, partner, 0, keepdims=False)[0])
        for m in range(1, chips):
            source = (my_chip ^ m) * 2 + core
            cand_pid.append(lax.dynamic_index_in_dim(send_pid, source, 0, keepdims=False)[m])
    cand_pid = jnp.concatenate(cand_pid)
    flat_owner = row_owner.reshape(-1)
    hits = (flat_owner == my_index).astype(jnp.int32)
    rank_in = jnp.cumsum(hits) - hits
    slot_ids = jnp.arange(CAP, dtype=jnp.int32)
    wanted = (hits[None, :] == 1) & (rank_in[None, :] == slot_ids[:, None])
    patch_ids = jnp.arange(sources * number, dtype=jnp.int32)
    slot_pid = jnp.sum(jnp.where(wanted, patch_ids[None, :], 0), axis=1)
    present = jnp.any(wanted, axis=1)
    cand_ids = jnp.arange(cand_pid.shape[0], dtype=jnp.int32)
    found = cand_pid[None, :] == slot_pid[:, None]
    take_idx = jnp.sum(jnp.where(found, cand_ids[None, :], 0), axis=1)
    take_idx = jnp.where(present, take_idx, cand_pid.shape[0])
    pieces = (patches, received, forwarded)
    return take_idx, pieces, jnp.where(present, slot_pid, sources * number), outgoing


def spectra_kernel(count_pieces, take_ref, *refs):
    piece_refs = refs[:count_pieces]
    scale_ref, half_ref, full_ref, re_ref, im_ref = refs[count_pieces:]
    extent = piece_refs[0].shape[-1]
    half_table = half_ref[...]
    full_table = full_ref[...]
    for s in range(re_ref.shape[0]):
        idx = take_ref[s]
        image = jnp.zeros((extent, extent), piece_refs[0].dtype)
        base = 0
        bounds = []
        for piece in piece_refs:
            bounds.append((piece, base, piece.shape[0]))
            base += piece.shape[0]
        for piece, start, size in reversed(bounds):
            picked = piece[jnp.clip(idx - start, 0, size - 1)]
            image = jnp.where((idx >= start) & (idx < start + size), picked, image)
        half = jnp.dot(image, half_table, preferred_element_type=jnp.float32).astype(jnp.bfloat16)
        half_stack = jnp.concatenate([half[:, :extent], half[:, extent:]], axis=0)
        spec = jnp.dot(full_table, half_stack, preferred_element_type=jnp.float32)
        scale = scale_ref[s]
        re_ref[s] = (spec[:extent] * scale).astype(jnp.bfloat16)
        im_ref[s] = (spec[extent:] * scale).astype(jnp.bfloat16)


def make_spectra(take_idx, pieces, scale, half_table, full_table):
    count, extent = (scale.shape[0], scale.shape[-1])
    whole = pl.BlockSpec(memory_space=pltpu.VMEM)
    spec_shape = jax.ShapeDtypeStruct((count, extent, extent), jnp.bfloat16)
    return pl.pallas_call(
        functools.partial(spectra_kernel, len(pieces)),
        in_specs=[pl.BlockSpec(memory_space=pltpu.SMEM)] + [whole] * (len(pieces) + 3),
        out_specs=[whole, whole],
        out_shape=[spec_shape, spec_shape],
        cost_estimate=pl.CostEstimate(
            flops=3 * count * 6 * extent * extent * extent, transcendentals=0,
            bytes_accessed=count * 10 * extent * extent),
    )(take_idx, *pieces, scale, half_table, full_table)


def corr_kernel(first, last, counts, orient_total, *refs):
    groups = len(counts)
    orient_ref, sr_ref, si_ref = refs[:3]
    templ_refs = refs[3:3 + groups]
    fw_ref, inv_ref = refs[3 + groups:5 + groups]
    rest = refs[5 + groups:]
    if first:
        top_ref, sum_ref, sq_ref, peak_ref = rest
    else:
        top_in, sum_in, sq_in, peak_in, top_ref, sum_ref, sq_ref, peak_ref = rest
    extent = sr_ref.shape[-1]
    sr = sr_ref[0].astype(jnp.float32)
    si = si_ref[0].astype(jnp.float32)
    forward = fw_ref[...]
    inverse = inv_ref[...]
    row_shape = (8, 128 * ((orient_total + 127) // 128))
    lanes = lax.broadcasted_iota(jnp.int32, row_shape, 1)
    peak_row = jnp.zeros(row_shape, jnp.float32) if first else peak_in[0]
    top = total = square = None
    prods = []
    for templ_ref, (count, parts) in zip(templ_refs, counts):
        for part in range(parts):
            for t in range(count):
                tr = templ_ref[2 * count * part + t].astype(jnp.float32)
                ti = templ_ref[2 * count * part + count + t].astype(jnp.float32)
                pre = (sr * tr + si * ti).astype(jnp.bfloat16)
                pim = (si * tr - sr * ti).astype(jnp.bfloat16)
                prods.append(jnp.concatenate([pre, pim], axis=1))
    q_all = jnp.dot(jnp.concatenate(prods, axis=0), forward,
                    preferred_element_type=jnp.float32).astype(jnp.bfloat16)
    for position in range(len(prods)):
        q = q_all[position * extent:(position + 1) * extent]
        q_stack = jnp.concatenate([q[:, :extent], q[:, extent:]], axis=0)
        corr = jnp.dot(inverse, q_stack, preferred_element_type=jnp.float32)
        peak_row = jnp.where(lanes == orient_ref[position], jnp.max(corr), peak_row)
        if top is None:
            top, total, square = corr, corr, corr * corr
        else:
            top = jnp.maximum(top, corr)
            total = total + corr
            square = square + corr * corr
    if not first:
        top = jnp.maximum(top_in[0], top)
        total = sum_in[0] + total
        square = sq_in[0] + square
    top_ref[0] = top
    if last:
        s = pl.program_id(0)
        peak_ref[pl.ds(s, 1), :] = peak_row[0:1, :orient_total]
    else:
        peak_ref[0] = peak_row
    if last:
        mean = total / orient_total
        sum_ref[0] = mean
        sq_ref[0] = square / orient_total - mean * mean
    else:
        sum_ref[0] = total
        sq_ref[0] = square


def correlate_chunk(spec_re, spec_im, templ_groups, template_counts, forward, inverse,
                    orient_chunk, orient_total, stats, last):
    count, extent = (spec_re.shape[0], spec_re.shape[-1])
    counts = tuple(template_counts)
    tiles = sum(count * parts for count, parts in counts)
    first = stats is None
    lanes = 128 * ((orient_total + 127) // 128)
    plane = pl.BlockSpec((1, extent, extent), lambda s: (s, 0, 0))
    peak_spec = pl.BlockSpec((1, 8, lanes), lambda s: (s, 0, 0))
    templ_specs = [pl.BlockSpec(group.shape, lambda s: (0, 0, 0)) for group in templ_groups]
    fw_spec = pl.BlockSpec(forward.shape, lambda s: (0, 0))
    inv_spec = pl.BlockSpec(inverse.shape, lambda s: (0, 0))
    in_specs = [pl.BlockSpec(memory_space=pltpu.SMEM), plane, plane] + templ_specs + [
        fw_spec, inv_spec]
    operands = [orient_chunk, spec_re, spec_im] + list(templ_groups) + [forward, inverse]
    aliases = {}
    if not first:
        base = len(operands)
        in_specs += [plane, plane, plane, peak_spec]
        operands += list(stats)
        aliases = {base: 0, base + 1: 1, base + 2: 2}
        if not last:
            aliases[base + 3] = 3
    map_shape = jax.ShapeDtypeStruct((count, extent, extent), jnp.float32)
    flops = 3 * tiles * count * 12 * extent * extent * extent
    return pl.pallas_call(
        functools.partial(corr_kernel, first, last, counts, orient_total),
        grid=(count,),
        in_specs=in_specs,
        out_specs=[plane, plane, plane,
                   pl.BlockSpec((count, orient_total), lambda s: (0, 0)) if last else peak_spec],
        out_shape=[map_shape, map_shape, map_shape,
                   jax.ShapeDtypeStruct((count, orient_total) if last else (count, 8, lanes),
                                        jnp.float32)],
        input_output_aliases=aliases,
        compiler_params=pltpu.CompilerParams(dimension_semantics=("arbitrary",)),
        cost_estimate=pl.CostEstimate(
            flops=flops, transcendentals=0,
            bytes_accessed=tiles * 4 * extent * extent * 2 + count * 10 * extent * extent * 4),
    )(*operands)


def correlate_all(spec_re, spec_im, templ_re, templ_im, orientation, forward, inverse):
    blocks = lax.axis_size("blk")
    me = lax.axis_index("blk")
    sources = lax.axis_size("patch")
    core = lax.axis_index("patch") % 2
    tiles = templ_re.shape[0]
    half = tiles // 2
    orient_total = orientation.shape[0]
    local = jnp.concatenate([templ_re, templ_im], axis=0)
    mine = jnp.concatenate(
        [lax.dynamic_slice_in_dim(templ_re, core * half, half, 0),
         lax.dynamic_slice_in_dim(templ_im, core * half, half, 0)], axis=0)
    within = jnp.arange(half, dtype=jnp.int32)
    first_groups = [(local, 1)]
    first_index = [me * tiles + jnp.arange(tiles, dtype=jnp.int32)]
    late_got, late_index = [], []
    for k in range(1, blocks):
        source = me ^ k
        got = lax.ppermute(mine, "blk", [(b, b ^ k) for b in range(blocks)])
        first_groups.append((got, 1))
        first_index.append(source * tiles + core * half + within)
        late_got.append(got)
        late_index.append(source * tiles + (1 - core) * half + within)
    chunks = [(first_groups, jnp.concatenate(first_index))]
    if late_got:
        passed = lax.ppermute(jnp.concatenate(late_got, axis=0), "patch", xor_pairs(sources, 1))
        chunks.append(([(passed, len(late_got))], jnp.concatenate(late_index)))
    stats = None
    for n, (groups, index) in enumerate(chunks):
        orient_chunk = jnp.take(orientation, index)
        counts = [(group.shape[0] // (2 * parts), parts) for group, parts in groups]
        stats = correlate_chunk(spec_re, spec_im, [group for group, parts in groups], counts,
                                forward, inverse, orient_chunk, orient_total, stats,
                                n == len(chunks) - 1)
    top_map, mean_map, var_map, peak = stats
    return (top_map, mean_map, var_map, peak)


def body(patches, owner_of_patch, group_of_patch, defocus, templ_re, templ_im, orientation):
    sources = lax.axis_size("patch")
    my_index = lax.axis_index("patch")
    number, extent = (patches.shape[0], patches.shape[1])
    forward, half_table, inverse = (jnp.asarray(table) for table in dft_tables(extent))
    row_owner = owner_of_patch.reshape(sources, number)
    take_idx, pieces, slot_row, outgoing = route_patches(patches, row_owner, my_index)
    templ_re, templ_im, unused = lax.optimization_barrier((templ_re, templ_im, outgoing))
    groups = jnp.take(jnp.concatenate([group_of_patch, jnp.zeros((1,), jnp.int32)]), slot_row)
    focus_values = jnp.take(defocus, groups)
    scale = ctf_scale(focus_values, extent)
    spec_re, spec_im = make_spectra(take_idx, pieces, scale, half_table, forward)
    return correlate_all(spec_re, spec_im, templ_re, templ_im, orientation, forward, inverse)


def solution(mesh):
    placed = (
        P(("blk", "patch"), None, None),
        P("blk"),
        P("blk"),
        P(),
        P("blk", None, None),
        P("blk", None, None),
        P(),
    )
    return jax.shard_map(
        body,
        mesh=mesh,
        in_specs=placed,
        out_specs=(
            P(("blk", "patch"), None, None),
            P(("blk", "patch"), None, None),
            P(("blk", "patch"), None, None),
            P(("blk", "patch"), None),
        ),
        check_vma=False,
    )
```

```python
import functools
import math

import jax
import ml_dtypes
import numpy as np
import jax.numpy as jnp
from jax import lax
from jax.experimental import pallas as pl
from jax.experimental.pallas import tpu as pltpu
from jax.sharding import PartitionSpec as P

SLOT = 2
CAP = 4
TILE_T = 4


AMPLITUDE = 0.07


def dft_tables(extent):
    indices = np.arange(extent, dtype=np.int64)
    turn_count = indices[:, None] * indices[None, :] % extent
    angles = turn_count.astype(np.float32) * np.float32(2.0 * math.pi / extent)
    cosine = np.cos(angles).astype(ml_dtypes.bfloat16)
    sine = np.sin(angles).astype(ml_dtypes.bfloat16)
    forward = np.concatenate(
        [np.concatenate([cosine, sine], axis=1), np.concatenate([-sine, cosine], axis=1)], axis=0
    )
    half_table = np.concatenate([cosine, -sine], axis=1)
    inverse = (half_table.astype(np.float32) / extent).astype(ml_dtypes.bfloat16)
    return forward, half_table, inverse


def ctf_filter(defocus_values, extent):
    indices = jnp.arange(extent, dtype=jnp.int32)
    signed = (
        jnp.where(indices < extent // 2, indices, indices - extent).astype(jnp.float32) / extent
    )
    radius = signed[:, None] * signed[:, None] + signed[None, :] * signed[None, :]
    phases = math.pi * defocus_values[:, None, None] * radius[None, :, :] - AMPLITUDE
    return -jnp.sin(phases)


def ctf_scale(defocus_values, extent):
    indices = jnp.arange(extent, dtype=jnp.int32)
    signed = (
        jnp.where(indices < extent // 2, indices, indices - extent).astype(jnp.float32) / extent
    )
    square = signed * signed
    turn = math.pi * defocus_values[:, None]
    row_phase = turn * square[None, :] - AMPLITUDE
    col_phase = turn * square[None, :]
    row_sin, row_cos = jnp.sin(row_phase), jnp.cos(row_phase)
    col_sin, col_cos = jnp.sin(col_phase), jnp.cos(col_phase)
    ctf = -(row_sin[:, :, None] * col_cos[:, None, :] + row_cos[:, :, None] * col_sin[:, None, :])
    return ctf / extent


def xor_pairs(count, shift):
    return [(d, d ^ shift) for d in range(count)]


def route_patches(patches, row_owner, my_index, tied):
    sources, number = row_owner.shape
    extent = patches.shape[-1]
    chips = sources // 2
    devs = jnp.arange(sources, dtype=jnp.int32)
    chip_of = devs // 2
    owner_chip = row_owner // 2
    masks = [row_owner == (devs ^ 1)[:, None]]
    for m in range(1, chips):
        masks.append(owner_chip == (chip_of ^ m)[:, None])
    match = jnp.stack(masks, axis=1)
    first = jnp.where(match[..., 0], 0, jnp.where(match[..., 1], 1, number))
    second = jnp.where(match[..., 0] & match[..., 1], 1, number)
    send_sel = jnp.stack([first, second], axis=-1)
    send_pid = jnp.where(send_sel < number, devs[:, None, None] * number + send_sel, -1)
    padded = jnp.concatenate([patches, jnp.zeros((1, extent, extent), patches.dtype)], axis=0)
    my_sel = lax.dynamic_index_in_dim(send_sel, my_index, 0, keepdims=False)
    outgoing = jnp.take(padded, my_sel.reshape(-1), axis=0).reshape(chips, 2, extent, extent)
    outgoing, tied = lax.optimization_barrier((outgoing, tied))
    partner = my_index ^ 1
    my_chip = my_index // 2
    received = []
    for m in range(1, chips):
        received.append(lax.ppermute(outgoing[m], "patch", xor_pairs(sources, 2 * m)))
    received = jnp.concatenate(received, axis=0)
    forwarded = lax.ppermute(jnp.concatenate([outgoing[0], received], axis=0), "patch",
                             xor_pairs(sources, 1))
    cand_pid = [my_index * number + jnp.arange(number, dtype=jnp.int32)]
    for which, core in enumerate((my_index % 2, partner % 2)):
        if which == 1:
            cand_pid.append(lax.dynamic_index_in_dim(send_pid, partner, 0, keepdims=False)[0])
        for m in range(1, chips):
            source = (my_chip ^ m) * 2 + core
            cand_pid.append(lax.dynamic_index_in_dim(send_pid, source, 0, keepdims=False)[m])
    cand_pid = jnp.concatenate(cand_pid)
    flat_owner = row_owner.reshape(-1)
    hits = (flat_owner == my_index).astype(jnp.int32)
    rank_in = jnp.cumsum(hits) - hits
    slot_ids = jnp.arange(CAP, dtype=jnp.int32)
    wanted = (hits[None, :] == 1) & (rank_in[None, :] == slot_ids[:, None])
    patch_ids = jnp.arange(sources * number, dtype=jnp.int32)
    slot_pid = jnp.sum(jnp.where(wanted, patch_ids[None, :], 0), axis=1)
    present = jnp.any(wanted, axis=1)
    cand_ids = jnp.arange(cand_pid.shape[0], dtype=jnp.int32)
    found = cand_pid[None, :] == slot_pid[:, None]
    take_idx = jnp.sum(jnp.where(found, cand_ids[None, :], 0), axis=1)
    take_idx = jnp.where(present, take_idx, cand_pid.shape[0])
    pieces = (patches, received, forwarded)
    return take_idx, pieces, jnp.where(present, slot_pid, sources * number), tied


def spectra_kernel(count_pieces, take_ref, *refs):
    piece_refs = refs[:count_pieces]
    scale_ref, half_ref, full_ref, re_ref, im_ref = refs[count_pieces:]
    extent = piece_refs[0].shape[-1]
    half_table = half_ref[...]
    full_table = full_ref[...]
    for s in range(re_ref.shape[0]):
        idx = take_ref[s]
        image = jnp.zeros((extent, extent), piece_refs[0].dtype)
        base = 0
        bounds = []
        for piece in piece_refs:
            bounds.append((piece, base, piece.shape[0]))
            base += piece.shape[0]
        for piece, start, size in reversed(bounds):
            picked = piece[jnp.clip(idx - start, 0, size - 1)]
            image = jnp.where((idx >= start) & (idx < start + size), picked, image)
        half = jnp.dot(image, half_table, preferred_element_type=jnp.float32).astype(jnp.bfloat16)
        half_stack = jnp.concatenate([half[:, :extent], half[:, extent:]], axis=0)
        spec = jnp.dot(full_table, half_stack, preferred_element_type=jnp.float32)
        scale = scale_ref[s]
        re_ref[s] = (spec[:extent] * scale).astype(jnp.bfloat16)
        im_ref[s] = (spec[extent:] * scale).astype(jnp.bfloat16)


def make_spectra(take_idx, pieces, scale, half_table, full_table):
    count, extent = (scale.shape[0], scale.shape[-1])
    whole = pl.BlockSpec(memory_space=pltpu.VMEM)
    spec_shape = jax.ShapeDtypeStruct((count, extent, extent), jnp.bfloat16)
    return pl.pallas_call(
        functools.partial(spectra_kernel, len(pieces)),
        in_specs=[pl.BlockSpec(memory_space=pltpu.SMEM)] + [whole] * (len(pieces) + 3),
        out_specs=[whole, whole],
        out_shape=[spec_shape, spec_shape],
        cost_estimate=pl.CostEstimate(
            flops=3 * count * 6 * extent * extent * extent, transcendentals=0,
            bytes_accessed=count * 10 * extent * extent),
    )(take_idx, *pieces, scale, half_table, full_table)


def corr_kernel(first, last, counts, orient_total, *refs):
    groups = len(counts)
    orient_ref, sr_ref, si_ref = refs[:3]
    templ_refs = refs[3:3 + groups]
    fw_ref, inv_ref = refs[3 + groups:5 + groups]
    rest = refs[5 + groups:]
    if first:
        top_ref, sum_ref, sq_ref, peak_ref = rest
    else:
        top_in, sum_in, sq_in, peak_in, top_ref, sum_ref, sq_ref, peak_ref = rest
    extent = sr_ref.shape[-1]
    sr = sr_ref[0].astype(jnp.float32)
    si = si_ref[0].astype(jnp.float32)
    forward = fw_ref[...]
    inverse = inv_ref[...]
    row_shape = (8, 128 * ((orient_total + 127) // 128))
    lanes = lax.broadcasted_iota(jnp.int32, row_shape, 1)
    peak_row = jnp.zeros(row_shape, jnp.float32) if first else peak_in[0]
    top = total = square = None
    prods = []
    for templ_ref, (count, parts) in zip(templ_refs, counts):
        for part in range(parts):
            for t in range(count):
                tr = templ_ref[2 * count * part + t].astype(jnp.float32)
                ti = templ_ref[2 * count * part + count + t].astype(jnp.float32)
                pre = (sr * tr + si * ti).astype(jnp.bfloat16)
                pim = (si * tr - sr * ti).astype(jnp.bfloat16)
                prods.append(jnp.concatenate([pre, pim], axis=1))
    q_all = jnp.dot(jnp.concatenate(prods, axis=0), forward,
                    preferred_element_type=jnp.float32).astype(jnp.bfloat16)
    for position in range(len(prods)):
        q = q_all[position * extent:(position + 1) * extent]
        q_stack = jnp.concatenate([q[:, :extent], q[:, extent:]], axis=0)
        corr = jnp.dot(inverse, q_stack, preferred_element_type=jnp.float32)
        peak_row = jnp.where(lanes == orient_ref[position], jnp.max(corr), peak_row)
        if top is None:
            top, total, square = corr, corr, corr * corr
        else:
            top = jnp.maximum(top, corr)
            total = total + corr
            square = square + corr * corr
    if not first:
        top = jnp.maximum(top_in[0], top)
        total = sum_in[0] + total
        square = sq_in[0] + square
    top_ref[0] = top
    if last:
        s = pl.program_id(0)
        peak_ref[pl.ds(s, 1), :] = peak_row[0:1, :orient_total]
    else:
        peak_ref[0] = peak_row
    if last:
        mean = total / orient_total
        sum_ref[0] = mean
        sq_ref[0] = square / orient_total - mean * mean
    else:
        sum_ref[0] = total
        sq_ref[0] = square


def correlate_chunk(spec_re, spec_im, templ_groups, template_counts, forward, inverse,
                    orient_chunk, orient_total, stats, last):
    count, extent = (spec_re.shape[0], spec_re.shape[-1])
    counts = tuple(template_counts)
    tiles = sum(count * parts for count, parts in counts)
    first = stats is None
    lanes = 128 * ((orient_total + 127) // 128)
    plane = pl.BlockSpec((1, extent, extent), lambda s: (s, 0, 0))
    peak_spec = pl.BlockSpec((1, 8, lanes), lambda s: (s, 0, 0))
    templ_specs = [pl.BlockSpec(group.shape, lambda s: (0, 0, 0)) for group in templ_groups]
    fw_spec = pl.BlockSpec(forward.shape, lambda s: (0, 0))
    inv_spec = pl.BlockSpec(inverse.shape, lambda s: (0, 0))
    in_specs = [pl.BlockSpec(memory_space=pltpu.SMEM), plane, plane] + templ_specs + [
        fw_spec, inv_spec]
    operands = [orient_chunk, spec_re, spec_im] + list(templ_groups) + [forward, inverse]
    aliases = {}
    if not first:
        base = len(operands)
        in_specs += [plane, plane, plane, peak_spec]
        operands += list(stats)
        aliases = {base: 0, base + 1: 1, base + 2: 2}
        if not last:
            aliases[base + 3] = 3
    map_shape = jax.ShapeDtypeStruct((count, extent, extent), jnp.float32)
    flops = 3 * tiles * count * 12 * extent * extent * extent
    return pl.pallas_call(
        functools.partial(corr_kernel, first, last, counts, orient_total),
        grid=(count,),
        in_specs=in_specs,
        out_specs=[plane, plane, plane,
                   pl.BlockSpec((count, orient_total), lambda s: (0, 0)) if last else peak_spec],
        out_shape=[map_shape, map_shape, map_shape,
                   jax.ShapeDtypeStruct((count, orient_total) if last else (count, 8, lanes),
                                        jnp.float32)],
        input_output_aliases=aliases,
        compiler_params=pltpu.CompilerParams(dimension_semantics=("arbitrary",)),
        cost_estimate=pl.CostEstimate(
            flops=flops, transcendentals=0,
            bytes_accessed=tiles * 4 * extent * extent * 2 + count * 10 * extent * extent * 4),
    )(*operands)


def correlate_all(spec_re, spec_im, templ_re, templ_im, orientation, forward, inverse):
    blocks = lax.axis_size("blk")
    me = lax.axis_index("blk")
    sources = lax.axis_size("patch")
    core = lax.axis_index("patch") % 2
    tiles = templ_re.shape[0]
    half = tiles // 2
    orient_total = orientation.shape[0]
    local = jnp.concatenate([templ_re, templ_im], axis=0)
    mine = jnp.concatenate(
        [lax.dynamic_slice_in_dim(templ_re, core * half, half, 0),
         lax.dynamic_slice_in_dim(templ_im, core * half, half, 0)], axis=0)
    within = jnp.arange(half, dtype=jnp.int32)
    first_groups = [(local, 1)]
    first_index = [me * tiles + jnp.arange(tiles, dtype=jnp.int32)]
    late_got, late_index = [], []
    for k in range(1, blocks):
        source = me ^ k
        got = lax.ppermute(mine, "blk", [(b, b ^ k) for b in range(blocks)])
        first_groups.append((got, 1))
        first_index.append(source * tiles + core * half + within)
        late_got.append(got)
        late_index.append(source * tiles + (1 - core) * half + within)
    chunks = [(first_groups, jnp.concatenate(first_index))]
    if late_got:
        passed = lax.ppermute(jnp.concatenate(late_got, axis=0), "patch", xor_pairs(sources, 1))
        chunks.append(([(passed, len(late_got))], jnp.concatenate(late_index)))
    stats = None
    for n, (groups, index) in enumerate(chunks):
        orient_chunk = jnp.take(orientation, index)
        counts = [(group.shape[0] // (2 * parts), parts) for group, parts in groups]
        stats = correlate_chunk(spec_re, spec_im, [group for group, parts in groups], counts,
                                forward, inverse, orient_chunk, orient_total, stats,
                                n == len(chunks) - 1)
    top_map, mean_map, var_map, peak = stats
    return (top_map, mean_map, var_map, peak)


def body(patches, owner_of_patch, group_of_patch, defocus, templ_re, templ_im, orientation):
    sources = lax.axis_size("patch")
    my_index = lax.axis_index("patch")
    number, extent = (patches.shape[0], patches.shape[1])
    forward, half_table, inverse = (jnp.asarray(table) for table in dft_tables(extent))
    row_owner = owner_of_patch.reshape(sources, number)
    take_idx, pieces, slot_row, (templ_re, templ_im) = route_patches(
        patches, row_owner, my_index, (templ_re, templ_im))
    groups = jnp.take(jnp.concatenate([group_of_patch, jnp.zeros((1,), jnp.int32)]), slot_row)
    focus_values = jnp.take(defocus, groups)
    scale = ctf_scale(focus_values, extent)
    spec_re, spec_im = make_spectra(take_idx, pieces, scale, half_table, forward)
    return correlate_all(spec_re, spec_im, templ_re, templ_im, orientation, forward, inverse)


def solution(mesh):
    placed = (
        P(("blk", "patch"), None, None),
        P("blk"),
        P("blk"),
        P(),
        P("blk", None, None),
        P("blk", None, None),
        P(),
    )
    return jax.shard_map(
        body,
        mesh=mesh,
        in_specs=placed,
        out_specs=(
            P(("blk", "patch"), None, None),
            P(("blk", "patch"), None, None),
            P(("blk", "patch"), None, None),
            P(("blk", "patch"), None),
        ),
        check_vma=False,
    )
```

```python
import functools
import math

import jax
import ml_dtypes
import numpy as np
import jax.numpy as jnp
from jax import lax
from jax.experimental import pallas as pl
from jax.experimental.pallas import tpu as pltpu
from jax.sharding import PartitionSpec as P

SLOT = 2
CAP = 4
TILE_T = 4


AMPLITUDE = 0.07


def dft_tables(extent):
    indices = np.arange(extent, dtype=np.int64)
    turn_count = indices[:, None] * indices[None, :] % extent
    angles = turn_count.astype(np.float32) * np.float32(2.0 * math.pi / extent)
    cosine = np.cos(angles).astype(ml_dtypes.bfloat16)
    sine = np.sin(angles).astype(ml_dtypes.bfloat16)
    forward = np.concatenate(
        [np.concatenate([cosine, sine], axis=1), np.concatenate([-sine, cosine], axis=1)], axis=0
    )
    half_table = np.concatenate([cosine, -sine], axis=1)
    inverse = (half_table.astype(np.float32) / extent).astype(ml_dtypes.bfloat16)
    return forward, half_table, inverse


def ctf_filter(defocus_values, extent):
    indices = jnp.arange(extent, dtype=jnp.int32)
    signed = (
        jnp.where(indices < extent // 2, indices, indices - extent).astype(jnp.float32) / extent
    )
    radius = signed[:, None] * signed[:, None] + signed[None, :] * signed[None, :]
    phases = math.pi * defocus_values[:, None, None] * radius[None, :, :] - AMPLITUDE
    return -jnp.sin(phases)


def ctf_scale(defocus_values, extent):
    indices = jnp.arange(extent, dtype=jnp.int32)
    signed = (
        jnp.where(indices < extent // 2, indices, indices - extent).astype(jnp.float32) / extent
    )
    square = signed * signed
    turn = math.pi * defocus_values[:, None]
    row_phase = turn * square[None, :] - AMPLITUDE
    col_phase = turn * square[None, :]
    row_sin, row_cos = jnp.sin(row_phase), jnp.cos(row_phase)
    col_sin, col_cos = jnp.sin(col_phase), jnp.cos(col_phase)
    ctf = -(row_sin[:, :, None] * col_cos[:, None, :] + row_cos[:, :, None] * col_sin[:, None, :])
    return ctf / extent


def xor_pairs(count, shift):
    return [(d, d ^ shift) for d in range(count)]


def route_patches(patches, row_owner, my_index):
    sources, number = row_owner.shape
    extent = patches.shape[-1]
    chips = sources // 2
    devs = jnp.arange(sources, dtype=jnp.int32)
    chip_of = devs // 2
    owner_chip = row_owner // 2
    masks = [row_owner == (devs ^ 1)[:, None]]
    for m in range(1, chips):
        masks.append(owner_chip == (chip_of ^ m)[:, None])
    match = jnp.stack(masks, axis=1)
    first = jnp.where(match[..., 0], 0, jnp.where(match[..., 1], 1, number))
    second = jnp.where(match[..., 0] & match[..., 1], 1, number)
    send_sel = jnp.stack([first, second], axis=-1)
    send_pid = jnp.where(send_sel < number, devs[:, None, None] * number + send_sel, -1)
    padded = jnp.concatenate([patches, jnp.zeros((1, extent, extent), patches.dtype)], axis=0)
    my_sel = lax.dynamic_index_in_dim(send_sel, my_index, 0, keepdims=False)
    outgoing = jnp.take(padded, my_sel.reshape(-1), axis=0).reshape(chips, 2, extent, extent)
    partner = my_index ^ 1
    my_chip = my_index // 2
    direct = lax.ppermute(outgoing[0], "patch", xor_pairs(sources, 1))
    received = []
    for m in range(1, chips):
        received.append(lax.ppermute(outgoing[m], "patch", xor_pairs(sources, 2 * m)))
    received = jnp.concatenate(received, axis=0)
    forwarded = lax.ppermute(received, "patch", xor_pairs(sources, 1))
    cand_pid = [my_index * number + jnp.arange(number, dtype=jnp.int32)]
    cand_pid.append(lax.dynamic_index_in_dim(send_pid, partner, 0, keepdims=False)[0])
    for core in (my_index % 2, partner % 2):
        for m in range(1, chips):
            source = (my_chip ^ m) * 2 + core
            cand_pid.append(lax.dynamic_index_in_dim(send_pid, source, 0, keepdims=False)[m])
    cand_pid = jnp.concatenate(cand_pid)
    flat_owner = row_owner.reshape(-1)
    hits = (flat_owner == my_index).astype(jnp.int32)
    rank_in = jnp.cumsum(hits) - hits
    slot_ids = jnp.arange(CAP, dtype=jnp.int32)
    wanted = (hits[None, :] == 1) & (rank_in[None, :] == slot_ids[:, None])
    patch_ids = jnp.arange(sources * number, dtype=jnp.int32)
    slot_pid = jnp.sum(jnp.where(wanted, patch_ids[None, :], 0), axis=1)
    present = jnp.any(wanted, axis=1)
    cand_ids = jnp.arange(cand_pid.shape[0], dtype=jnp.int32)
    found = cand_pid[None, :] == slot_pid[:, None]
    take_idx = jnp.sum(jnp.where(found, cand_ids[None, :], 0), axis=1)
    take_idx = jnp.where(present, take_idx, cand_pid.shape[0])
    pieces = (patches, direct, received, forwarded)
    return take_idx, pieces, jnp.where(present, slot_pid, sources * number), outgoing


def spectra_kernel(rows, take_ref, own_ref, direct_ref, recv_ref, fwd_ref, scale_ref, half_ref,
                   full_ref, re_ref, im_ref):
    number = own_ref.shape[0]
    extent = own_ref.shape[-1]
    half_table = half_ref[...]
    full_table = full_ref[...]
    step = re_ref.shape[0]
    for s in range(step):
        idx = take_ref[pl.program_id(0) * step + s]
        pick_own = own_ref[jnp.clip(idx, 0, number - 1)]
        pick_direct = direct_ref[jnp.clip(idx - number, 0, number - 1)]
        pick_recv = recv_ref[jnp.clip(idx - 2 * number, 0, rows - 1)]
        pick_fwd = fwd_ref[jnp.clip(idx - 2 * number - rows, 0, rows - 1)]
        zero = jnp.zeros_like(pick_own)
        image = jnp.where(
            idx < number, pick_own,
            jnp.where(idx < 2 * number, pick_direct,
                      jnp.where(idx < 2 * number + rows, pick_recv,
                                jnp.where(idx < 2 * number + 2 * rows, pick_fwd, zero))))
        half = jnp.dot(image, half_table, preferred_element_type=jnp.float32).astype(jnp.bfloat16)
        half_stack = jnp.concatenate([half[:, :extent], half[:, extent:]], axis=0)
        spec = jnp.dot(full_table, half_stack, preferred_element_type=jnp.float32)
        scale = scale_ref[s]
        re_ref[s] = (spec[:extent] * scale).astype(jnp.bfloat16)
        im_ref[s] = (spec[extent:] * scale).astype(jnp.bfloat16)


def make_spectra(take_idx, own, direct, received, forwarded, scale, half_table, full_table):
    count, extent = (scale.shape[0], scale.shape[-1])
    rows = received.shape[0]
    whole = pl.BlockSpec(memory_space=pltpu.VMEM)
    step = 2 if count % 2 == 0 else 1
    plane = pl.BlockSpec((step, extent, extent), lambda s: (s, 0, 0))
    spec_shape = jax.ShapeDtypeStruct((count, extent, extent), jnp.bfloat16)
    return pl.pallas_call(
        functools.partial(spectra_kernel, rows),
        grid=(count // step,),
        in_specs=[pl.BlockSpec(memory_space=pltpu.SMEM)] + [whole] * 4 + [plane] + [whole] * 2,
        out_specs=[plane, plane],
        out_shape=[spec_shape, spec_shape],
        cost_estimate=pl.CostEstimate(
            flops=3 * count * 6 * extent * extent * extent, transcendentals=0,
            bytes_accessed=count * 10 * extent * extent),
    )(take_idx, own, direct, received, forwarded, scale, half_table, full_table)


def corr_kernel(first, last, counts, orient_total, *refs):
    groups = len(counts)
    orient_ref, sr_ref, si_ref = refs[:3]
    templ_refs = refs[3:3 + groups]
    fw_ref, inv_ref = refs[3 + groups:5 + groups]
    rest = refs[5 + groups:]
    if first:
        top_ref, sum_ref, sq_ref, peak_ref = rest
    else:
        top_in, sum_in, sq_in, peak_in, top_ref, sum_ref, sq_ref, peak_ref = rest
    extent = sr_ref.shape[-1]
    sr = sr_ref[0].astype(jnp.float32)
    si = si_ref[0].astype(jnp.float32)
    forward = fw_ref[...]
    inverse = inv_ref[...]
    row_shape = (8, 128 * ((orient_total + 127) // 128))
    lanes = lax.broadcasted_iota(jnp.int32, row_shape, 1)
    peak_row = jnp.zeros(row_shape, jnp.float32) if first else peak_in[0]
    top = total = square = None
    prods = []
    for templ_ref, (count, parts) in zip(templ_refs, counts):
        for part in range(parts):
            for t in range(count):
                tr = templ_ref[2 * count * part + t].astype(jnp.float32)
                ti = templ_ref[2 * count * part + count + t].astype(jnp.float32)
                pre = (sr * tr + si * ti).astype(jnp.bfloat16)
                pim = (si * tr - sr * ti).astype(jnp.bfloat16)
                prods.append(jnp.concatenate([pre, pim], axis=1))
    q_all = jnp.dot(jnp.concatenate(prods, axis=0), forward,
                    preferred_element_type=jnp.float32).astype(jnp.bfloat16)
    for position in range(len(prods)):
        q = q_all[position * extent:(position + 1) * extent]
        q_stack = jnp.concatenate([q[:, :extent], q[:, extent:]], axis=0)
        corr = jnp.dot(inverse, q_stack, preferred_element_type=jnp.float32)
        peak_row = jnp.where(lanes == orient_ref[position], jnp.max(corr), peak_row)
        if top is None:
            top, total, square = corr, corr, corr * corr
        else:
            top = jnp.maximum(top, corr)
            total = total + corr
            square = square + corr * corr
    if not first:
        top = jnp.maximum(top_in[0], top)
        total = sum_in[0] + total
        square = sq_in[0] + square
    top_ref[0] = top
    if last:
        s = pl.program_id(0)
        peak_ref[pl.ds(s, 1), :] = peak_row[0:1, :orient_total]
    else:
        peak_ref[0] = peak_row
    if last:
        mean = total / orient_total
        sum_ref[0] = mean
        sq_ref[0] = square / orient_total - mean * mean
    else:
        sum_ref[0] = total
        sq_ref[0] = square


def correlate_chunk(spec_re, spec_im, templ_groups, template_counts, forward, inverse,
                    orient_chunk, orient_total, stats, last):
    count, extent = (spec_re.shape[0], spec_re.shape[-1])
    counts = tuple(template_counts)
    tiles = sum(count * parts for count, parts in counts)
    first = stats is None
    lanes = 128 * ((orient_total + 127) // 128)
    plane = pl.BlockSpec((1, extent, extent), lambda s: (s, 0, 0))
    peak_spec = pl.BlockSpec((1, 8, lanes), lambda s: (s, 0, 0))
    templ_specs = [pl.BlockSpec(group.shape, lambda s: (0, 0, 0)) for group in templ_groups]
    fw_spec = pl.BlockSpec(forward.shape, lambda s: (0, 0))
    inv_spec = pl.BlockSpec(inverse.shape, lambda s: (0, 0))
    in_specs = [pl.BlockSpec(memory_space=pltpu.SMEM), plane, plane] + templ_specs + [
        fw_spec, inv_spec]
    operands = [orient_chunk, spec_re, spec_im] + list(templ_groups) + [forward, inverse]
    aliases = {}
    if not first:
        base = len(operands)
        in_specs += [plane, plane, plane, peak_spec]
        operands += list(stats)
        aliases = {base: 0, base + 1: 1, base + 2: 2}
        if not last:
            aliases[base + 3] = 3
    map_shape = jax.ShapeDtypeStruct((count, extent, extent), jnp.float32)
    flops = 3 * tiles * count * 12 * extent * extent * extent
    return pl.pallas_call(
        functools.partial(corr_kernel, first, last, counts, orient_total),
        grid=(count,),
        in_specs=in_specs,
        out_specs=[plane, plane, plane,
                   pl.BlockSpec((count, orient_total), lambda s: (0, 0)) if last else peak_spec],
        out_shape=[map_shape, map_shape, map_shape,
                   jax.ShapeDtypeStruct((count, orient_total) if last else (count, 8, lanes),
                                        jnp.float32)],
        input_output_aliases=aliases,
        compiler_params=pltpu.CompilerParams(dimension_semantics=("arbitrary",)),
        cost_estimate=pl.CostEstimate(
            flops=flops, transcendentals=0,
            bytes_accessed=tiles * 4 * extent * extent * 2 + count * 10 * extent * extent * 4),
    )(*operands)


def correlate_all(spec_re, spec_im, templ_re, templ_im, orientation, forward, inverse):
    blocks = lax.axis_size("blk")
    me = lax.axis_index("blk")
    sources = lax.axis_size("patch")
    core = lax.axis_index("patch") % 2
    tiles = templ_re.shape[0]
    half = tiles // 2
    orient_total = orientation.shape[0]
    local = jnp.concatenate([templ_re, templ_im], axis=0)
    mine = jnp.concatenate(
        [lax.dynamic_slice_in_dim(templ_re, core * half, half, 0),
         lax.dynamic_slice_in_dim(templ_im, core * half, half, 0)], axis=0)
    within = jnp.arange(half, dtype=jnp.int32)
    first_groups = [(local, 1)]
    first_index = [me * tiles + jnp.arange(tiles, dtype=jnp.int32)]
    late_got, late_index = [], []
    for k in range(1, blocks):
        source = me ^ k
        got = lax.ppermute(mine, "blk", [(b, b ^ k) for b in range(blocks)])
        first_groups.append((got, 1))
        first_index.append(source * tiles + core * half + within)
        late_got.append(got)
        late_index.append(source * tiles + (1 - core) * half + within)
    chunks = [(first_groups, jnp.concatenate(first_index))]
    if late_got:
        passed = lax.ppermute(jnp.concatenate(late_got, axis=0), "patch", xor_pairs(sources, 1))
        chunks.append(([(passed, len(late_got))], jnp.concatenate(late_index)))
    stats = None
    for n, (groups, index) in enumerate(chunks):
        orient_chunk = jnp.take(orientation, index)
        counts = [(group.shape[0] // (2 * parts), parts) for group, parts in groups]
        stats = correlate_chunk(spec_re, spec_im, [group for group, parts in groups], counts,
                                forward, inverse, orient_chunk, orient_total, stats,
                                n == len(chunks) - 1)
    top_map, mean_map, var_map, peak = stats
    return (top_map, mean_map, var_map, peak)


def body(patches, owner_of_patch, group_of_patch, defocus, templ_re, templ_im, orientation):
    sources = lax.axis_size("patch")
    my_index = lax.axis_index("patch")
    number, extent = (patches.shape[0], patches.shape[1])
    forward, half_table, inverse = (jnp.asarray(table) for table in dft_tables(extent))
    row_owner = owner_of_patch.reshape(sources, number)
    take_idx, pieces, slot_row, outgoing = route_patches(patches, row_owner, my_index)
    templ_re, templ_im, unused = lax.optimization_barrier((templ_re, templ_im, outgoing))
    groups = jnp.take(jnp.concatenate([group_of_patch, jnp.zeros((1,), jnp.int32)]), slot_row)
    focus_values = jnp.take(defocus, groups)
    scale = ctf_scale(focus_values, extent)
    spec_re, spec_im = make_spectra(take_idx, *pieces, scale, half_table, forward)
    return correlate_all(spec_re, spec_im, templ_re, templ_im, orientation, forward, inverse)


def solution(mesh):
    placed = (
        P(("blk", "patch"), None, None),
        P("blk"),
        P("blk"),
        P(),
        P("blk", None, None),
        P("blk", None, None),
        P(),
    )
    return jax.shard_map(
        body,
        mesh=mesh,
        in_specs=placed,
        out_specs=(
            P(("blk", "patch"), None, None),
            P(("blk", "patch"), None, None),
            P(("blk", "patch"), None, None),
            P(("blk", "patch"), None),
        ),
        check_vma=False,
    )
```

```python
import functools
import math

import jax
import ml_dtypes
import numpy as np
import jax.numpy as jnp
from jax import lax
from jax.experimental import pallas as pl
from jax.experimental.pallas import tpu as pltpu
from jax.sharding import PartitionSpec as P

SLOT = 2
CAP = 4
TILE_T = 4


AMPLITUDE = 0.07


def dft_tables(extent):
    indices = np.arange(extent, dtype=np.int64)
    turn_count = indices[:, None] * indices[None, :] % extent
    angles = turn_count.astype(np.float32) * np.float32(2.0 * math.pi / extent)
    cosine = np.cos(angles).astype(ml_dtypes.bfloat16)
    sine = np.sin(angles).astype(ml_dtypes.bfloat16)
    forward = np.concatenate(
        [np.concatenate([cosine, sine], axis=1), np.concatenate([-sine, cosine], axis=1)], axis=0
    )
    half_table = np.concatenate([cosine, -sine], axis=1)
    inverse = (half_table.astype(np.float32) / extent).astype(ml_dtypes.bfloat16)
    return forward, half_table, inverse


def ctf_filter(defocus_values, extent):
    indices = jnp.arange(extent, dtype=jnp.int32)
    signed = (
        jnp.where(indices < extent // 2, indices, indices - extent).astype(jnp.float32) / extent
    )
    radius = signed[:, None] * signed[:, None] + signed[None, :] * signed[None, :]
    phases = math.pi * defocus_values[:, None, None] * radius[None, :, :] - AMPLITUDE
    return -jnp.sin(phases)


def ctf_scale(defocus_values, extent):
    indices = jnp.arange(extent, dtype=jnp.int32)
    signed = (
        jnp.where(indices < extent // 2, indices, indices - extent).astype(jnp.float32) / extent
    )
    square = signed * signed
    turn = math.pi * defocus_values[:, None]
    row_phase = turn * square[None, :] - AMPLITUDE
    col_phase = turn * square[None, :]
    row_sin, row_cos = jnp.sin(row_phase), jnp.cos(row_phase)
    col_sin, col_cos = jnp.sin(col_phase), jnp.cos(col_phase)
    ctf = -(row_sin[:, :, None] * col_cos[:, None, :] + row_cos[:, :, None] * col_sin[:, None, :])
    return ctf / extent


def xor_pairs(count, shift):
    return [(d, d ^ shift) for d in range(count)]


def route_patches(patches, row_owner, my_index):
    sources, number = row_owner.shape
    extent = patches.shape[-1]
    chips = sources // 2
    devs = jnp.arange(sources, dtype=jnp.int32)
    chip_of = devs // 2
    owner_chip = row_owner // 2
    masks = [row_owner == (devs ^ 1)[:, None]]
    for m in range(1, chips):
        masks.append(owner_chip == (chip_of ^ m)[:, None])
    match = jnp.stack(masks, axis=1)
    first = jnp.where(match[..., 0], 0, jnp.where(match[..., 1], 1, number))
    second = jnp.where(match[..., 0] & match[..., 1], 1, number)
    send_sel = jnp.stack([first, second], axis=-1)
    send_pid = jnp.where(send_sel < number, devs[:, None, None] * number + send_sel, -1)
    padded = jnp.concatenate([patches, jnp.zeros((1, extent, extent), patches.dtype)], axis=0)
    my_sel = lax.dynamic_index_in_dim(send_sel, my_index, 0, keepdims=False)
    outgoing = jnp.take(padded, my_sel.reshape(-1), axis=0).reshape(chips, 2, extent, extent)
    partner = my_index ^ 1
    my_chip = my_index // 2
    received = []
    for m in range(1, chips):
        received.append(lax.ppermute(outgoing[m], "patch", xor_pairs(sources, 2 * m)))
    received = jnp.concatenate(received, axis=0)
    forwarded = lax.ppermute(jnp.concatenate([outgoing[0], received], axis=0), "patch",
                             xor_pairs(sources, 1))
    cand_pid = [my_index * number + jnp.arange(number, dtype=jnp.int32)]
    for which, core in enumerate((my_index % 2, partner % 2)):
        if which == 1:
            cand_pid.append(lax.dynamic_index_in_dim(send_pid, partner, 0, keepdims=False)[0])
        for m in range(1, chips):
            source = (my_chip ^ m) * 2 + core
            cand_pid.append(lax.dynamic_index_in_dim(send_pid, source, 0, keepdims=False)[m])
    cand_pid = jnp.concatenate(cand_pid)
    flat_owner = row_owner.reshape(-1)
    hits = (flat_owner == my_index).astype(jnp.int32)
    rank_in = jnp.cumsum(hits) - hits
    slot_ids = jnp.arange(CAP, dtype=jnp.int32)
    wanted = (hits[None, :] == 1) & (rank_in[None, :] == slot_ids[:, None])
    patch_ids = jnp.arange(sources * number, dtype=jnp.int32)
    slot_pid = jnp.sum(jnp.where(wanted, patch_ids[None, :], 0), axis=1)
    present = jnp.any(wanted, axis=1)
    cand_ids = jnp.arange(cand_pid.shape[0], dtype=jnp.int32)
    found = cand_pid[None, :] == slot_pid[:, None]
    take_idx = jnp.sum(jnp.where(found, cand_ids[None, :], 0), axis=1)
    take_idx = jnp.where(present, take_idx, cand_pid.shape[0])
    pieces = (patches, received, forwarded)
    return take_idx, pieces, jnp.where(present, slot_pid, sources * number), outgoing


def spectra_kernel(count_pieces, take_ref, *refs):
    piece_refs = refs[:count_pieces]
    scale_ref, half_ref, full_ref, re_ref, im_ref = refs[count_pieces:]
    extent = piece_refs[0].shape[-1]
    half_table = half_ref[...]
    full_table = full_ref[...]
    step = re_ref.shape[0]
    for s in range(step):
        idx = take_ref[pl.program_id(0) * step + s]
        image = jnp.zeros((extent, extent), piece_refs[0].dtype)
        base = 0
        bounds = []
        for piece in piece_refs:
            bounds.append((piece, base, piece.shape[0]))
            base += piece.shape[0]
        for piece, start, size in reversed(bounds):
            picked = piece[jnp.clip(idx - start, 0, size - 1)]
            image = jnp.where((idx >= start) & (idx < start + size), picked, image)
        half = jnp.dot(image, half_table, preferred_element_type=jnp.float32).astype(jnp.bfloat16)
        half_stack = jnp.concatenate([half[:, :extent], half[:, extent:]], axis=0)
        spec = jnp.dot(full_table, half_stack, preferred_element_type=jnp.float32)
        scale = scale_ref[s]
        re_ref[s] = (spec[:extent] * scale).astype(jnp.bfloat16)
        im_ref[s] = (spec[extent:] * scale).astype(jnp.bfloat16)


def make_spectra(take_idx, pieces, scale, half_table, full_table):
    count, extent = (scale.shape[0], scale.shape[-1])
    whole = pl.BlockSpec(memory_space=pltpu.VMEM)
    step = 2 if count % 2 == 0 else 1
    plane = pl.BlockSpec((step, extent, extent), lambda s: (s, 0, 0))
    spec_shape = jax.ShapeDtypeStruct((count, extent, extent), jnp.bfloat16)
    return pl.pallas_call(
        functools.partial(spectra_kernel, len(pieces)),
        grid=(count // step,),
        in_specs=[pl.BlockSpec(memory_space=pltpu.SMEM)] + [whole] * len(pieces) + [plane]
        + [whole] * 2,
        out_specs=[plane, plane],
        out_shape=[spec_shape, spec_shape],
        cost_estimate=pl.CostEstimate(
            flops=3 * count * 6 * extent * extent * extent, transcendentals=0,
            bytes_accessed=count * 10 * extent * extent),
    )(take_idx, *pieces, scale, half_table, full_table)


def corr_kernel(first, last, counts, orient_total, *refs):
    groups = len(counts)
    orient_ref, sr_ref, si_ref = refs[:3]
    templ_refs = refs[3:3 + groups]
    fw_ref, inv_ref = refs[3 + groups:5 + groups]
    rest = refs[5 + groups:]
    if first:
        top_ref, sum_ref, sq_ref, peak_ref = rest
    else:
        top_in, sum_in, sq_in, peak_in, top_ref, sum_ref, sq_ref, peak_ref = rest
    extent = sr_ref.shape[-1]
    sr = sr_ref[0].astype(jnp.float32)
    si = si_ref[0].astype(jnp.float32)
    forward = fw_ref[...]
    inverse = inv_ref[...]
    row_shape = (8, 128 * ((orient_total + 127) // 128))
    lanes = lax.broadcasted_iota(jnp.int32, row_shape, 1)
    peak_row = jnp.zeros(row_shape, jnp.float32) if first else peak_in[0]
    top = total = square = None
    prods = []
    for templ_ref, (count, parts) in zip(templ_refs, counts):
        for part in range(parts):
            for t in range(count):
                tr = templ_ref[2 * count * part + t].astype(jnp.float32)
                ti = templ_ref[2 * count * part + count + t].astype(jnp.float32)
                pre = (sr * tr + si * ti).astype(jnp.bfloat16)
                pim = (si * tr - sr * ti).astype(jnp.bfloat16)
                prods.append(jnp.concatenate([pre, pim], axis=1))
    q_all = jnp.dot(jnp.concatenate(prods, axis=0), forward,
                    preferred_element_type=jnp.float32).astype(jnp.bfloat16)
    for position in range(len(prods)):
        q = q_all[position * extent:(position + 1) * extent]
        q_stack = jnp.concatenate([q[:, :extent], q[:, extent:]], axis=0)
        corr = jnp.dot(inverse, q_stack, preferred_element_type=jnp.float32)
        peak_row = jnp.where(lanes == orient_ref[position], jnp.max(corr), peak_row)
        if top is None:
            top, total, square = corr, corr, corr * corr
        else:
            top = jnp.maximum(top, corr)
            total = total + corr
            square = square + corr * corr
    if not first:
        top = jnp.maximum(top_in[0], top)
        total = sum_in[0] + total
        square = sq_in[0] + square
    top_ref[0] = top
    if last:
        s = pl.program_id(0)
        peak_ref[pl.ds(s, 1), :] = peak_row[0:1, :orient_total]
    else:
        peak_ref[0] = peak_row
    if last:
        mean = total / orient_total
        sum_ref[0] = mean
        sq_ref[0] = square / orient_total - mean * mean
    else:
        sum_ref[0] = total
        sq_ref[0] = square


def correlate_chunk(spec_re, spec_im, templ_groups, template_counts, forward, inverse,
                    orient_chunk, orient_total, stats, last):
    count, extent = (spec_re.shape[0], spec_re.shape[-1])
    counts = tuple(template_counts)
    tiles = sum(count * parts for count, parts in counts)
    first = stats is None
    lanes = 128 * ((orient_total + 127) // 128)
    plane = pl.BlockSpec((1, extent, extent), lambda s: (s, 0, 0))
    peak_spec = pl.BlockSpec((1, 8, lanes), lambda s: (s, 0, 0))
    templ_specs = [pl.BlockSpec(group.shape, lambda s: (0, 0, 0)) for group in templ_groups]
    fw_spec = pl.BlockSpec(forward.shape, lambda s: (0, 0))
    inv_spec = pl.BlockSpec(inverse.shape, lambda s: (0, 0))
    in_specs = [pl.BlockSpec(memory_space=pltpu.SMEM), plane, plane] + templ_specs + [
        fw_spec, inv_spec]
    operands = [orient_chunk, spec_re, spec_im] + list(templ_groups) + [forward, inverse]
    aliases = {}
    if not first:
        base = len(operands)
        in_specs += [plane, plane, plane, peak_spec]
        operands += list(stats)
        aliases = {base: 0, base + 1: 1, base + 2: 2}
        if not last:
            aliases[base + 3] = 3
    map_shape = jax.ShapeDtypeStruct((count, extent, extent), jnp.float32)
    flops = 3 * tiles * count * 12 * extent * extent * extent
    return pl.pallas_call(
        functools.partial(corr_kernel, first, last, counts, orient_total),
        grid=(count,),
        in_specs=in_specs,
        out_specs=[plane, plane, plane,
                   pl.BlockSpec((count, orient_total), lambda s: (0, 0)) if last else peak_spec],
        out_shape=[map_shape, map_shape, map_shape,
                   jax.ShapeDtypeStruct((count, orient_total) if last else (count, 8, lanes),
                                        jnp.float32)],
        input_output_aliases=aliases,
        compiler_params=pltpu.CompilerParams(dimension_semantics=("arbitrary",)),
        cost_estimate=pl.CostEstimate(
            flops=flops, transcendentals=0,
            bytes_accessed=tiles * 4 * extent * extent * 2 + count * 10 * extent * extent * 4),
    )(*operands)


def correlate_all(spec_re, spec_im, templ_re, templ_im, orientation, forward, inverse):
    blocks = lax.axis_size("blk")
    me = lax.axis_index("blk")
    sources = lax.axis_size("patch")
    core = lax.axis_index("patch") % 2
    tiles = templ_re.shape[0]
    half = tiles // 2
    orient_total = orientation.shape[0]
    local = jnp.concatenate([templ_re, templ_im], axis=0)
    mine = jnp.concatenate(
        [lax.dynamic_slice_in_dim(templ_re, core * half, half, 0),
         lax.dynamic_slice_in_dim(templ_im, core * half, half, 0)], axis=0)
    within = jnp.arange(half, dtype=jnp.int32)
    first_groups = [(local, 1)]
    first_index = [me * tiles + jnp.arange(tiles, dtype=jnp.int32)]
    late_got, late_index = [], []
    for k in range(1, blocks):
        source = me ^ k
        got = lax.ppermute(mine, "blk", [(b, b ^ k) for b in range(blocks)])
        first_groups.append((got, 1))
        first_index.append(source * tiles + core * half + within)
        late_got.append(got)
        late_index.append(source * tiles + (1 - core) * half + within)
    chunks = [(first_groups, jnp.concatenate(first_index))]
    if late_got:
        passed = lax.ppermute(jnp.concatenate(late_got, axis=0), "patch", xor_pairs(sources, 1))
        chunks.append(([(passed, len(late_got))], jnp.concatenate(late_index)))
    stats = None
    for n, (groups, index) in enumerate(chunks):
        orient_chunk = jnp.take(orientation, index)
        counts = [(group.shape[0] // (2 * parts), parts) for group, parts in groups]
        stats = correlate_chunk(spec_re, spec_im, [group for group, parts in groups], counts,
                                forward, inverse, orient_chunk, orient_total, stats,
                                n == len(chunks) - 1)
    top_map, mean_map, var_map, peak = stats
    return (top_map, mean_map, var_map, peak)


def body(patches, owner_of_patch, group_of_patch, defocus, templ_re, templ_im, orientation):
    sources = lax.axis_size("patch")
    my_index = lax.axis_index("patch")
    number, extent = (patches.shape[0], patches.shape[1])
    forward, half_table, inverse = (jnp.asarray(table) for table in dft_tables(extent))
    row_owner = owner_of_patch.reshape(sources, number)
    take_idx, pieces, slot_row, outgoing = route_patches(patches, row_owner, my_index)
    templ_re, templ_im, unused = lax.optimization_barrier((templ_re, templ_im, outgoing))
    groups = jnp.take(jnp.concatenate([group_of_patch, jnp.zeros((1,), jnp.int32)]), slot_row)
    focus_values = jnp.take(defocus, groups)
    scale = ctf_scale(focus_values, extent)
    spec_re, spec_im = make_spectra(take_idx, pieces, scale, half_table, forward)
    return correlate_all(spec_re, spec_im, templ_re, templ_im, orientation, forward, inverse)


def solution(mesh):
    placed = (
        P(("blk", "patch"), None, None),
        P("blk"),
        P("blk"),
        P(),
        P("blk", None, None),
        P("blk", None, None),
        P(),
    )
    return jax.shard_map(
        body,
        mesh=mesh,
        in_specs=placed,
        out_specs=(
            P(("blk", "patch"), None, None),
            P(("blk", "patch"), None, None),
            P(("blk", "patch"), None, None),
            P(("blk", "patch"), None),
        ),
        check_vma=False,
    )
```
